32 devices in a mesh: tm: 16 (over z, x, core), doc: 2 (over y).
Axes of the slice: x: 2, y: 2, z: 4, core: 2. Of those that a mesh axis runs over, the one named last changes fastest.
Arguments:
- beta: float32 [16, 4096, 128], P('tm', 'doc'), may hold values from -6 to 260
- word_ids: int32 [16, 8, 128], P('tm', 'doc'), may hold values from 0 to 4095
- word_counts: int32 [16, 8, 128], P('tm', 'doc'), may hold values from 1 to 8
- block_slot: int32 [32], replicated, may hold values from 0 to 31, each once
- topic_prior: float32 [128], replicated, may hold values from 0.05 to 0.5
- drift_var: float32 [128], replicated, may hold values from 0.0005 to 0.05
- obs_precision: float32 [16, 128], replicated, may hold values from 0.01 to 4
Outputs:
- smoothed_means: float32 [16, 4096, 128], P('tm', 'doc')
- doc_topics: float32 [16, 8, 128], P('tm', 'doc')
The draws below stay inside these ranges and needn't reach their ends.
Inputs may be any that keep to these rules, and one draw needn't show every extreme that they name: `block_slot`: each block has its own position.
All inputs are finite; a program needn't handle non-finite values.
Results may differ from the reference program's by a relative error of at most 0.0012.
The reference program's roundings to bfloat16 on the way (of `table`, `looked` and `weighted`) count: a program that leaves them out, or rounds other values in their place, can miss the bound.
Values may be sent and summed in bfloat16 or wider, within the bound.
No kernel may reach another device: no remote copies, remote signals or barrier semaphores. Data moves between devices by JAX's collectives and lax.ppermute only.
A program may use at most 192 MiB of HBM per device.

```python
import math
import jax
import jax.numpy as jnp
import numpy as np
from jax import lax

K = 128
BLOCK = 128
TOK_DOC = 128
EITERS = 4
YEARS = 16
V = 4096
NBLOCKS = 32
DOCS = 8


def draw_beta(key, part):
    base_key = jax.random.fold_in(key, 0)
    return jnp.clip(1.5 * jax.random.normal(base_key, (YEARS, V, K), jnp.float32), -6.0, 6.0)


def plant(entries, rng, least, largest):
    longest = entries.shape.index(max(entries.shape))
    spots = []
    for shift in (0, 1):
        where = [jax.random.randint(jax.random.fold_in(rng, axis), (), 0, length) for axis, length in enumerate(entries.shape)]
        where[longest] = (where[longest] + shift) % entries.shape[longest]
        spots.append(tuple(where))
    return entries.at[spots[0]].set(least).at[spots[1]].set(largest)


def rank_bounds(count, slope):
    loads = [(1 << 20) // math.isqrt(standing ** slope) + 1 for standing in range(1, count + 1)]
    deviation = 1 + sum(loads) // (1 << 30)
    return np.cumsum(np.array([max(1, weight // deviation) for weight in loads]))


def ranked_ids(own_key, shape, amount, skew):
    grid = rank_bounds(amount, skew)
    lot = jax.random.randint(jax.random.fold_in(own_key, 1), shape, 0, int(grid[amount - 1]))
    grade = jnp.searchsorted(jnp.asarray(grid, jnp.int32), lot, side="right")
    return jax.random.permutation(jax.random.fold_in(own_key, 2), amount)[grade].astype(jnp.int32)


def setup_inputs(seed: int = 0) -> dict:
    splits = jax.random.split(jax.random.key(seed), 8)
    beta = draw_beta(jax.random.fold_in(splits[7], 71), 0)
    word_ids = plant(ranked_ids(splits[1], (YEARS, DOCS, TOK_DOC), V, 2), jax.random.fold_in(splits[1], 3), 0, V - 1).astype(jnp.int32)
    word_counts = plant(jax.random.randint(splits[2], (YEARS, DOCS, TOK_DOC), 1, 9), jax.random.fold_in(splits[2], 1), 1, 8).astype(jnp.int32)
    block_slot = jax.random.permutation(splits[3], NBLOCKS).astype(jnp.int32)
    topic_prior = jnp.clip(jnp.exp(jax.random.uniform(splits[4], (K,), jnp.float32, math.log(0.05), math.log(0.5))), 0.05, 0.5)
    drift_var = jnp.clip(jnp.exp(jax.random.uniform(splits[5], (K,), jnp.float32, math.log(0.0005), math.log(0.05))), 0.0005, 0.05)
    obs_precision = jnp.clip(jnp.exp(jax.random.uniform(splits[6], (YEARS, K), jnp.float32, math.log(0.01), math.log(4.0))), 0.01, 4.0)
    return dict(beta=beta, word_ids=word_ids, word_counts=word_counts, block_slot=block_slot, topic_prior=topic_prior, drift_var=drift_var, obs_precision=obs_precision)


init_variance = 4.0


def variance_tables(obs_precision, drift_var):
    def forward_step(prior_var, precision):
        denominator = 1.0 + prior_var * precision
        gain_now = prior_var * precision / denominator
        filt_var = prior_var / denominator
        return filt_var + drift_var, (gain_now, filt_var)

    start_var = jnp.full(drift_var.shape, init_variance, dtype=jnp.float32)
    last_var, (gains, filt_vars) = lax.scan(forward_step, start_var, obs_precision)

    def backward_step(info_next, precision):
        merged = info_next + precision
        shrink = 1.0 / (1.0 + drift_var * merged)
        info_now = merged * shrink
        return info_now, (shrink, info_now)

    zero_info = jnp.zeros(drift_var.shape, dtype=jnp.float32)
    last_info, (shrinks, infos) = lax.scan(backward_step, zero_info, obs_precision[1:], reverse=True)
    shrinks = jnp.concatenate([shrinks, jnp.ones_like(zero_info)[None]], axis=0)
    infos = jnp.concatenate([infos, zero_info[None]], axis=0)
    return gains, filt_vars, shrinks, infos


def e_step(looked, word_counts, topic_prior):
    counts_float = word_counts.astype(jnp.float32)
    doc_topics = topic_prior + jnp.sum(counts_float, axis=-1, keepdims=True) / K
    scores = looked.astype(jnp.float32)
    for sweep in range(EITERS):
        resp = jax.nn.softmax(lax.digamma(doc_topics)[..., None, :] + scores, axis=-1)
        doc_topics = topic_prior + jnp.sum(counts_float[..., None] * resp, axis=-2)
    weighted = (counts_float[..., None] * resp).astype(jnp.bfloat16)
    return doc_topics, weighted


def reference(beta, word_ids, word_counts, block_slot, topic_prior, drift_var, obs_precision):
    normalizer = jax.nn.logsumexp(beta, axis=1, keepdims=True)
    table = (beta - normalizer).astype(jnp.bfloat16)
    columns = (jnp.take(block_slot, word_ids // BLOCK) * BLOCK + word_ids % BLOCK).astype(jnp.int32)
    looked = jax.vmap(lambda table_year, cols_year: jnp.take(table_year, cols_year, axis=0))(table, columns)
    doc_topics, weighted = e_step(looked, word_counts, topic_prior)

    def year_counts(cols_year, weights_year):
        return jax.ops.segment_sum(weights_year.reshape(-1, K).astype(jnp.float32), cols_year.reshape(-1), num_segments=V)

    counts = jax.vmap(year_counts)(columns, weighted)
    pseudo = beta + jnp.log1p(counts)
    gains, filt_vars, shrinks, infos = variance_tables(obs_precision, drift_var)

    def filter_step(mean_prev, inputs):
        gain_now, pseudo_now = inputs
        mean_now = (1.0 - gain_now) * mean_prev + gain_now * pseudo_now
        return mean_now, mean_now

    zero_mean = jnp.zeros(beta.shape[1:], dtype=jnp.float32)
    last_mean, filtered = lax.scan(filter_step, zero_mean, (gains[:, None, :], pseudo))
    pulls = filt_vars / (filt_vars + drift_var)
    pulls = pulls.at[-1].set(0.0)

    def smooth_step(mean_next, inputs):
        pull_now, filt_now = inputs
        mean_now = pull_now * mean_next + (1.0 - pull_now) * filt_now
        return mean_now, mean_now

    first_mean, smoothed = lax.scan(smooth_step, zero_mean, (pulls[:, None, :], filtered), reverse=True)
    return smoothed, doc_topics
```

```python
import jax
import jax.numpy as jnp
from jax import lax
from jax.sharding import PartitionSpec as P

K = 128
BLOCK = 128
EITERS = 4


init_variance = 4.0


def variance_tables(obs_precision, drift_var):

    def forward_step(prior_var, precision):
        denominator = 1.0 + prior_var * precision
        gain_now = prior_var * precision / denominator
        filt_var = prior_var / denominator
        return (filt_var + drift_var, (gain_now, filt_var))

    start_var = jnp.full(drift_var.shape, init_variance, dtype=jnp.float32)
    last_var, (gains, filt_vars) = lax.scan(forward_step, start_var, obs_precision)

    def backward_step(info_next, precision):
        merged = info_next + precision
        shrink = 1.0 / (1.0 + drift_var * merged)
        info_now = merged * shrink
        return (info_now, (shrink, info_now))

    zero_info = jnp.zeros(drift_var.shape, dtype=jnp.float32)
    last_info, (shrinks, infos) = lax.scan(
        backward_step, zero_info, obs_precision[1:], reverse=True
    )
    shrinks = jnp.concatenate([shrinks, jnp.ones_like(zero_info)[None]], axis=0)
    infos = jnp.concatenate([infos, zero_info[None]], axis=0)
    return (gains, filt_vars, shrinks, infos)


def e_step(looked, word_counts, topic_prior):
    counts_float = word_counts.astype(jnp.float32)
    doc_topics = topic_prior + jnp.sum(counts_float, axis=-1, keepdims=True) / K
    scores = looked.astype(jnp.float32)
    for sweep in range(EITERS):
        resp = jax.nn.softmax(lax.digamma(doc_topics)[..., None, :] + scores, axis=-1)
        doc_topics = topic_prior + jnp.sum(counts_float[..., None] * resp, axis=-2)
    weighted = (counts_float[..., None] * resp).astype(jnp.bfloat16)
    return (doc_topics, weighted)


def body(beta, word_ids, word_counts, block_slot, topic_prior, drift_var, obs_precision):
    local_beta = beta[0]
    own_words = local_beta.shape[0]
    topics = local_beta.shape[1]
    doc_devices = lax.axis_size("doc")
    doc_place = lax.axis_index("doc")
    local_peak = jnp.max(local_beta, axis=0)
    local_total = jnp.sum(jnp.exp(local_beta - local_peak), axis=0)

    slot_ids = word_ids[0]
    local_docs = slot_ids.shape[0]
    slot_width = slot_ids.shape[1]
    columns = jnp.take(block_slot, slot_ids // BLOCK) * BLOCK + slot_ids % BLOCK

    all_columns = lax.all_gather(columns, "doc", axis=0, tiled=True)
    all_counts = lax.all_gather(word_counts[0], "doc", axis=0, tiled=True)
    peaks = lax.all_gather(local_peak, "doc")
    totals = lax.all_gather(local_total, "doc")
    peak_value = jnp.max(peaks, axis=0)
    total_value = jnp.sum(totals * jnp.exp(peaks - peak_value), axis=0)
    normalizer = peak_value + jnp.log(total_value)

    flat_columns = all_columns.reshape(-1)
    local_columns = flat_columns - doc_place * own_words
    inside = (local_columns >= 0) & (local_columns < own_words)
    picked = jnp.take(local_beta, jnp.clip(local_columns, 0, own_words - 1), axis=0)
    partial = jnp.where(
        inside[:, None], (picked - normalizer).astype(jnp.bfloat16), jnp.zeros((), jnp.bfloat16)
    )
    looked = lax.psum(partial, "doc").reshape(local_docs * doc_devices, slot_width, topics)

    doc_topics_all, weighted = e_step(looked, all_counts, topic_prior)
    doc_topics = lax.dynamic_slice_in_dim(doc_topics_all, doc_place * local_docs, local_docs, 0)

    flat_weighted = weighted.reshape(-1, topics)
    row_words = lax.iota(jnp.int32, own_words)
    marks = (row_words[:, None] == local_columns[None, :]).astype(jnp.bfloat16)
    counts = jnp.dot(marks, flat_weighted, preferred_element_type=jnp.float32)
    pseudo = local_beta + jnp.log1p(counts)

    gains, filt_vars, shrinks, infos = variance_tables(obs_precision, drift_var)
    years_total = obs_precision.shape[0]
    pulls = filt_vars / (filt_vars + drift_var)
    pulls = pulls.at[-1].set(0.0)

    years = lax.axis_size("tm")
    chunk = own_words // years
    by_year = lax.all_to_all(
        pseudo.reshape(years, chunk, topics), "tm", split_axis=0, concat_axis=0, tiled=True
    )

    def filter_step(mean_prev, inputs):
        gain_now, pseudo_now = inputs
        mean_now = (1.0 - gain_now) * mean_prev + gain_now * pseudo_now
        return mean_now, mean_now

    zero_mean = jnp.zeros((chunk, topics), dtype=jnp.float32)
    last_mean, filtered = lax.scan(filter_step, zero_mean, (gains[:, None, :], by_year), unroll=True)

    def smooth_step(mean_next, inputs):
        pull_now, filt_now = inputs
        mean_now = pull_now * mean_next + (1.0 - pull_now) * filt_now
        return mean_now, mean_now

    first_mean, smoothed = lax.scan(
        smooth_step, zero_mean, (pulls[:, None, :], filtered), reverse=True, unroll=True
    )
    back = lax.all_to_all(smoothed, "tm", split_axis=0, concat_axis=0, tiled=True)
    return (back.reshape(own_words, topics)[None], doc_topics[None])


def solution(mesh):
    in_specs = (
        P("tm", "doc", None),
        P("tm", "doc", None),
        P("tm", "doc", None),
        P(),
        P(),
        P(),
        P(),
    )
    out_specs = (P("tm", "doc", None), P("tm", "doc", None))
    return jax.shard_map(body, mesh=mesh, in_specs=in_specs, out_specs=out_specs, check_vma=False)
```

```python
import jax
import jax.numpy as jnp
from jax import lax
from jax.experimental import pallas as pl
from jax.sharding import PartitionSpec as P

K = 128
BLOCK = 128
EITERS = 4


init_variance = 4.0


def variance_tables(obs_precision, drift_var):

    def forward_step(prior_var, precision):
        denominator = 1.0 + prior_var * precision
        gain_now = prior_var * precision / denominator
        filt_var = prior_var / denominator
        return (filt_var + drift_var, (gain_now, filt_var))

    start_var = jnp.full(drift_var.shape, init_variance, dtype=jnp.float32)
    last_var, (gains, filt_vars) = lax.scan(forward_step, start_var, obs_precision)

    def backward_step(info_next, precision):
        merged = info_next + precision
        shrink = 1.0 / (1.0 + drift_var * merged)
        info_now = merged * shrink
        return (info_now, (shrink, info_now))

    zero_info = jnp.zeros(drift_var.shape, dtype=jnp.float32)
    last_info, (shrinks, infos) = lax.scan(
        backward_step, zero_info, obs_precision[1:], reverse=True
    )
    shrinks = jnp.concatenate([shrinks, jnp.ones_like(zero_info)[None]], axis=0)
    infos = jnp.concatenate([infos, zero_info[None]], axis=0)
    return (gains, filt_vars, shrinks, infos)


def e_step(looked, word_counts, topic_prior):
    counts_float = word_counts.astype(jnp.float32)
    doc_topics = topic_prior + jnp.sum(counts_float, axis=-1, keepdims=True) / K
    scores = looked.astype(jnp.float32)
    for sweep in range(EITERS):
        resp = jax.nn.softmax(lax.digamma(doc_topics)[..., None, :] + scores, axis=-1)
        doc_topics = topic_prior + jnp.sum(counts_float[..., None] * resp, axis=-2)
    weighted = to_bf16(counts_float[..., None] * resp)
    return (doc_topics, weighted)


def to_bf16(value):
    return lax.reduce_precision(value, exponent_bits=8, mantissa_bits=7).astype(jnp.bfloat16)


def shift_doc(value, s):
    count = lax.axis_size("doc")
    return lax.ppermute(value, "doc", [(i, (i + s) % count) for i in range(count)])


def kalman_kernel(gain_ref, pull_ref, pseudo_ref, out_ref):
    years = pseudo_ref.shape[0]
    mean = jnp.zeros(pseudo_ref.shape[1:], jnp.float32)
    for t in range(years):
        gain_now = gain_ref[pl.ds(t, 1), :]
        mean = (1.0 - gain_now) * mean + gain_now * pseudo_ref[t]
        out_ref[t] = mean
    mean = jnp.zeros(pseudo_ref.shape[1:], jnp.float32)
    for t in reversed(range(years)):
        pull_now = pull_ref[pl.ds(t, 1), :]
        mean = pull_now * mean + (1.0 - pull_now) * out_ref[t]
        out_ref[t] = mean


def body(beta, word_ids, word_counts, block_slot, topic_prior, drift_var, obs_precision):
    local_beta = beta[0]
    own_words = local_beta.shape[0]
    topics = local_beta.shape[1]
    doc_devices = lax.axis_size("doc")
    doc_place = lax.axis_index("doc")
    local_peak = jnp.max(local_beta, axis=0)
    local_total = jnp.sum(jnp.exp(local_beta - local_peak), axis=0)

    slot_ids = word_ids[0]
    local_docs = slot_ids.shape[0]
    slot_width = slot_ids.shape[1]
    columns = jnp.take(block_slot, slot_ids // BLOCK) * BLOCK + slot_ids % BLOCK

    ints = jnp.stack([columns, word_counts[0]])
    stats = jnp.stack([local_peak, local_total])
    ints_seen = [ints] + [shift_doc(ints, s) for s in range(1, doc_devices)]
    stats_seen = jnp.stack([stats] + [shift_doc(stats, s) for s in range(1, doc_devices)])
    all_columns = jnp.concatenate([part[0] for part in ints_seen], axis=0)
    all_counts = jnp.concatenate([part[1] for part in ints_seen], axis=0)
    peaks = stats_seen[:, 0]
    totals = stats_seen[:, 1]
    peak_value = jnp.max(peaks, axis=0)
    total_value = jnp.sum(totals * jnp.exp(peaks - peak_value), axis=0)
    normalizer = peak_value + jnp.log(total_value)

    flat_columns = all_columns.reshape(-1)
    local_columns = flat_columns - doc_place * own_words
    inside = (local_columns >= 0) & (local_columns < own_words)
    picked = jnp.take(local_beta, jnp.clip(local_columns, 0, own_words - 1), axis=0)
    partial = jnp.where(
        inside[:, None], to_bf16(picked - normalizer), jnp.zeros((), jnp.bfloat16)
    ).reshape(doc_devices, local_docs * slot_width, topics)
    looked = partial
    for s in range(1, doc_devices):
        looked = looked + jnp.roll(shift_doc(partial, s), s, axis=0)
    looked = looked.reshape(local_docs * doc_devices, slot_width, topics)

    doc_topics_all, weighted = e_step(looked, all_counts, topic_prior)
    doc_topics = doc_topics_all[:local_docs]

    flat_weighted = weighted.reshape(-1, topics)
    row_words = lax.iota(jnp.int32, own_words)
    marks = (row_words[:, None] == local_columns[None, :]).astype(jnp.bfloat16)
    counts = jnp.dot(marks, flat_weighted, preferred_element_type=jnp.float32)
    pseudo = local_beta + jnp.log1p(counts)

    gains, filt_vars, shrinks, infos = variance_tables(obs_precision, drift_var)
    years_total = obs_precision.shape[0]
    pulls = filt_vars / (filt_vars + drift_var)
    pulls = pulls.at[-1].set(0.0)

    years = lax.axis_size("tm")
    chunk = own_words // years
    by_year = lax.all_to_all(
        pseudo.reshape(years, chunk, topics), "tm", split_axis=0, concat_axis=0, tiled=True
    )

    smoothed = pl.pallas_call(
        kalman_kernel, out_shape=jax.ShapeDtypeStruct(by_year.shape, jnp.float32)
    )(gains, pulls, by_year)
    back = lax.all_to_all(smoothed, "tm", split_axis=0, concat_axis=0, tiled=True)
    return (back.reshape(own_words, topics)[None], doc_topics[None])


def solution(mesh):
    in_specs = (
        P("tm", "doc", None),
        P("tm", "doc", None),
        P("tm", "doc", None),
        P(),
        P(),
        P(),
        P(),
    )
    out_specs = (P("tm", "doc", None), P("tm", "doc", None))
    return jax.shard_map(body, mesh=mesh, in_specs=in_specs, out_specs=out_specs, check_vma=False)
```

```python
import jax
import jax.numpy as jnp
from jax import lax
from jax.experimental import pallas as pl
from jax.sharding import PartitionSpec as P

K = 128
BLOCK = 128
EITERS = 4


init_variance = 4.0


def variance_tables(obs_precision, drift_var):

    def forward_step(prior_var, precision):
        denominator = 1.0 + prior_var * precision
        gain_now = prior_var * precision / denominator
        filt_var = prior_var / denominator
        return (filt_var + drift_var, (gain_now, filt_var))

    start_var = jnp.full(drift_var.shape, init_variance, dtype=jnp.float32)
    last_var, (gains, filt_vars) = lax.scan(forward_step, start_var, obs_precision)

    def backward_step(info_next, precision):
        merged = info_next + precision
        shrink = 1.0 / (1.0 + drift_var * merged)
        info_now = merged * shrink
        return (info_now, (shrink, info_now))

    zero_info = jnp.zeros(drift_var.shape, dtype=jnp.float32)
    last_info, (shrinks, infos) = lax.scan(
        backward_step, zero_info, obs_precision[1:], reverse=True
    )
    shrinks = jnp.concatenate([shrinks, jnp.ones_like(zero_info)[None]], axis=0)
    infos = jnp.concatenate([infos, zero_info[None]], axis=0)
    return (gains, filt_vars, shrinks, infos)


def e_step(looked, word_counts, topic_prior):
    counts_float = word_counts.astype(jnp.float32)
    doc_topics = topic_prior + jnp.sum(counts_float, axis=-1, keepdims=True) / K
    scores = looked.astype(jnp.float32)
    for sweep in range(EITERS):
        logits = lax.digamma(doc_topics)[..., None, :] + scores
        peak = lax.optimization_barrier(jnp.max(logits, axis=-1, keepdims=True))
        raised = jnp.exp(logits - peak)
        total = lax.optimization_barrier(jnp.sum(raised, axis=-1, keepdims=True))
        resp = raised / total
        doc_topics = topic_prior + jnp.sum(counts_float[..., None] * resp, axis=-2)
    weighted = to_bf16(counts_float[..., None] * resp)
    return (doc_topics, weighted)


def to_bf16(value):
    return lax.reduce_precision(value, exponent_bits=8, mantissa_bits=7).astype(jnp.bfloat16)


def shift_doc(value, s):
    count = lax.axis_size("doc")
    return lax.ppermute(value, "doc", [(i, (i + s) % count) for i in range(count)])


def kalman_kernel(gain_ref, pull_ref, pseudo_ref, out_ref):
    years = pseudo_ref.shape[0]
    mean = jnp.zeros(pseudo_ref.shape[1:], jnp.float32)
    for t in range(years):
        gain_now = gain_ref[pl.ds(t, 1), :]
        mean = (1.0 - gain_now) * mean + gain_now * pseudo_ref[t]
        out_ref[t] = mean
    mean = jnp.zeros(pseudo_ref.shape[1:], jnp.float32)
    for t in reversed(range(years)):
        pull_now = pull_ref[pl.ds(t, 1), :]
        mean = pull_now * mean + (1.0 - pull_now) * out_ref[t]
        out_ref[t] = mean


def body(beta, word_ids, word_counts, block_slot, topic_prior, drift_var, obs_precision):
    local_beta = beta[0]
    own_words = local_beta.shape[0]
    topics = local_beta.shape[1]
    doc_devices = lax.axis_size("doc")
    doc_place = lax.axis_index("doc")
    local_peak = jnp.max(local_beta, axis=0)
    local_total = jnp.sum(jnp.exp(local_beta - local_peak), axis=0)

    slot_ids = word_ids[0]
    local_docs = slot_ids.shape[0]
    slot_width = slot_ids.shape[1]

    ints = jnp.stack([slot_ids, word_counts[0]])
    stats = jnp.stack([local_peak, local_total])
    ints_seen = [ints] + [shift_doc(ints, s) for s in range(1, doc_devices)]
    stats_seen = jnp.stack([stats] + [shift_doc(stats, s) for s in range(1, doc_devices)])
    all_ids = jnp.concatenate([part[0] for part in ints_seen], axis=0)
    block_match = (all_ids // BLOCK)[..., None] == lax.iota(jnp.int32, block_slot.shape[0])
    all_columns = (
        jnp.sum(jnp.where(block_match, block_slot, 0), axis=-1) * BLOCK + all_ids % BLOCK
    )
    all_counts = jnp.concatenate([part[1] for part in ints_seen], axis=0)
    peaks = stats_seen[:, 0]
    totals = stats_seen[:, 1]
    peak_value = jnp.max(peaks, axis=0)
    total_value = jnp.sum(totals * jnp.exp(peaks - peak_value), axis=0)
    normalizer = peak_value + jnp.log(total_value)

    flat_columns = all_columns.reshape(-1)
    local_columns = flat_columns - doc_place * own_words
    inside = (local_columns >= 0) & (local_columns < own_words)
    picked = jnp.take(local_beta, jnp.clip(local_columns, 0, own_words - 1), axis=0)
    partial = jnp.where(
        inside[:, None], to_bf16(picked - normalizer), jnp.zeros((), jnp.bfloat16)
    ).reshape(doc_devices, local_docs * slot_width, topics)
    looked = partial
    for s in range(1, doc_devices):
        looked = looked + jnp.roll(shift_doc(partial, s), s, axis=0)
    looked = looked.reshape(local_docs * doc_devices, slot_width, topics)

    doc_topics_all, weighted = e_step(looked, all_counts, topic_prior)
    doc_topics = doc_topics_all[:local_docs]

    flat_weighted = weighted.reshape(-1, topics)
    row_words = lax.iota(jnp.int32, own_words)
    marks = (row_words[:, None] == local_columns[None, :]).astype(jnp.bfloat16)
    counts = jnp.dot(marks, flat_weighted, preferred_element_type=jnp.float32)
    pseudo = local_beta + jnp.log1p(counts)

    gains, filt_vars, shrinks, infos = variance_tables(obs_precision, drift_var)
    years_total = obs_precision.shape[0]
    pulls = filt_vars / (filt_vars + drift_var)
    pulls = pulls.at[-1].set(0.0)

    years = lax.axis_size("tm")
    chunk = own_words // years
    by_year = lax.all_to_all(
        pseudo.reshape(years, chunk, topics), "tm", split_axis=0, concat_axis=0, tiled=True
    )

    smoothed = pl.pallas_call(
        kalman_kernel, out_shape=jax.ShapeDtypeStruct(by_year.shape, jnp.float32)
    )(gains, pulls, by_year)
    back = lax.all_to_all(smoothed, "tm", split_axis=0, concat_axis=0, tiled=True)
    return (back.reshape(own_words, topics)[None], doc_topics[None])


def solution(mesh):
    in_specs = (
        P("tm", "doc", None),
        P("tm", "doc", None),
        P("tm", "doc", None),
        P(),
        P(),
        P(),
        P(),
    )
    out_specs = (P("tm", "doc", None), P("tm", "doc", None))
    return jax.shard_map(body, mesh=mesh, in_specs=in_specs, out_specs=out_specs, check_vma=False)
```

```python
import jax
import jax.numpy as jnp
from jax import lax
from jax.experimental import pallas as pl
from jax.sharding import PartitionSpec as P

K = 128
BLOCK = 128
EITERS = 4


init_variance = 4.0


def variance_tables(obs_precision, drift_var):

    def forward_step(prior_var, precision):
        denominator = 1.0 + prior_var * precision
        gain_now = prior_var * precision / denominator
        filt_var = prior_var / denominator
        return (filt_var + drift_var, (gain_now, filt_var))

    start_var = jnp.full(drift_var.shape, init_variance, dtype=jnp.float32)
    last_var, (gains, filt_vars) = lax.scan(forward_step, start_var, obs_precision, unroll=True)

    def backward_step(info_next, precision):
        merged = info_next + precision
        shrink = 1.0 / (1.0 + drift_var * merged)
        info_now = merged * shrink
        return (info_now, (shrink, info_now))

    zero_info = jnp.zeros(drift_var.shape, dtype=jnp.float32)
    last_info, (shrinks, infos) = lax.scan(
        backward_step, zero_info, obs_precision[1:], reverse=True
    )
    shrinks = jnp.concatenate([shrinks, jnp.ones_like(zero_info)[None]], axis=0)
    infos = jnp.concatenate([infos, zero_info[None]], axis=0)
    return (gains, filt_vars, shrinks, infos)


def e_step(looked, word_counts, topic_prior):
    counts_float = word_counts.astype(jnp.float32)
    doc_topics = topic_prior + jnp.sum(counts_float, axis=-1, keepdims=True) / K
    scores = looked.astype(jnp.float32)
    for sweep in range(EITERS):
        logits = lax.digamma(doc_topics)[..., None, :] + scores
        peak = lax.optimization_barrier(jnp.max(logits, axis=-1, keepdims=True))
        raised = jnp.exp(logits - peak)
        total = lax.optimization_barrier(jnp.sum(raised, axis=-1, keepdims=True))
        resp = raised / total
        doc_topics = topic_prior + jnp.sum(counts_float[..., None] * resp, axis=-2)
    weighted = to_bf16(counts_float[..., None] * resp)
    return (doc_topics, weighted)


def to_bf16(value):
    return lax.reduce_precision(value, exponent_bits=8, mantissa_bits=7).astype(jnp.bfloat16)


def shift_axis(value, axis, s):
    count = lax.axis_size(axis)
    return lax.ppermute(value, axis, [(i, (i + s) % count) for i in range(count)])


def shift_doc(value, s):
    return shift_axis(value, "doc", s)


def kalman_kernel(gain_ref, pull_ref, start_ref, after_ref, pseudo_ref, out_ref, last_ref):
    years = pseudo_ref.shape[0]
    mean = start_ref[...]
    for t in range(years):
        gain_now = gain_ref[pl.ds(t, 1), :]
        mean = (1.0 - gain_now) * mean + gain_now * pseudo_ref[t]
        out_ref[t] = mean
    last_ref[...] = mean
    mean = after_ref[...]
    for t in reversed(range(years)):
        pull_now = pull_ref[pl.ds(t, 1), :]
        mean = pull_now * mean + (1.0 - pull_now) * out_ref[t]
        out_ref[t] = mean


def kalman(gains, pulls, start, after, by_year):
    return pl.pallas_call(
        kalman_kernel,
        out_shape=(
            jax.ShapeDtypeStruct(by_year.shape, jnp.float32),
            jax.ShapeDtypeStruct(start.shape, jnp.float32),
        ),
    )(gains, pulls, start, after, by_year)


def group_maps(gains, pulls, groups):
    gains_g = gains.reshape(groups, -1, gains.shape[-1])
    pulls_g = pulls.reshape(groups, -1, pulls.shape[-1])
    span = gains_g.shape[1]
    carry = jnp.ones_like(gains_g[:, 0])
    responses = []
    for i in range(span):
        carry = (1.0 - gains_g[:, i]) * carry
        responses.append(carry)
    from_start = jnp.zeros_like(carry)
    from_after = jnp.ones_like(carry)
    for i in reversed(range(span)):
        from_start = pulls_g[:, i] * from_start + (1.0 - pulls_g[:, i]) * responses[i]
        from_after = pulls_g[:, i] * from_after
    return carry, from_start, from_after


def body(beta, word_ids, word_counts, block_slot, topic_prior, drift_var, obs_precision):
    local_beta = beta[0]
    own_words = local_beta.shape[0]
    topics = local_beta.shape[1]
    doc_devices = lax.axis_size("doc")
    doc_place = lax.axis_index("doc")
    local_peak = jnp.max(local_beta, axis=0)
    local_total = jnp.sum(jnp.exp(local_beta - local_peak), axis=0)

    slot_ids = word_ids[0]
    local_docs = slot_ids.shape[0]
    slot_width = slot_ids.shape[1]

    ints = jnp.stack([slot_ids, word_counts[0]])
    stats = jnp.stack([local_peak, local_total])
    ints_seen = [ints] + [shift_doc(ints, s) for s in range(1, doc_devices)]
    stats_seen = jnp.stack([stats] + [shift_doc(stats, s) for s in range(1, doc_devices)])
    all_ids = jnp.concatenate([part[0] for part in ints_seen], axis=0)
    block_match = (all_ids // BLOCK)[..., None] == lax.iota(jnp.int32, block_slot.shape[0])
    all_columns = (
        jnp.sum(jnp.where(block_match, block_slot, 0), axis=-1) * BLOCK + all_ids % BLOCK
    )
    all_counts = jnp.concatenate([part[1] for part in ints_seen], axis=0)
    peaks = stats_seen[:, 0]
    totals = stats_seen[:, 1]
    peak_value = jnp.max(peaks, axis=0)
    total_value = jnp.sum(totals * jnp.exp(peaks - peak_value), axis=0)
    normalizer = peak_value + jnp.log(total_value)

    flat_columns = all_columns.reshape(-1)
    local_columns = flat_columns - doc_place * own_words
    inside = (local_columns >= 0) & (local_columns < own_words)
    picked = jnp.take(local_beta, jnp.clip(local_columns, 0, own_words - 1), axis=0)
    partial = jnp.where(
        inside[:, None], to_bf16(picked - normalizer), jnp.zeros((), jnp.bfloat16)
    ).reshape(doc_devices, local_docs * slot_width, topics)
    looked = partial
    for s in range(1, doc_devices):
        looked = looked + jnp.roll(shift_doc(partial, s), s, axis=0)
    looked = looked.reshape(local_docs * doc_devices, slot_width, topics)

    doc_topics_all, weighted = e_step(looked, all_counts, topic_prior)
    doc_topics = doc_topics_all[:local_docs]

    flat_weighted = weighted.reshape(-1, topics)
    row_words = lax.iota(jnp.int32, own_words)
    marks = (row_words[:, None] == local_columns[None, :]).astype(jnp.bfloat16)
    counts = jnp.dot(marks, flat_weighted, preferred_element_type=jnp.float32)
    pseudo = local_beta + jnp.log1p(counts)

    gains, filt_vars, shrinks, infos = variance_tables(obs_precision, drift_var)
    years_total = obs_precision.shape[0]
    pulls = filt_vars / (filt_vars + drift_var)
    pulls = pulls.at[-1].set(0.0)

    groups = lax.axis_size("tg")
    span = lax.axis_size("tl")
    group = lax.axis_index("tg")
    chunk = own_words // span
    by_year = lax.all_to_all(
        pseudo.reshape(span, chunk, topics), "tl", split_axis=0, concat_axis=0, tiled=True
    )
    gains_here = lax.dynamic_slice_in_dim(gains, group * span, span, 0)
    pulls_here = lax.dynamic_slice_in_dim(pulls, group * span, span, 0)
    zero_mean = jnp.zeros((chunk, topics), jnp.float32)
    if groups == 1:
        smoothed, _ = kalman(gains_here, pulls_here, zero_mean, zero_mean, by_year)
    else:
        local_smoothed, local_last = kalman(gains_here, pulls_here, zero_mean, zero_mean, by_year)
        summary = jnp.stack([local_last, local_smoothed[0]])
        seen = [summary] + [shift_axis(summary, "tg", s) for s in range(1, groups)]
        ordered = jnp.stack(seen)[(group - jnp.arange(groups)) % groups]
        carry, from_start, from_after = group_maps(gains, pulls, groups)
        entering = [zero_mean]
        for g in range(groups - 1):
            entering.append(ordered[g, 0] + carry[g] * entering[g])
        leaving = [zero_mean] * groups
        for g in reversed(range(1, groups)):
            leaving[g - 1] = (
                ordered[g, 1] + from_start[g] * entering[g] + from_after[g] * leaving[g]
            )
        start = jnp.stack(entering)[group]
        after = jnp.stack(leaving)[group]
        smoothed, _ = kalman(gains_here, pulls_here, start, after, by_year)
    back = lax.all_to_all(smoothed, "tl", split_axis=0, concat_axis=0, tiled=True)
    return (back.reshape(own_words, topics)[None], doc_topics[None])


def solution(mesh):
    years = mesh.shape["tm"]
    span = 8 if years % 8 == 0 else years
    devices = mesh.devices.reshape(years // span, span, mesh.shape["doc"])
    grouped = jax.sharding.Mesh(devices, ("tg", "tl", "doc"))
    split = P(("tg", "tl"), "doc", None)
    in_specs = (split, split, split, P(), P(), P(), P())
    out_specs = (split, split)
    return jax.shard_map(body, mesh=grouped, in_specs=in_specs, out_specs=out_specs, check_vma=False)
```

```python
import jax
import jax.numpy as jnp
from jax import lax
from jax.experimental import pallas as pl
from jax.sharding import PartitionSpec as P

K = 128
BLOCK = 128
EITERS = 4


init_variance = 4.0


def variance_tables(obs_precision, drift_var):

    def forward_step(prior_var, precision):
        denominator = 1.0 + prior_var * precision
        gain_now = prior_var * precision / denominator
        filt_var = prior_var / denominator
        return (filt_var + drift_var, (gain_now, filt_var))

    start_var = jnp.full(drift_var.shape, init_variance, dtype=jnp.float32)
    last_var, (gains, filt_vars) = lax.scan(forward_step, start_var, obs_precision, unroll=True)

    def backward_step(info_next, precision):
        merged = info_next + precision
        shrink = 1.0 / (1.0 + drift_var * merged)
        info_now = merged * shrink
        return (info_now, (shrink, info_now))

    zero_info = jnp.zeros(drift_var.shape, dtype=jnp.float32)
    last_info, (shrinks, infos) = lax.scan(
        backward_step, zero_info, obs_precision[1:], reverse=True
    )
    shrinks = jnp.concatenate([shrinks, jnp.ones_like(zero_info)[None]], axis=0)
    infos = jnp.concatenate([infos, zero_info[None]], axis=0)
    return (gains, filt_vars, shrinks, infos)


def e_step(looked, word_counts, topic_prior):
    counts_float = word_counts.astype(jnp.float32)
    doc_topics = topic_prior + jnp.sum(counts_float, axis=-1, keepdims=True) / K
    scores = looked.astype(jnp.float32)
    for sweep in range(EITERS):
        logits = lax.digamma(doc_topics)[..., None, :] + scores
        peak = lax.optimization_barrier(jnp.max(logits, axis=-1, keepdims=True))
        raised = jnp.exp(logits - peak)
        total = lax.optimization_barrier(jnp.sum(raised, axis=-1, keepdims=True))
        resp = raised / total
        doc_topics = topic_prior + jnp.sum(counts_float[..., None] * resp, axis=-2)
    weighted = to_bf16(counts_float[..., None] * resp)
    return (doc_topics, weighted)


def to_bf16(value):
    return lax.reduce_precision(value, exponent_bits=8, mantissa_bits=7).astype(jnp.bfloat16)


def shift_axis(value, axis, s):
    count = lax.axis_size(axis)
    return lax.ppermute(value, axis, [(i, (i + s) % count) for i in range(count)])


def shift_doc(value, s):
    return shift_axis(value, "doc", s)


def kalman_kernel(gain_ref, pull_ref, start_ref, after_ref, pseudo_ref, out_ref, last_ref):
    years = pseudo_ref.shape[0]
    mean = start_ref[...]
    for t in range(years):
        gain_now = gain_ref[pl.ds(t, 1), :]
        mean = (1.0 - gain_now) * mean + gain_now * pseudo_ref[t]
        out_ref[t] = mean
    last_ref[...] = mean
    mean = after_ref[...]
    for t in reversed(range(years)):
        pull_now = pull_ref[pl.ds(t, 1), :]
        mean = pull_now * mean + (1.0 - pull_now) * out_ref[t]
        out_ref[t] = mean


def kalman(gains, pulls, start, after, by_year):
    return pl.pallas_call(
        kalman_kernel,
        out_shape=(
            jax.ShapeDtypeStruct(by_year.shape, jnp.float32),
            jax.ShapeDtypeStruct(start.shape, jnp.float32),
        ),
    )(gains, pulls, start, after, by_year)


def group_maps(gains, pulls, groups):
    gains_g = gains.reshape(groups, -1, gains.shape[-1])
    pulls_g = pulls.reshape(groups, -1, pulls.shape[-1])
    span = gains_g.shape[1]
    carry = jnp.ones_like(gains_g[:, 0])
    responses = []
    for i in range(span):
        carry = (1.0 - gains_g[:, i]) * carry
        responses.append(carry)
    from_start = jnp.zeros_like(carry)
    from_after = jnp.ones_like(carry)
    for i in reversed(range(span)):
        from_start = pulls_g[:, i] * from_start + (1.0 - pulls_g[:, i]) * responses[i]
        from_after = pulls_g[:, i] * from_after
    return carry, from_start, from_after


def body(beta, word_ids, word_counts, block_slot, topic_prior, drift_var, obs_precision):
    local_beta = beta[0]
    own_words = local_beta.shape[0]
    topics = local_beta.shape[1]
    doc_devices = lax.axis_size("doc")
    doc_place = lax.axis_index("doc")
    local_peak = jnp.max(local_beta, axis=0)
    local_total = jnp.sum(jnp.exp(local_beta - local_peak), axis=0)

    slot_ids = word_ids[0]
    local_docs = slot_ids.shape[0]
    slot_width = slot_ids.shape[1]

    ints = jnp.stack([slot_ids, word_counts[0]])
    stats = jnp.stack([local_peak, local_total])
    ints_seen = [ints] + [shift_doc(ints, s) for s in range(1, doc_devices)]
    stats_seen = jnp.stack([stats] + [shift_doc(stats, s) for s in range(1, doc_devices)])
    all_ids = jnp.concatenate([part[0] for part in ints_seen], axis=0)
    block_match = (all_ids // BLOCK)[..., None] == lax.iota(jnp.int32, block_slot.shape[0])
    all_columns = (
        jnp.sum(jnp.where(block_match, block_slot, 0), axis=-1) * BLOCK + all_ids % BLOCK
    )
    all_counts = jnp.concatenate([part[1] for part in ints_seen], axis=0)
    peaks = stats_seen[:, 0]
    totals = stats_seen[:, 1]
    peak_value = jnp.max(peaks, axis=0)
    total_value = jnp.sum(totals * jnp.exp(peaks - peak_value), axis=0)
    normalizer = peak_value + jnp.log(total_value)

    flat_columns = all_columns.reshape(-1)
    local_columns = flat_columns - doc_place * own_words
    inside = (local_columns >= 0) & (local_columns < own_words)
    picked = jnp.take(local_beta, jnp.clip(local_columns, 0, own_words - 1), axis=0)
    partial = jnp.where(
        inside[:, None], to_bf16(picked - normalizer), jnp.zeros((), jnp.bfloat16)
    ).reshape(doc_devices, local_docs * slot_width, topics)
    looked = partial
    for s in range(1, doc_devices):
        looked = looked + jnp.roll(shift_doc(partial, s), s, axis=0)
    looked = looked.reshape(local_docs * doc_devices, slot_width, topics)

    doc_topics_all, weighted = e_step(looked, all_counts, topic_prior)
    doc_topics = doc_topics_all[:local_docs]

    flat_weighted = weighted.reshape(-1, topics)
    row_words = lax.iota(jnp.int32, own_words)
    marks = (row_words[:, None] == local_columns[None, :]).astype(jnp.bfloat16)
    counts = jnp.dot(marks, flat_weighted, preferred_element_type=jnp.float32)
    pseudo = local_beta + jnp.log1p(counts)

    gains, filt_vars, shrinks, infos = variance_tables(obs_precision, drift_var)
    years_total = obs_precision.shape[0]
    pulls = filt_vars / (filt_vars + drift_var)
    pulls = pulls.at[-1].set(0.0)

    groups = lax.axis_size("tg")
    span = lax.axis_size("tl")
    group = lax.axis_index("tg")
    chunk = own_words // span
    by_year = lax.all_to_all(
        pseudo.reshape(span, chunk, topics), "tl", split_axis=0, concat_axis=0, tiled=True
    )
    gains_here = lax.dynamic_slice_in_dim(gains, group * span, span, 0)
    pulls_here = lax.dynamic_slice_in_dim(pulls, group * span, span, 0)
    zero_mean = jnp.zeros((chunk, topics), jnp.float32)
    if groups == 1:
        smoothed, _ = kalman(gains_here, pulls_here, zero_mean, zero_mean, by_year)
    else:
        local_smoothed, local_last = kalman(gains_here, pulls_here, zero_mean, zero_mean, by_year)
        summary = jnp.stack([local_last, local_smoothed[0]])
        if groups == 2:
            sent = jnp.where(group == 0, local_last, local_smoothed[0])
            other = shift_axis(sent, "tg", 1)
            ordered = jnp.where(
                group == 0, jnp.stack([summary, jnp.stack([other, other])]),
                jnp.stack([jnp.stack([other, other]), summary]),
            )
        else:
            seen = [summary] + [shift_axis(summary, "tg", s) for s in range(1, groups)]
            ordered = jnp.stack(seen)[(group - jnp.arange(groups)) % groups]
        carry, from_start, from_after = group_maps(gains, pulls, groups)
        entering = [zero_mean]
        for g in range(groups - 1):
            entering.append(ordered[g, 0] + carry[g] * entering[g])
        leaving = [zero_mean] * groups
        for g in reversed(range(1, groups)):
            leaving[g - 1] = (
                ordered[g, 1] + from_start[g] * entering[g] + from_after[g] * leaving[g]
            )
        start = jnp.stack(entering)[group]
        after = jnp.stack(leaving)[group]
        smoothed, _ = kalman(gains_here, pulls_here, start, after, by_year)
    back = lax.all_to_all(smoothed, "tl", split_axis=0, concat_axis=0, tiled=True)
    return (back.reshape(own_words, topics)[None], doc_topics[None])


def solution(mesh):
    years = mesh.shape["tm"]
    span = 8 if years % 8 == 0 else years
    devices = mesh.devices.reshape(years // span, span, mesh.shape["doc"])
    grouped = jax.sharding.Mesh(devices, ("tg", "tl", "doc"))
    split = P(("tg", "tl"), "doc", None)
    in_specs = (split, split, split, P(), P(), P(), P())
    out_specs = (split, split)
    return jax.shard_map(body, mesh=grouped, in_specs=in_specs, out_specs=out_specs, check_vma=False)
```

```python
import jax
import jax.numpy as jnp
from jax import lax
from jax.experimental import pallas as pl
from jax.sharding import PartitionSpec as P

K = 128
BLOCK = 128
EITERS = 4


init_variance = 4.0


def variance_tables(obs_precision, drift_var):

    def forward_step(prior_var, precision):
        denominator = 1.0 + prior_var * precision
        gain_now = prior_var * precision / denominator
        filt_var = prior_var / denominator
        return (filt_var + drift_var, (gain_now, filt_var))

    start_var = jnp.full(drift_var.shape, init_variance, dtype=jnp.float32)
    last_var, (gains, filt_vars) = lax.scan(forward_step, start_var, obs_precision, unroll=True)

    def backward_step(info_next, precision):
        merged = info_next + precision
        shrink = 1.0 / (1.0 + drift_var * merged)
        info_now = merged * shrink
        return (info_now, (shrink, info_now))

    zero_info = jnp.zeros(drift_var.shape, dtype=jnp.float32)
    last_info, (shrinks, infos) = lax.scan(
        backward_step, zero_info, obs_precision[1:], reverse=True
    )
    shrinks = jnp.concatenate([shrinks, jnp.ones_like(zero_info)[None]], axis=0)
    infos = jnp.concatenate([infos, zero_info[None]], axis=0)
    return (gains, filt_vars, shrinks, infos)


def e_step(looked, word_counts, topic_prior):
    counts_float = word_counts.astype(jnp.float32)
    doc_topics = topic_prior + jnp.sum(counts_float, axis=-1, keepdims=True) / K
    scores = looked.astype(jnp.float32)
    for sweep in range(EITERS):
        logits = lax.digamma(doc_topics)[..., None, :] + scores
        peak = lax.optimization_barrier(jnp.max(logits, axis=-1, keepdims=True))
        raised = jnp.exp(logits - peak)
        total = lax.optimization_barrier(jnp.sum(raised, axis=-1, keepdims=True))
        resp = raised / total
        doc_topics = topic_prior + jnp.sum(counts_float[..., None] * resp, axis=-2)
    weighted = to_bf16(counts_float[..., None] * resp)
    return (doc_topics, weighted)


def to_bf16(value):
    return lax.reduce_precision(value, exponent_bits=8, mantissa_bits=7).astype(jnp.bfloat16)


def shift_axis(value, axis, s):
    count = lax.axis_size(axis)
    return lax.ppermute(value, axis, [(i, (i + s) % count) for i in range(count)])


def shift_doc(value, s):
    return shift_axis(value, "doc", s)


def kalman_kernel(gain_ref, pull_ref, start_ref, after_ref, pseudo_ref, out_ref, last_ref):
    years = pseudo_ref.shape[0]
    mean = start_ref[...]
    for t in range(years):
        gain_now = gain_ref[pl.ds(t, 1), :]
        mean = (1.0 - gain_now) * mean + gain_now * pseudo_ref[t]
        out_ref[t] = mean
    last_ref[...] = mean
    mean = after_ref[...]
    for t in reversed(range(years)):
        pull_now = pull_ref[pl.ds(t, 1), :]
        mean = pull_now * mean + (1.0 - pull_now) * out_ref[t]
        out_ref[t] = mean


def kalman(gains, pulls, start, after, by_year):
    years, rows, topics = by_year.shape
    block = 64 if rows % 64 == 0 else rows
    whole = pl.BlockSpec((years, topics), lambda i: (0, 0))
    edge = pl.BlockSpec((block, topics), lambda i: (i, 0))
    stack = pl.BlockSpec((years, block, topics), lambda i: (0, i, 0))
    return pl.pallas_call(
        kalman_kernel,
        grid=(rows // block,),
        in_specs=[whole, whole, edge, edge, stack],
        out_specs=(stack, edge),
        out_shape=(
            jax.ShapeDtypeStruct(by_year.shape, jnp.float32),
            jax.ShapeDtypeStruct(start.shape, jnp.float32),
        ),
    )(gains, pulls, start, after, by_year)


def group_maps(gains, pulls, groups):
    gains_g = gains.reshape(groups, -1, gains.shape[-1])
    pulls_g = pulls.reshape(groups, -1, pulls.shape[-1])
    span = gains_g.shape[1]
    carry = jnp.ones_like(gains_g[:, 0])
    responses = []
    for i in range(span):
        carry = (1.0 - gains_g[:, i]) * carry
        responses.append(carry)
    from_start = jnp.zeros_like(carry)
    from_after = jnp.ones_like(carry)
    for i in reversed(range(span)):
        from_start = pulls_g[:, i] * from_start + (1.0 - pulls_g[:, i]) * responses[i]
        from_after = pulls_g[:, i] * from_after
    return carry, from_start, from_after


def body(beta, word_ids, word_counts, block_slot, topic_prior, drift_var, obs_precision):
    local_beta = beta[0]
    own_words = local_beta.shape[0]
    topics = local_beta.shape[1]
    doc_devices = lax.axis_size("doc")
    doc_place = lax.axis_index("doc")
    local_peak = jnp.max(local_beta, axis=0)
    local_total = jnp.sum(jnp.exp(local_beta - local_peak), axis=0)

    slot_ids = word_ids[0]
    local_docs = slot_ids.shape[0]
    slot_width = slot_ids.shape[1]

    ints = jnp.stack([slot_ids, word_counts[0]])
    stats = jnp.stack([local_peak, local_total])
    ints_seen = [ints] + [shift_doc(ints, s) for s in range(1, doc_devices)]
    stats_seen = jnp.stack([stats] + [shift_doc(stats, s) for s in range(1, doc_devices)])
    all_ids = jnp.concatenate([part[0] for part in ints_seen], axis=0)
    block_match = (all_ids // BLOCK)[..., None] == lax.iota(jnp.int32, block_slot.shape[0])
    all_columns = (
        jnp.sum(jnp.where(block_match, block_slot, 0), axis=-1) * BLOCK + all_ids % BLOCK
    )
    all_counts = jnp.concatenate([part[1] for part in ints_seen], axis=0)
    peaks = stats_seen[:, 0]
    totals = stats_seen[:, 1]
    peak_value = jnp.max(peaks, axis=0)
    total_value = jnp.sum(totals * jnp.exp(peaks - peak_value), axis=0)
    normalizer = peak_value + jnp.log(total_value)

    flat_columns = all_columns.reshape(-1)
    local_columns = flat_columns - doc_place * own_words
    row_words = lax.iota(jnp.int32, own_words)
    marks = (row_words[:, None] == local_columns[None, :]).astype(jnp.bfloat16)
    table = to_bf16(local_beta - normalizer)
    partial = (
        lax.dot_general(marks, table, (((0,), (0,)), ((), ())), preferred_element_type=jnp.float32)
        .astype(jnp.bfloat16)
        .reshape(doc_devices, local_docs * slot_width, topics)
    )
    looked = partial
    for s in range(1, doc_devices):
        looked = looked + jnp.roll(shift_doc(partial, s), s, axis=0)
    looked = looked.reshape(local_docs * doc_devices, slot_width, topics)

    doc_topics_all, weighted = e_step(looked, all_counts, topic_prior)
    doc_topics = doc_topics_all[:local_docs]

    flat_weighted = weighted.reshape(-1, topics)
    counts = jnp.dot(marks, flat_weighted, preferred_element_type=jnp.float32)
    pseudo = local_beta + jnp.log1p(counts)

    gains, filt_vars, shrinks, infos = variance_tables(obs_precision, drift_var)
    years_total = obs_precision.shape[0]
    pulls = filt_vars / (filt_vars + drift_var)
    pulls = pulls.at[-1].set(0.0)

    groups = lax.axis_size("tg")
    span = lax.axis_size("tl")
    group = lax.axis_index("tg")
    chunk = own_words // span
    by_year = lax.all_to_all(
        pseudo.reshape(span, chunk, topics), "tl", split_axis=0, concat_axis=0, tiled=True
    )
    gains_here = lax.dynamic_slice_in_dim(gains, group * span, span, 0)
    pulls_here = lax.dynamic_slice_in_dim(pulls, group * span, span, 0)
    zero_mean = jnp.zeros((chunk, topics), jnp.float32)
    if groups == 1:
        smoothed, _ = kalman(gains_here, pulls_here, zero_mean, zero_mean, by_year)
    else:
        local_smoothed, local_last = kalman(gains_here, pulls_here, zero_mean, zero_mean, by_year)
        summary = jnp.stack([local_last, local_smoothed[0]])
        if groups == 2:
            sent = jnp.where(group == 0, local_last, local_smoothed[0])
            other = shift_axis(sent, "tg", 1)
            ordered = jnp.where(
                group == 0, jnp.stack([summary, jnp.stack([other, other])]),
                jnp.stack([jnp.stack([other, other]), summary]),
            )
        else:
            seen = [summary] + [shift_axis(summary, "tg", s) for s in range(1, groups)]
            ordered = jnp.stack(seen)[(group - jnp.arange(groups)) % groups]
        carry, from_start, from_after = group_maps(gains, pulls, groups)
        entering = [zero_mean]
        for g in range(groups - 1):
            entering.append(ordered[g, 0] + carry[g] * entering[g])
        leaving = [zero_mean] * groups
        for g in reversed(range(1, groups)):
            leaving[g - 1] = (
                ordered[g, 1] + from_start[g] * entering[g] + from_after[g] * leaving[g]
            )
        start = jnp.stack(entering)[group]
        after = jnp.stack(leaving)[group]
        smoothed, _ = kalman(gains_here, pulls_here, start, after, by_year)
    back = lax.all_to_all(smoothed, "tl", split_axis=0, concat_axis=0, tiled=True)
    return (back.reshape(own_words, topics)[None], doc_topics[None])


def solution(mesh):
    years = mesh.shape["tm"]
    span = 8 if years % 8 == 0 else years
    devices = mesh.devices.reshape(years // span, span, mesh.shape["doc"])
    grouped = jax.sharding.Mesh(devices, ("tg", "tl", "doc"))
    split = P(("tg", "tl"), "doc", None)
    in_specs = (split, split, split, P(), P(), P(), P())
    out_specs = (split, split)
    return jax.shard_map(body, mesh=grouped, in_specs=in_specs, out_specs=out_specs, check_vma=False)
```

```python
import jax
import jax.numpy as jnp
from jax import lax
from jax.experimental import pallas as pl
from jax.sharding import PartitionSpec as P

K = 128
BLOCK = 128
EITERS = 4
PARTS = 2


init_variance = 4.0


def variance_tables(obs_precision, drift_var):

    def forward_step(prior_var, precision):
        denominator = 1.0 + prior_var * precision
        gain_now = prior_var * precision / denominator
        filt_var = prior_var / denominator
        return (filt_var + drift_var, (gain_now, filt_var))

    start_var = jnp.full(drift_var.shape, init_variance, dtype=jnp.float32)
    last_var, (gains, filt_vars) = lax.scan(forward_step, start_var, obs_precision, unroll=True)

    def backward_step(info_next, precision):
        merged = info_next + precision
        shrink = 1.0 / (1.0 + drift_var * merged)
        info_now = merged * shrink
        return (info_now, (shrink, info_now))

    zero_info = jnp.zeros(drift_var.shape, dtype=jnp.float32)
    last_info, (shrinks, infos) = lax.scan(
        backward_step, zero_info, obs_precision[1:], reverse=True
    )
    shrinks = jnp.concatenate([shrinks, jnp.ones_like(zero_info)[None]], axis=0)
    infos = jnp.concatenate([infos, zero_info[None]], axis=0)
    return (gains, filt_vars, shrinks, infos)


def e_step(looked, word_counts, topic_prior):
    counts_float = word_counts.astype(jnp.float32)
    doc_topics = topic_prior + jnp.sum(counts_float, axis=-1, keepdims=True) / K
    scores = looked.astype(jnp.float32)
    for sweep in range(EITERS):
        logits = lax.digamma(doc_topics)[..., None, :] + scores
        peak = lax.optimization_barrier(jnp.max(logits, axis=-1, keepdims=True))
        raised = jnp.exp(logits - peak)
        total = lax.optimization_barrier(jnp.sum(raised, axis=-1, keepdims=True))
        resp = raised / total
        doc_topics = topic_prior + jnp.sum(counts_float[..., None] * resp, axis=-2)
    weighted = to_bf16(counts_float[..., None] * resp)
    return (doc_topics, weighted)


def to_bf16(value):
    return lax.reduce_precision(value, exponent_bits=8, mantissa_bits=7).astype(jnp.bfloat16)


def shift_axis(value, axis, s):
    count = lax.axis_size(axis)
    return lax.ppermute(value, axis, [(i, (i + s) % count) for i in range(count)])


def shift_doc(value, s):
    return shift_axis(value, "doc", s)


def kalman_kernel(gain_ref, pull_ref, start_ref, after_ref, pseudo_ref, out_ref, last_ref):
    years = pseudo_ref.shape[0]
    mean = start_ref[...]
    for t in range(years):
        gain_now = gain_ref[pl.ds(t, 1), :]
        mean = (1.0 - gain_now) * mean + gain_now * pseudo_ref[t]
        out_ref[t] = mean
    last_ref[...] = mean
    mean = after_ref[...]
    for t in reversed(range(years)):
        pull_now = pull_ref[pl.ds(t, 1), :]
        mean = pull_now * mean + (1.0 - pull_now) * out_ref[t]
        out_ref[t] = mean


def kalman(gains, pulls, start, after, by_year):
    years, rows, topics = by_year.shape
    block = rows
    whole = pl.BlockSpec((years, topics), lambda i: (0, 0))
    edge = pl.BlockSpec((block, topics), lambda i: (i, 0))
    stack = pl.BlockSpec((years, block, topics), lambda i: (0, i, 0))
    return pl.pallas_call(
        kalman_kernel,
        grid=(rows // block,),
        in_specs=[whole, whole, edge, edge, stack],
        out_specs=(stack, edge),
        out_shape=(
            jax.ShapeDtypeStruct(by_year.shape, jnp.float32),
            jax.ShapeDtypeStruct(start.shape, jnp.float32),
        ),
    )(gains, pulls, start, after, by_year)


def group_maps(gains, pulls, groups):
    gains_g = gains.reshape(groups, -1, gains.shape[-1])
    pulls_g = pulls.reshape(groups, -1, pulls.shape[-1])
    span = gains_g.shape[1]
    carry = jnp.ones_like(gains_g[:, 0])
    responses = []
    for i in range(span):
        carry = (1.0 - gains_g[:, i]) * carry
        responses.append(carry)
    from_start = jnp.zeros_like(carry)
    from_after = jnp.ones_like(carry)
    for i in reversed(range(span)):
        from_start = pulls_g[:, i] * from_start + (1.0 - pulls_g[:, i]) * responses[i]
        from_after = pulls_g[:, i] * from_after
    return carry, from_start, from_after


def body(beta, word_ids, word_counts, block_slot, topic_prior, drift_var, obs_precision):
    local_beta = beta[0]
    own_words = local_beta.shape[0]
    topics = local_beta.shape[1]
    doc_devices = lax.axis_size("doc")
    doc_place = lax.axis_index("doc")
    local_peak = jnp.max(local_beta, axis=0)
    local_total = jnp.sum(jnp.exp(local_beta - local_peak), axis=0)

    slot_ids = word_ids[0]
    local_docs = slot_ids.shape[0]
    slot_width = slot_ids.shape[1]

    ints = jnp.stack([slot_ids, word_counts[0]])
    stats = jnp.stack([local_peak, local_total])
    ints_seen = [ints] + [shift_doc(ints, s) for s in range(1, doc_devices)]
    stats_seen = jnp.stack([stats] + [shift_doc(stats, s) for s in range(1, doc_devices)])
    all_ids = jnp.concatenate([part[0] for part in ints_seen], axis=0)
    block_match = (all_ids // BLOCK)[..., None] == lax.iota(jnp.int32, block_slot.shape[0])
    all_columns = (
        jnp.sum(jnp.where(block_match, block_slot, 0), axis=-1) * BLOCK + all_ids % BLOCK
    )
    all_counts = jnp.concatenate([part[1] for part in ints_seen], axis=0)
    peaks = stats_seen[:, 0]
    totals = stats_seen[:, 1]
    peak_value = jnp.max(peaks, axis=0)
    total_value = jnp.sum(totals * jnp.exp(peaks - peak_value), axis=0)
    normalizer = peak_value + jnp.log(total_value)

    flat_columns = all_columns.reshape(-1)
    local_columns = flat_columns - doc_place * own_words
    row_words = lax.iota(jnp.int32, own_words)
    marks = (row_words[:, None] == local_columns[None, :]).astype(jnp.bfloat16)
    table = to_bf16(local_beta - normalizer)
    partial = (
        lax.dot_general(marks, table, (((0,), (0,)), ((), ())), preferred_element_type=jnp.float32)
        .astype(jnp.bfloat16)
        .reshape(doc_devices, local_docs * slot_width, topics)
    )
    looked = partial
    for s in range(1, doc_devices):
        looked = looked + jnp.roll(shift_doc(partial, s), s, axis=0)
    looked = looked.reshape(local_docs * doc_devices, slot_width, topics)

    doc_topics_all, weighted = e_step(looked, all_counts, topic_prior)
    doc_topics = doc_topics_all[:local_docs]

    flat_weighted = weighted.reshape(-1, topics)
    counts = jnp.dot(marks, flat_weighted, preferred_element_type=jnp.float32)
    pseudo = local_beta + jnp.log1p(counts)

    gains, filt_vars, shrinks, infos = variance_tables(obs_precision, drift_var)
    years_total = obs_precision.shape[0]
    pulls = filt_vars / (filt_vars + drift_var)
    pulls = pulls.at[-1].set(0.0)

    span = lax.axis_size("tl")
    chunk = own_words // span
    by_dest = pseudo.reshape(span, chunk, topics)
    parts = PARTS if chunk % (8 * PARTS) == 0 else 1
    rows = chunk // parts
    done = [
        smooth_part(by_dest[:, i * rows:(i + 1) * rows], gains, pulls) for i in range(parts)
    ]
    back = jnp.concatenate(done, axis=1)
    return (back.reshape(own_words, topics)[None], doc_topics[None])


def smooth_part(by_dest, gains, pulls):
    groups = lax.axis_size("tg")
    span, rows, topics = by_dest.shape
    group = lax.axis_index("tg")
    by_year = lax.all_to_all(by_dest, "tl", split_axis=0, concat_axis=0, tiled=True)
    gains_here = lax.dynamic_slice_in_dim(gains, group * span, span, 0)
    pulls_here = lax.dynamic_slice_in_dim(pulls, group * span, span, 0)
    zero_mean = jnp.zeros((rows, topics), jnp.float32)
    if groups == 1:
        smoothed, _ = kalman(gains_here, pulls_here, zero_mean, zero_mean, by_year)
    else:
        local_smoothed, local_last = kalman(gains_here, pulls_here, zero_mean, zero_mean, by_year)
        summary = jnp.stack([local_last, local_smoothed[0]])
        if groups == 2:
            sent = jnp.where(group == 0, local_last, local_smoothed[0])
            other = shift_axis(sent, "tg", 1)
            ordered = jnp.where(
                group == 0, jnp.stack([summary, jnp.stack([other, other])]),
                jnp.stack([jnp.stack([other, other]), summary]),
            )
        else:
            seen = [summary] + [shift_axis(summary, "tg", s) for s in range(1, groups)]
            ordered = jnp.stack(seen)[(group - jnp.arange(groups)) % groups]
        carry, from_start, from_after = group_maps(gains, pulls, groups)
        entering = [zero_mean]
        for g in range(groups - 1):
            entering.append(ordered[g, 0] + carry[g] * entering[g])
        leaving = [zero_mean] * groups
        for g in reversed(range(1, groups)):
            leaving[g - 1] = (
                ordered[g, 1] + from_start[g] * entering[g] + from_after[g] * leaving[g]
            )
        start = jnp.stack(entering)[group]
        after = jnp.stack(leaving)[group]
        smoothed, _ = kalman(gains_here, pulls_here, start, after, by_year)
    return lax.all_to_all(smoothed, "tl", split_axis=0, concat_axis=0, tiled=True)


def solution(mesh):
    years = mesh.shape["tm"]
    span = 8 if years % 8 == 0 else years
    devices = mesh.devices.reshape(years // span, span, mesh.shape["doc"])
    grouped = jax.sharding.Mesh(devices, ("tg", "tl", "doc"))
    split = P(("tg", "tl"), "doc", None)
    in_specs = (split, split, split, P(), P(), P(), P())
    out_specs = (split, split)
    return jax.shard_map(body, mesh=grouped, in_specs=in_specs, out_specs=out_specs, check_vma=False)
```

```python
import jax
import jax.numpy as jnp
from jax import lax
from jax.experimental import pallas as pl
from jax.sharding import PartitionSpec as P

K = 128
BLOCK = 128
EITERS = 4
PARTS = 1


init_variance = 4.0


def variance_tables(obs_precision, drift_var):

    def forward_step(prior_var, precision):
        denominator = 1.0 + prior_var * precision
        gain_now = prior_var * precision / denominator
        filt_var = prior_var / denominator
        return (filt_var + drift_var, (gain_now, filt_var))

    start_var = jnp.full(drift_var.shape, init_variance, dtype=jnp.float32)
    last_var, (gains, filt_vars) = lax.scan(forward_step, start_var, obs_precision, unroll=True)

    def backward_step(info_next, precision):
        merged = info_next + precision
        shrink = 1.0 / (1.0 + drift_var * merged)
        info_now = merged * shrink
        return (info_now, (shrink, info_now))

    zero_info = jnp.zeros(drift_var.shape, dtype=jnp.float32)
    last_info, (shrinks, infos) = lax.scan(
        backward_step, zero_info, obs_precision[1:], reverse=True
    )
    shrinks = jnp.concatenate([shrinks, jnp.ones_like(zero_info)[None]], axis=0)
    infos = jnp.concatenate([infos, zero_info[None]], axis=0)
    return (gains, filt_vars, shrinks, infos)


def e_step(looked, word_counts, topic_prior):
    counts_float = word_counts.astype(jnp.float32)
    doc_topics = topic_prior + jnp.sum(counts_float, axis=-1, keepdims=True) / K
    scores = looked.astype(jnp.float32)
    for sweep in range(EITERS):
        logits = lax.digamma(doc_topics)[..., None, :] + scores
        peak = lax.optimization_barrier(jnp.max(logits, axis=-1, keepdims=True))
        raised = jnp.exp(logits - peak)
        total = lax.optimization_barrier(jnp.sum(raised, axis=-1, keepdims=True))
        resp = raised / total
        doc_topics = topic_prior + jnp.sum(counts_float[..., None] * resp, axis=-2)
    weighted = to_bf16(counts_float[..., None] * resp)
    return (doc_topics, weighted)


def to_bf16(value):
    return lax.reduce_precision(value, exponent_bits=8, mantissa_bits=7).astype(jnp.bfloat16)


def shift_axis(value, axis, s):
    count = lax.axis_size(axis)
    return lax.ppermute(value, axis, [(i, (i + s) % count) for i in range(count)])


def shift_doc(value, s):
    return shift_axis(value, "doc", s)


def kalman_kernel(gain_ref, pull_ref, start_ref, after_ref, pseudo_ref, out_ref, last_ref):
    years = pseudo_ref.shape[0]
    mean = start_ref[...]
    for t in range(years):
        gain_now = gain_ref[pl.ds(t, 1), :]
        mean = (1.0 - gain_now) * mean + gain_now * pseudo_ref[t]
        out_ref[t] = mean
    last_ref[...] = mean
    mean = after_ref[...]
    for t in reversed(range(years)):
        pull_now = pull_ref[pl.ds(t, 1), :]
        mean = pull_now * mean + (1.0 - pull_now) * out_ref[t]
        out_ref[t] = mean


def kalman(gains, pulls, start, after, by_year):
    years, rows, topics = by_year.shape
    block = rows
    whole = pl.BlockSpec((years, topics), lambda i: (0, 0))
    edge = pl.BlockSpec((block, topics), lambda i: (i, 0))
    stack = pl.BlockSpec((years, block, topics), lambda i: (0, i, 0))
    return pl.pallas_call(
        kalman_kernel,
        grid=(rows // block,),
        in_specs=[whole, whole, edge, edge, stack],
        out_specs=(stack, edge),
        out_shape=(
            jax.ShapeDtypeStruct(by_year.shape, jnp.float32),
            jax.ShapeDtypeStruct(start.shape, jnp.float32),
        ),
    )(gains, pulls, start, after, by_year)


def group_maps(gains, pulls, groups):
    gains_g = gains.reshape(groups, -1, gains.shape[-1])
    pulls_g = pulls.reshape(groups, -1, pulls.shape[-1])
    span = gains_g.shape[1]
    carry = jnp.ones_like(gains_g[:, 0])
    responses = []
    for i in range(span):
        carry = (1.0 - gains_g[:, i]) * carry
        responses.append(carry)
    from_start = jnp.zeros_like(carry)
    from_after = jnp.ones_like(carry)
    for i in reversed(range(span)):
        from_start = pulls_g[:, i] * from_start + (1.0 - pulls_g[:, i]) * responses[i]
        from_after = pulls_g[:, i] * from_after
    return carry, from_start, from_after


def body(beta, word_ids, word_counts, block_slot, topic_prior, drift_var, obs_precision):
    local_beta = beta[0]
    own_words = local_beta.shape[0]
    topics = local_beta.shape[1]
    doc_devices = lax.axis_size("doc")
    doc_place = lax.axis_index("doc")
    local_peak = jnp.max(local_beta, axis=0)
    local_total = jnp.sum(jnp.exp(local_beta - local_peak), axis=0)

    slot_ids = word_ids[0]
    local_docs = slot_ids.shape[0]
    slot_width = slot_ids.shape[1]

    per_docs = local_docs * slot_width
    message = jnp.concatenate([
        slot_ids.reshape(-1).astype(jnp.float32),
        word_counts[0].reshape(-1).astype(jnp.float32),
        local_peak,
        local_total,
    ])
    seen = jnp.stack([message] + [shift_doc(message, s) for s in range(1, doc_devices)])
    ints_seen = [
        seen[:, :2 * per_docs].astype(jnp.int32).reshape(doc_devices, 2, local_docs, slot_width)[i]
        for i in range(doc_devices)
    ]
    stats_seen = seen[:, 2 * per_docs:].reshape(doc_devices, 2, topics)
    all_ids = jnp.concatenate([part[0] for part in ints_seen], axis=0)
    block_match = (all_ids // BLOCK)[..., None] == lax.iota(jnp.int32, block_slot.shape[0])
    all_columns = (
        jnp.sum(jnp.where(block_match, block_slot, 0), axis=-1) * BLOCK + all_ids % BLOCK
    )
    all_counts = jnp.concatenate([part[1] for part in ints_seen], axis=0)
    peaks = stats_seen[:, 0]
    totals = stats_seen[:, 1]
    peak_value = jnp.max(peaks, axis=0)
    total_value = jnp.sum(totals * jnp.exp(peaks - peak_value), axis=0)
    normalizer = peak_value + jnp.log(total_value)

    flat_columns = all_columns.reshape(-1)
    local_columns = flat_columns - doc_place * own_words
    row_words = lax.iota(jnp.int32, own_words)
    marks = (row_words[:, None] == local_columns[None, :]).astype(jnp.bfloat16)
    table = to_bf16(local_beta - normalizer)
    partial = (
        lax.dot_general(marks, table, (((0,), (0,)), ((), ())), preferred_element_type=jnp.float32)
        .astype(jnp.bfloat16)
        .reshape(doc_devices, local_docs * slot_width, topics)
    )
    looked = partial
    for s in range(1, doc_devices):
        looked = looked + jnp.roll(shift_doc(partial, s), s, axis=0)
    looked = looked.reshape(local_docs * doc_devices, slot_width, topics)

    doc_topics_all, weighted = e_step(looked, all_counts, topic_prior)
    doc_topics = doc_topics_all[:local_docs]

    flat_weighted = weighted.reshape(-1, topics)
    counts = jnp.dot(marks, flat_weighted, preferred_element_type=jnp.float32)
    pseudo = local_beta + jnp.log1p(counts)

    gains, filt_vars, shrinks, infos = variance_tables(obs_precision, drift_var)
    years_total = obs_precision.shape[0]
    pulls = filt_vars / (filt_vars + drift_var)
    pulls = pulls.at[-1].set(0.0)

    span = lax.axis_size("tl")
    chunk = own_words // span
    by_dest = pseudo.reshape(span, chunk, topics)
    parts = PARTS if chunk % (8 * PARTS) == 0 else 1
    rows = chunk // parts
    done = [
        smooth_part(by_dest[:, i * rows:(i + 1) * rows], gains, pulls) for i in range(parts)
    ]
    back = jnp.concatenate(done, axis=1)
    return (back.reshape(own_words, topics)[None], doc_topics[None])


def smooth_part(by_dest, gains, pulls):
    groups = lax.axis_size("tg")
    span, rows, topics = by_dest.shape
    group = lax.axis_index("tg")
    by_year = lax.all_to_all(by_dest, "tl", split_axis=0, concat_axis=0, tiled=True)
    gains_here = lax.dynamic_slice_in_dim(gains, group * span, span, 0)
    pulls_here = lax.dynamic_slice_in_dim(pulls, group * span, span, 0)
    zero_mean = jnp.zeros((rows, topics), jnp.float32)
    if groups == 1:
        smoothed, _ = kalman(gains_here, pulls_here, zero_mean, zero_mean, by_year)
    else:
        local_smoothed, local_last = kalman(gains_here, pulls_here, zero_mean, zero_mean, by_year)
        summary = jnp.stack([local_last, local_smoothed[0]])
        if groups == 2:
            sent = jnp.where(group == 0, local_last, local_smoothed[0])
            other = shift_axis(sent, "tg", 1)
            ordered = jnp.where(
                group == 0, jnp.stack([summary, jnp.stack([other, other])]),
                jnp.stack([jnp.stack([other, other]), summary]),
            )
        else:
            seen = [summary] + [shift_axis(summary, "tg", s) for s in range(1, groups)]
            ordered = jnp.stack(seen)[(group - jnp.arange(groups)) % groups]
        carry, from_start, from_after = group_maps(gains, pulls, groups)
        entering = [zero_mean]
        for g in range(groups - 1):
            entering.append(ordered[g, 0] + carry[g] * entering[g])
        leaving = [zero_mean] * groups
        for g in reversed(range(1, groups)):
            leaving[g - 1] = (
                ordered[g, 1] + from_start[g] * entering[g] + from_after[g] * leaving[g]
            )
        start = jnp.stack(entering)[group]
        after = jnp.stack(leaving)[group]
        smoothed, _ = kalman(gains_here, pulls_here, start, after, by_year)
    return lax.all_to_all(smoothed, "tl", split_axis=0, concat_axis=0, tiled=True)


def solution(mesh):
    years = mesh.shape["tm"]
    span = 8 if years % 8 == 0 else years
    devices = mesh.devices.reshape(years // span, span, mesh.shape["doc"])
    grouped = jax.sharding.Mesh(devices, ("tg", "tl", "doc"))
    split = P(("tg", "tl"), "doc", None)
    in_specs = (split, split, split, P(), P(), P(), P())
    out_specs = (split, split)
    return jax.shard_map(body, mesh=grouped, in_specs=in_specs, out_specs=out_specs, check_vma=False)
```

```python
import jax
import jax.numpy as jnp
from jax import lax
from jax.experimental import pallas as pl
from jax.experimental.pallas import tpu as pltpu
from jax.sharding import PartitionSpec as P

K = 128
BLOCK = 128
EITERS = 4
PARTS = 1


init_variance = 4.0


def variance_tables(obs_precision, drift_var):

    def forward_step(prior_var, precision):
        denominator = 1.0 + prior_var * precision
        gain_now = prior_var * precision / denominator
        filt_var = prior_var / denominator
        return (filt_var + drift_var, (gain_now, filt_var))

    start_var = jnp.full(drift_var.shape, init_variance, dtype=jnp.float32)
    last_var, (gains, filt_vars) = lax.scan(forward_step, start_var, obs_precision, unroll=True)

    def backward_step(info_next, precision):
        merged = info_next + precision
        shrink = 1.0 / (1.0 + drift_var * merged)
        info_now = merged * shrink
        return (info_now, (shrink, info_now))

    zero_info = jnp.zeros(drift_var.shape, dtype=jnp.float32)
    last_info, (shrinks, infos) = lax.scan(
        backward_step, zero_info, obs_precision[1:], reverse=True
    )
    shrinks = jnp.concatenate([shrinks, jnp.ones_like(zero_info)[None]], axis=0)
    infos = jnp.concatenate([infos, zero_info[None]], axis=0)
    return (gains, filt_vars, shrinks, infos)


def e_step(looked, word_counts, topic_prior):
    counts_float = word_counts.astype(jnp.float32)
    doc_topics = topic_prior + jnp.sum(counts_float, axis=-1, keepdims=True) / K
    scores = looked.astype(jnp.float32)
    for sweep in range(EITERS):
        logits = lax.digamma(doc_topics)[..., None, :] + scores
        peak = lax.optimization_barrier(jnp.max(logits, axis=-1, keepdims=True))
        raised = jnp.exp(logits - peak)
        total = lax.optimization_barrier(jnp.sum(raised, axis=-1, keepdims=True))
        resp = raised / total
        doc_topics = topic_prior + jnp.sum(counts_float[..., None] * resp, axis=-2)
    weighted = to_bf16(counts_float[..., None] * resp)
    return (doc_topics, weighted)


def to_bf16(value):
    return lax.reduce_precision(value, exponent_bits=8, mantissa_bits=7).astype(jnp.bfloat16)


def shift_axis(value, axis, s):
    count = lax.axis_size(axis)
    return lax.ppermute(value, axis, [(i, (i + s) % count) for i in range(count)])


def shift_doc(value, s):
    return shift_axis(value, "doc", s)


def kalman_kernel(gain_ref, pull_ref, start_ref, after_ref, pseudo_ref, out_ref, last_ref):
    years = pseudo_ref.shape[0]
    mean = start_ref[...]
    for t in range(years):
        gain_now = gain_ref[pl.ds(t, 1), :]
        mean = (1.0 - gain_now) * mean + gain_now * pseudo_ref[t]
        out_ref[t] = mean
    last_ref[...] = mean
    mean = after_ref[...]
    for t in reversed(range(years)):
        pull_now = pull_ref[pl.ds(t, 1), :]
        mean = pull_now * mean + (1.0 - pull_now) * out_ref[t]
        out_ref[t] = mean


def kalman(gains, pulls, start, after, by_year):
    years, rows, topics = by_year.shape
    block = rows
    whole = pl.BlockSpec((years, topics), lambda i: (0, 0))
    edge = pl.BlockSpec((block, topics), lambda i: (i, 0))
    stack = pl.BlockSpec((years, block, topics), lambda i: (0, i, 0))
    return pl.pallas_call(
        kalman_kernel,
        grid=(rows // block,),
        in_specs=[whole, whole, edge, edge, stack],
        out_specs=(stack, edge),
        out_shape=(
            jax.ShapeDtypeStruct(by_year.shape, jnp.float32),
            jax.ShapeDtypeStruct(start.shape, jnp.float32),
        ),
    )(gains, pulls, start, after, by_year)


def first_pass_kernel(gain_ref, pull_ref, weight_ref, pseudo_ref, sent_ref, last_ref, filt_ref):
    years = pseudo_ref.shape[0]
    mean = jnp.zeros(pseudo_ref.shape[1:], jnp.float32)
    for t in range(years):
        gain_now = gain_ref[pl.ds(t, 1), :]
        mean = (1.0 - gain_now) * mean + gain_now * pseudo_ref[t]
        filt_ref[t] = mean
    last = mean
    mean = jnp.zeros(pseudo_ref.shape[1:], jnp.float32)
    for t in reversed(range(years)):
        pull_now = pull_ref[pl.ds(t, 1), :]
        mean = pull_now * mean + (1.0 - pull_now) * filt_ref[t]
    weight = weight_ref[...]
    sent_ref[...] = weight * last + (1.0 - weight) * mean
    last_ref[...] = last


def second_pass_kernel(
    gain_ref, pull_ref, weight_ref, reach_ref, other_ref, last_ref, pseudo_ref, out_ref
):
    years = pseudo_ref.shape[0]
    weight = weight_ref[...]
    other = other_ref[...]
    mean = (1.0 - weight) * other
    for t in range(years):
        gain_now = gain_ref[pl.ds(t, 1), :]
        mean = (1.0 - gain_now) * mean + gain_now * pseudo_ref[t]
        out_ref[t] = mean
    mean = weight * (other + reach_ref[...] * last_ref[...])
    for t in reversed(range(years)):
        pull_now = pull_ref[pl.ds(t, 1), :]
        mean = pull_now * mean + (1.0 - pull_now) * out_ref[t]
        out_ref[t] = mean


def two_group_kalman(gains_here, pulls_here, weight, reach, by_year):
    years, rows, topics = by_year.shape
    edge = jax.ShapeDtypeStruct((rows, topics), jnp.float32)
    sent, last = pl.pallas_call(
        first_pass_kernel,
        out_shape=(edge, edge),
        scratch_shapes=[pltpu.VMEM(by_year.shape, jnp.float32)],
    )(gains_here, pulls_here, weight, by_year)
    other = shift_axis(sent, "tg", 1)
    return pl.pallas_call(
        second_pass_kernel, out_shape=jax.ShapeDtypeStruct(by_year.shape, jnp.float32)
    )(gains_here, pulls_here, weight, reach, other, last, by_year)


def group_maps(gains, pulls, groups):
    gains_g = gains.reshape(groups, -1, gains.shape[-1])
    pulls_g = pulls.reshape(groups, -1, pulls.shape[-1])
    span = gains_g.shape[1]
    carry = jnp.ones_like(gains_g[:, 0])
    responses = []
    for i in range(span):
        carry = (1.0 - gains_g[:, i]) * carry
        responses.append(carry)
    from_start = jnp.zeros_like(carry)
    from_after = jnp.ones_like(carry)
    for i in reversed(range(span)):
        from_start = pulls_g[:, i] * from_start + (1.0 - pulls_g[:, i]) * responses[i]
        from_after = pulls_g[:, i] * from_after
    return carry, from_start, from_after


def body(beta, word_ids, word_counts, block_slot, topic_prior, drift_var, obs_precision):
    local_beta = beta[0]
    own_words = local_beta.shape[0]
    topics = local_beta.shape[1]
    doc_devices = lax.axis_size("doc")
    doc_place = lax.axis_index("doc")
    local_peak = jnp.max(local_beta, axis=0)
    local_total = jnp.sum(jnp.exp(local_beta - local_peak), axis=0)

    slot_ids = word_ids[0]
    local_docs = slot_ids.shape[0]
    slot_width = slot_ids.shape[1]

    per_docs = local_docs * slot_width
    message = jnp.concatenate([
        slot_ids.reshape(-1).astype(jnp.float32),
        word_counts[0].reshape(-1).astype(jnp.float32),
        local_peak,
        local_total,
    ])
    seen = jnp.stack([message] + [shift_doc(message, s) for s in range(1, doc_devices)])
    ints_seen = [
        seen[:, :2 * per_docs].astype(jnp.int32).reshape(doc_devices, 2, local_docs, slot_width)[i]
        for i in range(doc_devices)
    ]
    stats_seen = seen[:, 2 * per_docs:].reshape(doc_devices, 2, topics)
    all_ids = jnp.concatenate([part[0] for part in ints_seen], axis=0)
    block_match = (all_ids // BLOCK)[..., None] == lax.iota(jnp.int32, block_slot.shape[0])
    all_columns = (
        jnp.sum(jnp.where(block_match, block_slot, 0), axis=-1) * BLOCK + all_ids % BLOCK
    )
    all_counts = jnp.concatenate([part[1] for part in ints_seen], axis=0)
    peaks = stats_seen[:, 0]
    totals = stats_seen[:, 1]
    peak_value = jnp.max(peaks, axis=0)
    total_value = jnp.sum(totals * jnp.exp(peaks - peak_value), axis=0)
    normalizer = peak_value + jnp.log(total_value)

    flat_columns = all_columns.reshape(-1)
    local_columns = flat_columns - doc_place * own_words
    row_words = lax.iota(jnp.int32, own_words)
    marks = (row_words[:, None] == local_columns[None, :]).astype(jnp.bfloat16)
    table = to_bf16(local_beta - normalizer)
    partial = (
        lax.dot_general(marks, table, (((0,), (0,)), ((), ())), preferred_element_type=jnp.float32)
        .astype(jnp.bfloat16)
        .reshape(doc_devices, local_docs * slot_width, topics)
    )
    looked = partial
    for s in range(1, doc_devices):
        looked = looked + jnp.roll(shift_doc(partial, s), s, axis=0)
    looked = looked.reshape(local_docs * doc_devices, slot_width, topics)

    doc_topics_all, weighted = e_step(looked, all_counts, topic_prior)
    doc_topics = doc_topics_all[:local_docs]

    flat_weighted = weighted.reshape(-1, topics)
    counts = jnp.dot(marks, flat_weighted, preferred_element_type=jnp.float32)
    pseudo = local_beta + jnp.log1p(counts)

    gains, filt_vars, shrinks, infos = variance_tables(obs_precision, drift_var)
    years_total = obs_precision.shape[0]
    pulls = filt_vars / (filt_vars + drift_var)
    pulls = pulls.at[-1].set(0.0)

    span = lax.axis_size("tl")
    chunk = own_words // span
    by_dest = pseudo.reshape(span, chunk, topics)
    parts = PARTS if chunk % (8 * PARTS) == 0 else 1
    rows = chunk // parts
    done = [
        smooth_part(by_dest[:, i * rows:(i + 1) * rows], gains, pulls) for i in range(parts)
    ]
    back = jnp.concatenate(done, axis=1)
    return (back.reshape(own_words, topics)[None], doc_topics[None])


def smooth_part(by_dest, gains, pulls):
    groups = lax.axis_size("tg")
    span, rows, topics = by_dest.shape
    group = lax.axis_index("tg")
    by_year = lax.all_to_all(by_dest, "tl", split_axis=0, concat_axis=0, tiled=True)
    gains_here = lax.dynamic_slice_in_dim(gains, group * span, span, 0)
    pulls_here = lax.dynamic_slice_in_dim(pulls, group * span, span, 0)
    zero_mean = jnp.zeros((rows, topics), jnp.float32)
    if groups == 1:
        smoothed, _ = kalman(gains_here, pulls_here, zero_mean, zero_mean, by_year)
    elif groups == 2:
        carry, from_start, from_after = group_maps(gains, pulls, groups)
        weight = jnp.where(group == 0, 1.0, 0.0) * jnp.ones((1, topics), jnp.float32)
        smoothed = two_group_kalman(gains_here, pulls_here, weight, from_start[1:2], by_year)
    else:
        local_smoothed, local_last = kalman(gains_here, pulls_here, zero_mean, zero_mean, by_year)
        summary = jnp.stack([local_last, local_smoothed[0]])
        if groups == 2:
            sent = jnp.where(group == 0, local_last, local_smoothed[0])
            other = shift_axis(sent, "tg", 1)
            ordered = jnp.where(
                group == 0, jnp.stack([summary, jnp.stack([other, other])]),
                jnp.stack([jnp.stack([other, other]), summary]),
            )
        else:
            seen = [summary] + [shift_axis(summary, "tg", s) for s in range(1, groups)]
            ordered = jnp.stack(seen)[(group - jnp.arange(groups)) % groups]
        carry, from_start, from_after = group_maps(gains, pulls, groups)
        entering = [zero_mean]
        for g in range(groups - 1):
            entering.append(ordered[g, 0] + carry[g] * entering[g])
        leaving = [zero_mean] * groups
        for g in reversed(range(1, groups)):
            leaving[g - 1] = (
                ordered[g, 1] + from_start[g] * entering[g] + from_after[g] * leaving[g]
            )
        start = jnp.stack(entering)[group]
        after = jnp.stack(leaving)[group]
        smoothed, _ = kalman(gains_here, pulls_here, start, after, by_year)
    return lax.all_to_all(smoothed, "tl", split_axis=0, concat_axis=0, tiled=True)


def solution(mesh):
    years = mesh.shape["tm"]
    span = 8 if years % 8 == 0 else years
    devices = mesh.devices.reshape(years // span, span, mesh.shape["doc"])
    grouped = jax.sharding.Mesh(devices, ("tg", "tl", "doc"))
    split = P(("tg", "tl"), "doc", None)
    in_specs = (split, split, split, P(), P(), P(), P())
    out_specs = (split, split)
    return jax.shard_map(body, mesh=grouped, in_specs=in_specs, out_specs=out_specs, check_vma=False)
```

```python
import jax
import jax.numpy as jnp
from jax import lax
from jax.experimental import pallas as pl
from jax.experimental.pallas import tpu as pltpu
from jax.sharding import PartitionSpec as P

K = 128
BLOCK = 128
EITERS = 4
PARTS = 1


init_variance = 4.0


def variance_tables(obs_precision, drift_var):

    def forward_step(prior_var, precision):
        denominator = 1.0 + prior_var * precision
        gain_now = prior_var * precision / denominator
        filt_var = prior_var / denominator
        return (filt_var + drift_var, (gain_now, filt_var))

    start_var = jnp.full(drift_var.shape, init_variance, dtype=jnp.float32)
    last_var, (gains, filt_vars) = lax.scan(forward_step, start_var, obs_precision, unroll=True)

    def backward_step(info_next, precision):
        merged = info_next + precision
        shrink = 1.0 / (1.0 + drift_var * merged)
        info_now = merged * shrink
        return (info_now, (shrink, info_now))

    zero_info = jnp.zeros(drift_var.shape, dtype=jnp.float32)
    last_info, (shrinks, infos) = lax.scan(
        backward_step, zero_info, obs_precision[1:], reverse=True
    )
    shrinks = jnp.concatenate([shrinks, jnp.ones_like(zero_info)[None]], axis=0)
    infos = jnp.concatenate([infos, zero_info[None]], axis=0)
    return (gains, filt_vars, shrinks, infos)


def e_step(looked, word_counts, topic_prior):
    counts_float = word_counts.astype(jnp.float32)
    doc_topics = topic_prior + jnp.sum(counts_float, axis=-1, keepdims=True) / K
    scores = looked.astype(jnp.float32)
    for sweep in range(EITERS):
        logits = lax.digamma(doc_topics)[..., None, :] + scores
        peak = lax.optimization_barrier(jnp.max(logits, axis=-1, keepdims=True))
        raised = jnp.exp(logits - peak)
        total = lax.optimization_barrier(jnp.sum(raised, axis=-1, keepdims=True))
        resp = raised / total
        doc_topics = topic_prior + jnp.sum(counts_float[..., None] * resp, axis=-2)
    weighted = to_bf16(counts_float[..., None] * resp)
    return (doc_topics, weighted)


def to_bf16(value):
    return lax.reduce_precision(value, exponent_bits=8, mantissa_bits=7).astype(jnp.bfloat16)


def shift_axis(value, axis, s):
    count = lax.axis_size(axis)
    return lax.ppermute(value, axis, [(i, (i + s) % count) for i in range(count)])


def shift_doc(value, s):
    return shift_axis(value, "doc", s)


def kalman_kernel(gain_ref, pull_ref, start_ref, after_ref, pseudo_ref, out_ref, last_ref):
    years = pseudo_ref.shape[0]
    mean = start_ref[...]
    for t in range(years):
        gain_now = gain_ref[pl.ds(t, 1), :]
        mean = (1.0 - gain_now) * mean + gain_now * pseudo_ref[t]
        out_ref[t] = mean
    last_ref[...] = mean
    mean = after_ref[...]
    for t in reversed(range(years)):
        pull_now = pull_ref[pl.ds(t, 1), :]
        mean = pull_now * mean + (1.0 - pull_now) * out_ref[t]
        out_ref[t] = mean


def kalman(gains, pulls, start, after, by_year):
    years, rows, topics = by_year.shape
    block = rows
    whole = pl.BlockSpec((years, topics), lambda i: (0, 0))
    edge = pl.BlockSpec((block, topics), lambda i: (i, 0))
    stack = pl.BlockSpec((years, block, topics), lambda i: (0, i, 0))
    return pl.pallas_call(
        kalman_kernel,
        grid=(rows // block,),
        in_specs=[whole, whole, edge, edge, stack],
        out_specs=(stack, edge),
        out_shape=(
            jax.ShapeDtypeStruct(by_year.shape, jnp.float32),
            jax.ShapeDtypeStruct(start.shape, jnp.float32),
        ),
    )(gains, pulls, start, after, by_year)


def first_pass_kernel(gain_ref, pull_ref, pseudo_ref, sent_ref, last_ref, filt_ref):
    years = pseudo_ref.shape[0]
    group = lax.axis_index("tg")
    base = group * years
    mean = jnp.zeros(pseudo_ref.shape[1:], jnp.float32)
    for t in range(years):
        gain_now = gain_ref[pl.ds(base + t, 1), :]
        mean = (1.0 - gain_now) * mean + gain_now * pseudo_ref[t]
        filt_ref[t] = mean
    last = mean
    mean = jnp.zeros(pseudo_ref.shape[1:], jnp.float32)
    for t in reversed(range(years)):
        pull_now = pull_ref[pl.ds(base + t, 1), :]
        mean = pull_now * mean + (1.0 - pull_now) * filt_ref[t]
    weight = jnp.where(group == 0, 1.0, 0.0)
    sent_ref[...] = weight * last + (1.0 - weight) * mean
    last_ref[...] = last


def second_pass_kernel(gain_ref, pull_ref, other_ref, last_ref, pseudo_ref, out_ref):
    years = pseudo_ref.shape[0]
    group = lax.axis_index("tg")
    base = group * years
    weight = jnp.where(group == 0, 1.0, 0.0)
    carry = jnp.ones((1, gain_ref.shape[1]), jnp.float32)
    responses = []
    for t in range(years):
        carry = (1.0 - gain_ref[pl.ds(years + t, 1), :]) * carry
        responses.append(carry)
    reach = jnp.zeros_like(carry)
    for t in reversed(range(years)):
        pull_now = pull_ref[pl.ds(years + t, 1), :]
        reach = pull_now * reach + (1.0 - pull_now) * responses[t]
    other = other_ref[...]
    mean = (1.0 - weight) * other
    for t in range(years):
        gain_now = gain_ref[pl.ds(base + t, 1), :]
        mean = (1.0 - gain_now) * mean + gain_now * pseudo_ref[t]
        out_ref[t] = mean
    mean = weight * (other + reach * last_ref[...])
    for t in reversed(range(years)):
        pull_now = pull_ref[pl.ds(base + t, 1), :]
        mean = pull_now * mean + (1.0 - pull_now) * out_ref[t]
        out_ref[t] = mean


def two_group_kalman(gains, pulls, by_year):
    years, rows, topics = by_year.shape
    edge = jax.ShapeDtypeStruct((rows, topics), jnp.float32)
    sent, last = pl.pallas_call(
        first_pass_kernel,
        out_shape=(edge, edge),
        scratch_shapes=[pltpu.VMEM(by_year.shape, jnp.float32)],
    )(gains, pulls, by_year)
    other = shift_axis(sent, "tg", 1)
    return pl.pallas_call(
        second_pass_kernel, out_shape=jax.ShapeDtypeStruct(by_year.shape, jnp.float32)
    )(gains, pulls, other, last, by_year)


def group_maps(gains, pulls, groups):
    gains_g = gains.reshape(groups, -1, gains.shape[-1])
    pulls_g = pulls.reshape(groups, -1, pulls.shape[-1])
    span = gains_g.shape[1]
    carry = jnp.ones_like(gains_g[:, 0])
    responses = []
    for i in range(span):
        carry = (1.0 - gains_g[:, i]) * carry
        responses.append(carry)
    from_start = jnp.zeros_like(carry)
    from_after = jnp.ones_like(carry)
    for i in reversed(range(span)):
        from_start = pulls_g[:, i] * from_start + (1.0 - pulls_g[:, i]) * responses[i]
        from_after = pulls_g[:, i] * from_after
    return carry, from_start, from_after


def body(beta, word_ids, word_counts, block_slot, topic_prior, drift_var, obs_precision):
    local_beta = beta[0]
    own_words = local_beta.shape[0]
    topics = local_beta.shape[1]
    doc_devices = lax.axis_size("doc")
    doc_place = lax.axis_index("doc")
    local_peak = jnp.max(local_beta, axis=0)
    local_total = jnp.sum(jnp.exp(local_beta - local_peak), axis=0)

    slot_ids = word_ids[0]
    local_docs = slot_ids.shape[0]
    slot_width = slot_ids.shape[1]

    per_docs = local_docs * slot_width
    message = jnp.concatenate([
        slot_ids.reshape(-1).astype(jnp.float32),
        word_counts[0].reshape(-1).astype(jnp.float32),
        local_peak,
        local_total,
    ])
    seen = jnp.stack([message] + [shift_doc(message, s) for s in range(1, doc_devices)])
    ints_seen = [
        seen[:, :2 * per_docs].astype(jnp.int32).reshape(doc_devices, 2, local_docs, slot_width)[i]
        for i in range(doc_devices)
    ]
    stats_seen = seen[:, 2 * per_docs:].reshape(doc_devices, 2, topics)
    all_ids = jnp.concatenate([part[0] for part in ints_seen], axis=0)
    block_match = (all_ids // BLOCK)[..., None] == lax.iota(jnp.int32, block_slot.shape[0])
    all_columns = (
        jnp.sum(jnp.where(block_match, block_slot, 0), axis=-1) * BLOCK + all_ids % BLOCK
    )
    all_counts = jnp.concatenate([part[1] for part in ints_seen], axis=0)
    peaks = stats_seen[:, 0]
    totals = stats_seen[:, 1]
    peak_value = jnp.max(peaks, axis=0)
    total_value = jnp.sum(totals * jnp.exp(peaks - peak_value), axis=0)
    normalizer = peak_value + jnp.log(total_value)

    flat_columns = all_columns.reshape(-1)
    local_columns = flat_columns - doc_place * own_words
    row_words = lax.iota(jnp.int32, own_words)
    marks = (row_words[:, None] == local_columns[None, :]).astype(jnp.bfloat16)
    table = to_bf16(local_beta - normalizer)
    partial = (
        lax.dot_general(marks, table, (((0,), (0,)), ((), ())), preferred_element_type=jnp.float32)
        .astype(jnp.bfloat16)
        .reshape(doc_devices, local_docs * slot_width, topics)
    )
    looked = partial
    for s in range(1, doc_devices):
        looked = looked + jnp.roll(shift_doc(partial, s), s, axis=0)
    looked = looked.reshape(local_docs * doc_devices, slot_width, topics)

    doc_topics_all, weighted = e_step(looked, all_counts, topic_prior)
    doc_topics = doc_topics_all[:local_docs]

    flat_weighted = weighted.reshape(-1, topics)
    counts = jnp.dot(marks, flat_weighted, preferred_element_type=jnp.float32)
    pseudo = local_beta + jnp.log1p(counts)

    gains, filt_vars, shrinks, infos = variance_tables(obs_precision, drift_var)
    years_total = obs_precision.shape[0]
    pulls = filt_vars / (filt_vars + drift_var)
    pulls = pulls.at[-1].set(0.0)

    span = lax.axis_size("tl")
    chunk = own_words // span
    by_dest = pseudo.reshape(span, chunk, topics)
    parts = PARTS if chunk % (8 * PARTS) == 0 else 1
    rows = chunk // parts
    done = [
        smooth_part(by_dest[:, i * rows:(i + 1) * rows], gains, pulls) for i in range(parts)
    ]
    back = jnp.concatenate(done, axis=1)
    return (back.reshape(own_words, topics)[None], doc_topics[None])


def smooth_part(by_dest, gains, pulls):
    groups = lax.axis_size("tg")
    span, rows, topics = by_dest.shape
    group = lax.axis_index("tg")
    by_year = lax.all_to_all(by_dest, "tl", split_axis=0, concat_axis=0, tiled=True)
    gains_here = lax.dynamic_slice_in_dim(gains, group * span, span, 0)
    pulls_here = lax.dynamic_slice_in_dim(pulls, group * span, span, 0)
    zero_mean = jnp.zeros((rows, topics), jnp.float32)
    if groups == 1:
        smoothed, _ = kalman(gains_here, pulls_here, zero_mean, zero_mean, by_year)
    elif groups == 2:
        smoothed = two_group_kalman(gains, pulls, by_year)
    else:
        local_smoothed, local_last = kalman(gains_here, pulls_here, zero_mean, zero_mean, by_year)
        summary = jnp.stack([local_last, local_smoothed[0]])
        if groups == 2:
            sent = jnp.where(group == 0, local_last, local_smoothed[0])
            other = shift_axis(sent, "tg", 1)
            ordered = jnp.where(
                group == 0, jnp.stack([summary, jnp.stack([other, other])]),
                jnp.stack([jnp.stack([other, other]), summary]),
            )
        else:
            seen = [summary] + [shift_axis(summary, "tg", s) for s in range(1, groups)]
            ordered = jnp.stack(seen)[(group - jnp.arange(groups)) % groups]
        carry, from_start, from_after = group_maps(gains, pulls, groups)
        entering = [zero_mean]
        for g in range(groups - 1):
            entering.append(ordered[g, 0] + carry[g] * entering[g])
        leaving = [zero_mean] * groups
        for g in reversed(range(1, groups)):
            leaving[g - 1] = (
                ordered[g, 1] + from_start[g] * entering[g] + from_after[g] * leaving[g]
            )
        start = jnp.stack(entering)[group]
        after = jnp.stack(leaving)[group]
        smoothed, _ = kalman(gains_here, pulls_here, start, after, by_year)
    return lax.all_to_all(smoothed, "tl", split_axis=0, concat_axis=0, tiled=True)


def solution(mesh):
    years = mesh.shape["tm"]
    span = 8 if years % 8 == 0 else years
    devices = mesh.devices.reshape(years // span, span, mesh.shape["doc"])
    grouped = jax.sharding.Mesh(devices, ("tg", "tl", "doc"))
    split = P(("tg", "tl"), "doc", None)
    in_specs = (split, split, split, P(), P(), P(), P())
    out_specs = (split, split)
    return jax.shard_map(body, mesh=grouped, in_specs=in_specs, out_specs=out_specs, check_vma=False)
```

```python
import jax
import jax.numpy as jnp
from jax import lax
from jax.experimental import pallas as pl
from jax.experimental.pallas import tpu as pltpu
from jax.sharding import PartitionSpec as P

K = 128
BLOCK = 128
EITERS = 4
PARTS = 1


init_variance = 4.0


def variance_tables(obs_precision, drift_var):

    def forward_step(prior_var, precision):
        denominator = 1.0 + prior_var * precision
        gain_now = prior_var * precision / denominator
        filt_var = prior_var / denominator
        return (filt_var + drift_var, (gain_now, filt_var))

    start_var = jnp.full(drift_var.shape, init_variance, dtype=jnp.float32)
    last_var, (gains, filt_vars) = lax.scan(forward_step, start_var, obs_precision, unroll=True)

    def backward_step(info_next, precision):
        merged = info_next + precision
        shrink = 1.0 / (1.0 + drift_var * merged)
        info_now = merged * shrink
        return (info_now, (shrink, info_now))

    zero_info = jnp.zeros(drift_var.shape, dtype=jnp.float32)
    last_info, (shrinks, infos) = lax.scan(
        backward_step, zero_info, obs_precision[1:], reverse=True
    )
    shrinks = jnp.concatenate([shrinks, jnp.ones_like(zero_info)[None]], axis=0)
    infos = jnp.concatenate([infos, zero_info[None]], axis=0)
    return (gains, filt_vars, shrinks, infos)


def e_step(looked, word_counts, topic_prior):
    counts_float = word_counts.astype(jnp.float32)
    doc_topics = topic_prior + jnp.sum(counts_float, axis=-1, keepdims=True) / K
    scores = looked.astype(jnp.float32)
    for sweep in range(EITERS):
        logits = lax.digamma(doc_topics)[..., None, :] + scores
        peak = lax.optimization_barrier(jnp.max(logits, axis=-1, keepdims=True))
        raised = jnp.exp(logits - peak)
        total = jnp.sum(raised, axis=-1)
        if sweep < EITERS - 1:
            share = counts_float / total
            doc_topics = topic_prior + jnp.sum(share[..., None] * raised, axis=-2)
        else:
            resp = raised / total[..., None]
            doc_topics = topic_prior + jnp.sum(counts_float[..., None] * resp, axis=-2)
    weighted = to_bf16(counts_float[..., None] * resp)
    return (doc_topics, weighted)


def to_bf16(value):
    return lax.reduce_precision(value, exponent_bits=8, mantissa_bits=7).astype(jnp.bfloat16)


def shift_axis(value, axis, s):
    count = lax.axis_size(axis)
    return lax.ppermute(value, axis, [(i, (i + s) % count) for i in range(count)])


def shift_doc(value, s):
    return shift_axis(value, "doc", s)


def kalman_kernel(gain_ref, pull_ref, start_ref, after_ref, pseudo_ref, out_ref, last_ref):
    years = pseudo_ref.shape[0]
    mean = start_ref[...]
    for t in range(years):
        gain_now = gain_ref[pl.ds(t, 1), :]
        mean = (1.0 - gain_now) * mean + gain_now * pseudo_ref[t]
        out_ref[t] = mean
    last_ref[...] = mean
    mean = after_ref[...]
    for t in reversed(range(years)):
        pull_now = pull_ref[pl.ds(t, 1), :]
        mean = pull_now * mean + (1.0 - pull_now) * out_ref[t]
        out_ref[t] = mean


def kalman(gains, pulls, start, after, by_year):
    years, rows, topics = by_year.shape
    block = rows
    whole = pl.BlockSpec((years, topics), lambda i: (0, 0))
    edge = pl.BlockSpec((block, topics), lambda i: (i, 0))
    stack = pl.BlockSpec((years, block, topics), lambda i: (0, i, 0))
    return pl.pallas_call(
        kalman_kernel,
        grid=(rows // block,),
        in_specs=[whole, whole, edge, edge, stack],
        out_specs=(stack, edge),
        out_shape=(
            jax.ShapeDtypeStruct(by_year.shape, jnp.float32),
            jax.ShapeDtypeStruct(start.shape, jnp.float32),
        ),
    )(gains, pulls, start, after, by_year)


def first_pass_kernel(gain_ref, pull_ref, pseudo_ref, sent_ref, last_ref, filt_ref):
    years = pseudo_ref.shape[0]
    group = lax.axis_index("tg")
    base = group * years
    mean = jnp.zeros(pseudo_ref.shape[1:], jnp.float32)
    for t in range(years):
        gain_now = gain_ref[pl.ds(base + t, 1), :]
        mean = (1.0 - gain_now) * mean + gain_now * pseudo_ref[t]
        filt_ref[t] = mean
    last = mean
    mean = jnp.zeros(pseudo_ref.shape[1:], jnp.float32)
    for t in reversed(range(years)):
        pull_now = pull_ref[pl.ds(base + t, 1), :]
        mean = pull_now * mean + (1.0 - pull_now) * filt_ref[t]
    weight = jnp.where(group == 0, 1.0, 0.0)
    sent_ref[...] = weight * last + (1.0 - weight) * mean
    last_ref[...] = last


def second_pass_kernel(gain_ref, pull_ref, other_ref, last_ref, pseudo_ref, out_ref):
    years = pseudo_ref.shape[0]
    group = lax.axis_index("tg")
    base = group * years
    weight = jnp.where(group == 0, 1.0, 0.0)
    carry = jnp.ones((1, gain_ref.shape[1]), jnp.float32)
    responses = []
    for t in range(years):
        carry = (1.0 - gain_ref[pl.ds(years + t, 1), :]) * carry
        responses.append(carry)
    reach = jnp.zeros_like(carry)
    for t in reversed(range(years)):
        pull_now = pull_ref[pl.ds(years + t, 1), :]
        reach = pull_now * reach + (1.0 - pull_now) * responses[t]
    other = other_ref[...]
    mean = (1.0 - weight) * other
    for t in range(years):
        gain_now = gain_ref[pl.ds(base + t, 1), :]
        mean = (1.0 - gain_now) * mean + gain_now * pseudo_ref[t]
        out_ref[t] = mean
    mean = weight * (other + reach * last_ref[...])
    for t in reversed(range(years)):
        pull_now = pull_ref[pl.ds(base + t, 1), :]
        mean = pull_now * mean + (1.0 - pull_now) * out_ref[t]
        out_ref[t] = mean


def two_group_kalman(gains, pulls, by_year):
    years, rows, topics = by_year.shape
    edge = jax.ShapeDtypeStruct((rows, topics), jnp.float32)
    sent, last = pl.pallas_call(
        first_pass_kernel,
        out_shape=(edge, edge),
        scratch_shapes=[pltpu.VMEM(by_year.shape, jnp.float32)],
    )(gains, pulls, by_year)
    other = shift_axis(sent, "tg", 1)
    return pl.pallas_call(
        second_pass_kernel, out_shape=jax.ShapeDtypeStruct(by_year.shape, jnp.float32)
    )(gains, pulls, other, last, by_year)


def group_maps(gains, pulls, groups):
    gains_g = gains.reshape(groups, -1, gains.shape[-1])
    pulls_g = pulls.reshape(groups, -1, pulls.shape[-1])
    span = gains_g.shape[1]
    carry = jnp.ones_like(gains_g[:, 0])
    responses = []
    for i in range(span):
        carry = (1.0 - gains_g[:, i]) * carry
        responses.append(carry)
    from_start = jnp.zeros_like(carry)
    from_after = jnp.ones_like(carry)
    for i in reversed(range(span)):
        from_start = pulls_g[:, i] * from_start + (1.0 - pulls_g[:, i]) * responses[i]
        from_after = pulls_g[:, i] * from_after
    return carry, from_start, from_after


def body(beta, word_ids, word_counts, block_slot, topic_prior, drift_var, obs_precision):
    local_beta = beta[0]
    own_words = local_beta.shape[0]
    topics = local_beta.shape[1]
    doc_devices = lax.axis_size("doc")
    doc_place = lax.axis_index("doc")
    local_peak = jnp.max(local_beta, axis=0)
    local_total = jnp.sum(jnp.exp(local_beta - local_peak), axis=0)

    slot_ids = word_ids[0]
    local_docs = slot_ids.shape[0]
    slot_width = slot_ids.shape[1]

    per_docs = local_docs * slot_width
    message = jnp.concatenate([
        slot_ids.reshape(-1).astype(jnp.float32),
        word_counts[0].reshape(-1).astype(jnp.float32),
        local_peak,
        local_total,
    ])
    seen = jnp.stack([message] + [shift_doc(message, s) for s in range(1, doc_devices)])
    ints_seen = [
        seen[:, :2 * per_docs].astype(jnp.int32).reshape(doc_devices, 2, local_docs, slot_width)[i]
        for i in range(doc_devices)
    ]
    stats_seen = seen[:, 2 * per_docs:].reshape(doc_devices, 2, topics)
    all_ids = jnp.concatenate([part[0] for part in ints_seen], axis=0)
    block_match = (all_ids // BLOCK)[..., None] == lax.iota(jnp.int32, block_slot.shape[0])
    all_columns = (
        jnp.sum(jnp.where(block_match, block_slot, 0), axis=-1) * BLOCK + all_ids % BLOCK
    )
    all_counts = jnp.concatenate([part[1] for part in ints_seen], axis=0)
    peaks = stats_seen[:, 0]
    totals = stats_seen[:, 1]
    peak_value = jnp.max(peaks, axis=0)
    total_value = jnp.sum(totals * jnp.exp(peaks - peak_value), axis=0)
    normalizer = peak_value + jnp.log(total_value)

    flat_columns = all_columns.reshape(-1)
    local_columns = flat_columns - doc_place * own_words
    row_words = lax.iota(jnp.int32, own_words)
    marks = (row_words[:, None] == local_columns[None, :]).astype(jnp.bfloat16)
    table = to_bf16(local_beta - normalizer)
    partial = (
        lax.dot_general(marks, table, (((0,), (0,)), ((), ())), preferred_element_type=jnp.float32)
        .astype(jnp.bfloat16)
        .reshape(doc_devices, local_docs * slot_width, topics)
    )
    looked = partial
    for s in range(1, doc_devices):
        looked = looked + jnp.roll(shift_doc(partial, s), s, axis=0)
    looked = looked.reshape(local_docs * doc_devices, slot_width, topics)

    doc_topics_all, weighted = e_step(looked, all_counts, topic_prior)
    doc_topics = doc_topics_all[:local_docs]

    flat_weighted = weighted.reshape(-1, topics)
    counts = jnp.dot(marks, flat_weighted, preferred_element_type=jnp.float32)
    pseudo = local_beta + jnp.log1p(counts)

    gains, filt_vars, shrinks, infos = variance_tables(obs_precision, drift_var)
    years_total = obs_precision.shape[0]
    pulls = filt_vars / (filt_vars + drift_var)
    pulls = pulls.at[-1].set(0.0)

    span = lax.axis_size("tl")
    chunk = own_words // span
    by_dest = pseudo.reshape(span, chunk, topics)
    parts = PARTS if chunk % (8 * PARTS) == 0 else 1
    rows = chunk // parts
    done = [
        smooth_part(by_dest[:, i * rows:(i + 1) * rows], gains, pulls) for i in range(parts)
    ]
    back = jnp.concatenate(done, axis=1)
    return (back.reshape(own_words, topics)[None], doc_topics[None])


def smooth_part(by_dest, gains, pulls):
    groups = lax.axis_size("tg")
    span, rows, topics = by_dest.shape
    group = lax.axis_index("tg")
    by_year = lax.all_to_all(by_dest, "tl", split_axis=0, concat_axis=0, tiled=True)
    gains_here = lax.dynamic_slice_in_dim(gains, group * span, span, 0)
    pulls_here = lax.dynamic_slice_in_dim(pulls, group * span, span, 0)
    zero_mean = jnp.zeros((rows, topics), jnp.float32)
    if groups == 1:
        smoothed, _ = kalman(gains_here, pulls_here, zero_mean, zero_mean, by_year)
    elif groups == 2:
        smoothed = two_group_kalman(gains, pulls, by_year)
    else:
        local_smoothed, local_last = kalman(gains_here, pulls_here, zero_mean, zero_mean, by_year)
        summary = jnp.stack([local_last, local_smoothed[0]])
        if groups == 2:
            sent = jnp.where(group == 0, local_last, local_smoothed[0])
            other = shift_axis(sent, "tg", 1)
            ordered = jnp.where(
                group == 0, jnp.stack([summary, jnp.stack([other, other])]),
                jnp.stack([jnp.stack([other, other]), summary]),
            )
        else:
            seen = [summary] + [shift_axis(summary, "tg", s) for s in range(1, groups)]
            ordered = jnp.stack(seen)[(group - jnp.arange(groups)) % groups]
        carry, from_start, from_after = group_maps(gains, pulls, groups)
        entering = [zero_mean]
        for g in range(groups - 1):
            entering.append(ordered[g, 0] + carry[g] * entering[g])
        leaving = [zero_mean] * groups
        for g in reversed(range(1, groups)):
            leaving[g - 1] = (
                ordered[g, 1] + from_start[g] * entering[g] + from_after[g] * leaving[g]
            )
        start = jnp.stack(entering)[group]
        after = jnp.stack(leaving)[group]
        smoothed, _ = kalman(gains_here, pulls_here, start, after, by_year)
    return lax.all_to_all(smoothed, "tl", split_axis=0, concat_axis=0, tiled=True)


def solution(mesh):
    years = mesh.shape["tm"]
    span = 8 if years % 8 == 0 else years
    devices = mesh.devices.reshape(years // span, span, mesh.shape["doc"])
    grouped = jax.sharding.Mesh(devices, ("tg", "tl", "doc"))
    split = P(("tg", "tl"), "doc", None)
    in_specs = (split, split, split, P(), P(), P(), P())
    out_specs = (split, split)
    return jax.shard_map(body, mesh=grouped, in_specs=in_specs, out_specs=out_specs, check_vma=False)
```

```python
import jax
import jax.numpy as jnp
from jax import lax
from jax.experimental import pallas as pl
from jax.experimental.pallas import tpu as pltpu
from jax.sharding import PartitionSpec as P

K = 128
BLOCK = 128
EITERS = 4
PARTS = 1


init_variance = 4.0


def variance_tables(obs_precision, drift_var):

    def forward_step(prior_var, precision):
        denominator = 1.0 + prior_var * precision
        gain_now = prior_var * precision / denominator
        filt_var = prior_var / denominator
        return (filt_var + drift_var, (gain_now, filt_var))

    start_var = jnp.full(drift_var.shape, init_variance, dtype=jnp.float32)
    last_var, (gains, filt_vars) = lax.scan(forward_step, start_var, obs_precision, unroll=True)

    def backward_step(info_next, precision):
        merged = info_next + precision
        shrink = 1.0 / (1.0 + drift_var * merged)
        info_now = merged * shrink
        return (info_now, (shrink, info_now))

    zero_info = jnp.zeros(drift_var.shape, dtype=jnp.float32)
    last_info, (shrinks, infos) = lax.scan(
        backward_step, zero_info, obs_precision[1:], reverse=True
    )
    shrinks = jnp.concatenate([shrinks, jnp.ones_like(zero_info)[None]], axis=0)
    infos = jnp.concatenate([infos, zero_info[None]], axis=0)
    return (gains, filt_vars, shrinks, infos)


def e_step(looked, word_counts, topic_prior):
    counts_float = word_counts.astype(jnp.float32)
    doc_topics = topic_prior + jnp.sum(counts_float, axis=-1, keepdims=True) / K
    scores = looked.astype(jnp.float32)
    for sweep in range(EITERS):
        logits = lax.digamma(doc_topics)[..., None, :] + scores
        peak = lax.optimization_barrier(jnp.max(logits, axis=-1, keepdims=True))
        raised = jnp.exp(logits - peak)
        total = jnp.sum(raised, axis=-1)
        if sweep < EITERS - 1:
            share = counts_float / total
            doc_topics = topic_prior + jnp.sum(share[..., None] * raised, axis=-2)
        else:
            resp = raised / total[..., None]
            doc_topics = topic_prior + jnp.sum(counts_float[..., None] * resp, axis=-2)
    weighted = to_bf16(counts_float[..., None] * resp)
    return (doc_topics, weighted)


def to_bf16(value):
    return lax.reduce_precision(value, exponent_bits=8, mantissa_bits=7).astype(jnp.bfloat16)


def shift_axis(value, axis, s):
    count = lax.axis_size(axis)
    return lax.ppermute(value, axis, [(i, (i + s) % count) for i in range(count)])


def shift_doc(value, s):
    return shift_axis(value, "doc", s)


def kalman_kernel(gain_ref, pull_ref, start_ref, after_ref, pseudo_ref, out_ref, last_ref):
    years = pseudo_ref.shape[0]
    mean = start_ref[...]
    for t in range(years):
        gain_now = gain_ref[pl.ds(t, 1), :]
        mean = (1.0 - gain_now) * mean + gain_now * pseudo_ref[t]
        out_ref[t] = mean
    last_ref[...] = mean
    mean = after_ref[...]
    for t in reversed(range(years)):
        pull_now = pull_ref[pl.ds(t, 1), :]
        mean = pull_now * mean + (1.0 - pull_now) * out_ref[t]
        out_ref[t] = mean


def kalman(gains, pulls, start, after, by_year):
    years, rows, topics = by_year.shape
    block = rows
    whole = pl.BlockSpec((years, topics), lambda i: (0, 0))
    edge = pl.BlockSpec((block, topics), lambda i: (i, 0))
    stack = pl.BlockSpec((years, block, topics), lambda i: (0, i, 0))
    return pl.pallas_call(
        kalman_kernel,
        grid=(rows // block,),
        in_specs=[whole, whole, edge, edge, stack],
        out_specs=(stack, edge),
        out_shape=(
            jax.ShapeDtypeStruct(by_year.shape, jnp.float32),
            jax.ShapeDtypeStruct(start.shape, jnp.float32),
        ),
    )(gains, pulls, start, after, by_year)


def first_pass_kernel(gain_ref, pull_ref, pseudo_ref, sent_ref, last_ref, filt_ref):
    years = pseudo_ref.shape[0]
    group = lax.axis_index("tg")
    base = group * years
    mean = jnp.zeros(pseudo_ref.shape[1:], jnp.float32)
    for t in range(years):
        gain_now = gain_ref[pl.ds(base + t, 1), :]
        mean = (1.0 - gain_now) * mean + gain_now * pseudo_ref[t]
        filt_ref[t] = mean
    last = mean
    mean = jnp.zeros(pseudo_ref.shape[1:], jnp.float32)
    for t in reversed(range(years)):
        pull_now = pull_ref[pl.ds(base + t, 1), :]
        mean = pull_now * mean + (1.0 - pull_now) * filt_ref[t]
    weight = jnp.where(group == 0, 1.0, 0.0)
    sent_ref[...] = weight * last + (1.0 - weight) * mean
    last_ref[...] = last


def second_pass_kernel(gain_ref, pull_ref, other_ref, last_ref, pseudo_ref, out_ref):
    years = pseudo_ref.shape[0]
    group = lax.axis_index("tg")
    base = group * years
    weight = jnp.where(group == 0, 1.0, 0.0)
    carry = jnp.ones((1, gain_ref.shape[1]), jnp.float32)
    responses = []
    for t in range(years):
        carry = (1.0 - gain_ref[pl.ds(years + t, 1), :]) * carry
        responses.append(carry)
    reach = jnp.zeros_like(carry)
    for t in reversed(range(years)):
        pull_now = pull_ref[pl.ds(years + t, 1), :]
        reach = pull_now * reach + (1.0 - pull_now) * responses[t]
    other = other_ref[...]
    mean = (1.0 - weight) * other
    for t in range(years):
        gain_now = gain_ref[pl.ds(base + t, 1), :]
        mean = (1.0 - gain_now) * mean + gain_now * pseudo_ref[t]
        out_ref[t] = mean
    mean = weight * (other + reach * last_ref[...])
    for t in reversed(range(years)):
        pull_now = pull_ref[pl.ds(base + t, 1), :]
        mean = pull_now * mean + (1.0 - pull_now) * out_ref[t]
        out_ref[t] = mean


def two_group_kalman(gains, pulls, by_year):
    years, rows, topics = by_year.shape
    edge = jax.ShapeDtypeStruct((rows, topics), jnp.float32)
    group = lax.axis_index("tg")
    gains_here = lax.dynamic_slice_in_dim(gains, group * years, years, 0)
    pulls_here = lax.dynamic_slice_in_dim(pulls, group * years, years, 0)
    mean = jnp.zeros((rows, topics), jnp.float32)
    filtered = []
    for t in range(years):
        mean = (1.0 - gains_here[t]) * mean + gains_here[t] * by_year[t]
        filtered.append(mean)
    last = mean
    mean = jnp.zeros((rows, topics), jnp.float32)
    for t in reversed(range(years)):
        mean = pulls_here[t] * mean + (1.0 - pulls_here[t]) * filtered[t]
    sent = jnp.where(group == 0, last, mean)
    other = shift_axis(sent, "tg", 1)
    return pl.pallas_call(
        second_pass_kernel, out_shape=jax.ShapeDtypeStruct(by_year.shape, jnp.float32)
    )(gains, pulls, other, last, by_year)


def group_maps(gains, pulls, groups):
    gains_g = gains.reshape(groups, -1, gains.shape[-1])
    pulls_g = pulls.reshape(groups, -1, pulls.shape[-1])
    span = gains_g.shape[1]
    carry = jnp.ones_like(gains_g[:, 0])
    responses = []
    for i in range(span):
        carry = (1.0 - gains_g[:, i]) * carry
        responses.append(carry)
    from_start = jnp.zeros_like(carry)
    from_after = jnp.ones_like(carry)
    for i in reversed(range(span)):
        from_start = pulls_g[:, i] * from_start + (1.0 - pulls_g[:, i]) * responses[i]
        from_after = pulls_g[:, i] * from_after
    return carry, from_start, from_after


def body(beta, word_ids, word_counts, block_slot, topic_prior, drift_var, obs_precision):
    local_beta = beta[0]
    own_words = local_beta.shape[0]
    topics = local_beta.shape[1]
    doc_devices = lax.axis_size("doc")
    doc_place = lax.axis_index("doc")
    local_peak = jnp.max(local_beta, axis=0)
    local_total = jnp.sum(jnp.exp(local_beta - local_peak), axis=0)

    slot_ids = word_ids[0]
    local_docs = slot_ids.shape[0]
    slot_width = slot_ids.shape[1]

    per_docs = local_docs * slot_width
    message = jnp.concatenate([
        slot_ids.reshape(-1).astype(jnp.float32),
        word_counts[0].reshape(-1).astype(jnp.float32),
        local_peak,
        local_total,
    ])
    seen = jnp.stack([message] + [shift_doc(message, s) for s in range(1, doc_devices)])
    ints_seen = [
        seen[:, :2 * per_docs].astype(jnp.int32).reshape(doc_devices, 2, local_docs, slot_width)[i]
        for i in range(doc_devices)
    ]
    stats_seen = seen[:, 2 * per_docs:].reshape(doc_devices, 2, topics)
    all_ids = jnp.concatenate([part[0] for part in ints_seen], axis=0)
    block_match = (all_ids // BLOCK)[..., None] == lax.iota(jnp.int32, block_slot.shape[0])
    all_columns = (
        jnp.sum(jnp.where(block_match, block_slot, 0), axis=-1) * BLOCK + all_ids % BLOCK
    )
    all_counts = jnp.concatenate([part[1] for part in ints_seen], axis=0)
    peaks = stats_seen[:, 0]
    totals = stats_seen[:, 1]
    peak_value = jnp.max(peaks, axis=0)
    total_value = jnp.sum(totals * jnp.exp(peaks - peak_value), axis=0)
    normalizer = peak_value + jnp.log(total_value)

    flat_columns = all_columns.reshape(-1)
    local_columns = flat_columns - doc_place * own_words
    row_words = lax.iota(jnp.int32, own_words)
    marks = (row_words[:, None] == local_columns[None, :]).astype(jnp.bfloat16)
    table = to_bf16(local_beta - normalizer)
    partial = (
        lax.dot_general(marks, table, (((0,), (0,)), ((), ())), preferred_element_type=jnp.float32)
        .astype(jnp.bfloat16)
        .reshape(doc_devices, local_docs * slot_width, topics)
    )
    looked = partial
    for s in range(1, doc_devices):
        looked = looked + jnp.roll(shift_doc(partial, s), s, axis=0)
    looked = looked.reshape(local_docs * doc_devices, slot_width, topics)

    doc_topics_all, weighted = e_step(looked, all_counts, topic_prior)
    doc_topics = doc_topics_all[:local_docs]

    flat_weighted = weighted.reshape(-1, topics)
    counts = jnp.dot(marks, flat_weighted, preferred_element_type=jnp.float32)
    pseudo = local_beta + jnp.log1p(counts)

    gains, filt_vars, shrinks, infos = variance_tables(obs_precision, drift_var)
    years_total = obs_precision.shape[0]
    pulls = filt_vars / (filt_vars + drift_var)
    pulls = pulls.at[-1].set(0.0)

    span = lax.axis_size("tl")
    chunk = own_words // span
    by_dest = pseudo.reshape(span, chunk, topics)
    parts = PARTS if chunk % (8 * PARTS) == 0 else 1
    rows = chunk // parts
    done = [
        smooth_part(by_dest[:, i * rows:(i + 1) * rows], gains, pulls) for i in range(parts)
    ]
    back = jnp.concatenate(done, axis=1)
    return (back.reshape(own_words, topics)[None], doc_topics[None])


def smooth_part(by_dest, gains, pulls):
    groups = lax.axis_size("tg")
    span, rows, topics = by_dest.shape
    group = lax.axis_index("tg")
    by_year = lax.all_to_all(by_dest, "tl", split_axis=0, concat_axis=0, tiled=True)
    gains_here = lax.dynamic_slice_in_dim(gains, group * span, span, 0)
    pulls_here = lax.dynamic_slice_in_dim(pulls, group * span, span, 0)
    zero_mean = jnp.zeros((rows, topics), jnp.float32)
    if groups == 1:
        smoothed, _ = kalman(gains_here, pulls_here, zero_mean, zero_mean, by_year)
    elif groups == 2:
        smoothed = two_group_kalman(gains, pulls, by_year)
    else:
        local_smoothed, local_last = kalman(gains_here, pulls_here, zero_mean, zero_mean, by_year)
        summary = jnp.stack([local_last, local_smoothed[0]])
        if groups == 2:
            sent = jnp.where(group == 0, local_last, local_smoothed[0])
            other = shift_axis(sent, "tg", 1)
            ordered = jnp.where(
                group == 0, jnp.stack([summary, jnp.stack([other, other])]),
                jnp.stack([jnp.stack([other, other]), summary]),
            )
        else:
            seen = [summary] + [shift_axis(summary, "tg", s) for s in range(1, groups)]
            ordered = jnp.stack(seen)[(group - jnp.arange(groups)) % groups]
        carry, from_start, from_after = group_maps(gains, pulls, groups)
        entering = [zero_mean]
        for g in range(groups - 1):
            entering.append(ordered[g, 0] + carry[g] * entering[g])
        leaving = [zero_mean] * groups
        for g in reversed(range(1, groups)):
            leaving[g - 1] = (
                ordered[g, 1] + from_start[g] * entering[g] + from_after[g] * leaving[g]
            )
        start = jnp.stack(entering)[group]
        after = jnp.stack(leaving)[group]
        smoothed, _ = kalman(gains_here, pulls_here, start, after, by_year)
    return lax.all_to_all(smoothed, "tl", split_axis=0, concat_axis=0, tiled=True)


def solution(mesh):
    years = mesh.shape["tm"]
    span = 8 if years % 8 == 0 else years
    devices = mesh.devices.reshape(years // span, span, mesh.shape["doc"])
    grouped = jax.sharding.Mesh(devices, ("tg", "tl", "doc"))
    split = P(("tg", "tl"), "doc", None)
    in_specs = (split, split, split, P(), P(), P(), P())
    out_specs = (split, split)
    return jax.shard_map(body, mesh=grouped, in_specs=in_specs, out_specs=out_specs, check_vma=False)
```

```python
import jax
import jax.numpy as jnp
from jax import lax
from jax.experimental import pallas as pl
from jax.experimental.pallas import tpu as pltpu
from jax.sharding import PartitionSpec as P

K = 128
BLOCK = 128
EITERS = 4
PARTS = 1


init_variance = 4.0


def variance_tables(obs_precision, drift_var):

    def forward_step(prior_var, precision):
        denominator = 1.0 + prior_var * precision
        gain_now = prior_var * precision / denominator
        filt_var = prior_var / denominator
        return (filt_var + drift_var, (gain_now, filt_var))

    start_var = jnp.full(drift_var.shape, init_variance, dtype=jnp.float32)
    last_var, (gains, filt_vars) = lax.scan(forward_step, start_var, obs_precision, unroll=True)

    def backward_step(info_next, precision):
        merged = info_next + precision
        shrink = 1.0 / (1.0 + drift_var * merged)
        info_now = merged * shrink
        return (info_now, (shrink, info_now))

    zero_info = jnp.zeros(drift_var.shape, dtype=jnp.float32)
    last_info, (shrinks, infos) = lax.scan(
        backward_step, zero_info, obs_precision[1:], reverse=True
    )
    shrinks = jnp.concatenate([shrinks, jnp.ones_like(zero_info)[None]], axis=0)
    infos = jnp.concatenate([infos, zero_info[None]], axis=0)
    return (gains, filt_vars, shrinks, infos)


def e_step(looked, word_counts, topic_prior):
    counts_float = word_counts.astype(jnp.float32)
    doc_topics = topic_prior + jnp.sum(counts_float, axis=-1, keepdims=True) / K
    scores = looked.astype(jnp.float32)
    for sweep in range(EITERS):
        logits = lax.digamma(doc_topics)[..., None, :] + scores
        peak = lax.optimization_barrier(jnp.max(logits, axis=-1, keepdims=True))
        raised = jnp.exp(logits - peak)
        total = jnp.sum(raised, axis=-1)
        if sweep < EITERS - 1:
            share = counts_float / total
            doc_topics = topic_prior + jnp.sum(share[..., None] * raised, axis=-2)
        else:
            resp = raised / total[..., None]
            doc_topics = topic_prior + jnp.sum(counts_float[..., None] * resp, axis=-2)
    weighted = to_bf16(counts_float[..., None] * resp)
    return (doc_topics, weighted)


def to_bf16(value):
    return lax.reduce_precision(value, exponent_bits=8, mantissa_bits=7).astype(jnp.bfloat16)


def shift_axis(value, axis, s):
    count = lax.axis_size(axis)
    return lax.ppermute(value, axis, [(i, (i + s) % count) for i in range(count)])


def shift_doc(value, s):
    return shift_axis(value, "doc", s)


def kalman_kernel(gain_ref, pull_ref, start_ref, after_ref, pseudo_ref, out_ref, last_ref):
    years = pseudo_ref.shape[0]
    mean = start_ref[...]
    for t in range(years):
        gain_now = gain_ref[pl.ds(t, 1), :]
        mean = (1.0 - gain_now) * mean + gain_now * pseudo_ref[t]
        out_ref[t] = mean
    last_ref[...] = mean
    mean = after_ref[...]
    for t in reversed(range(years)):
        pull_now = pull_ref[pl.ds(t, 1), :]
        mean = pull_now * mean + (1.0 - pull_now) * out_ref[t]
        out_ref[t] = mean


def kalman(gains, pulls, start, after, by_year):
    years, rows, topics = by_year.shape
    block = rows
    whole = pl.BlockSpec((years, topics), lambda i: (0, 0))
    edge = pl.BlockSpec((block, topics), lambda i: (i, 0))
    stack = pl.BlockSpec((years, block, topics), lambda i: (0, i, 0))
    return pl.pallas_call(
        kalman_kernel,
        grid=(rows // block,),
        in_specs=[whole, whole, edge, edge, stack],
        out_specs=(stack, edge),
        out_shape=(
            jax.ShapeDtypeStruct(by_year.shape, jnp.float32),
            jax.ShapeDtypeStruct(start.shape, jnp.float32),
        ),
    )(gains, pulls, start, after, by_year)


def first_pass_kernel(gain_ref, pull_ref, pseudo_ref, sent_ref, last_ref, filt_ref):
    years = pseudo_ref.shape[0]
    group = lax.axis_index("tg")
    base = group * years
    mean = jnp.zeros(pseudo_ref.shape[1:], jnp.float32)
    for t in range(years):
        gain_now = gain_ref[pl.ds(base + t, 1), :]
        mean = (1.0 - gain_now) * mean + gain_now * pseudo_ref[t]
        filt_ref[t] = mean
    last = mean
    mean = jnp.zeros(pseudo_ref.shape[1:], jnp.float32)
    for t in reversed(range(years)):
        pull_now = pull_ref[pl.ds(base + t, 1), :]
        mean = pull_now * mean + (1.0 - pull_now) * filt_ref[t]
    weight = jnp.where(group == 0, 1.0, 0.0)
    sent_ref[...] = weight * last + (1.0 - weight) * mean
    last_ref[...] = last


def second_pass_kernel(gain_ref, pull_ref, other_ref, last_ref, pseudo_ref, out_ref):
    years = pseudo_ref.shape[0]
    group = lax.axis_index("tg")
    base = group * years
    weight = jnp.where(group == 0, 1.0, 0.0)
    carry = jnp.ones((1, gain_ref.shape[1]), jnp.float32)
    responses = []
    for t in range(years):
        carry = (1.0 - gain_ref[pl.ds(years + t, 1), :]) * carry
        responses.append(carry)
    reach = jnp.zeros_like(carry)
    for t in reversed(range(years)):
        pull_now = pull_ref[pl.ds(years + t, 1), :]
        reach = pull_now * reach + (1.0 - pull_now) * responses[t]
    other = other_ref[...]
    mean = (1.0 - weight) * other
    for t in range(years):
        gain_now = gain_ref[pl.ds(base + t, 1), :]
        mean = (1.0 - gain_now) * mean + gain_now * pseudo_ref[t]
        out_ref[t] = mean
    mean = weight * (other + reach * last_ref[...])
    for t in reversed(range(years)):
        pull_now = pull_ref[pl.ds(base + t, 1), :]
        mean = pull_now * mean + (1.0 - pull_now) * out_ref[t]
        out_ref[t] = mean


def two_group_kalman(gains, pulls, by_year):
    years, rows, topics = by_year.shape
    edge = jax.ShapeDtypeStruct((rows, topics), jnp.float32)
    group = lax.axis_index("tg")
    gains_here = lax.dynamic_slice_in_dim(gains, group * years, years, 0)
    pulls_here = lax.dynamic_slice_in_dim(pulls, group * years, years, 0)
    mean = jnp.zeros((rows, topics), jnp.float32)
    filtered = []
    for t in range(years):
        mean = (1.0 - gains_here[t]) * mean + gains_here[t] * by_year[t]
        filtered.append(mean)
    last = mean
    mean = jnp.zeros((rows, topics), jnp.float32)
    for t in reversed(range(years)):
        mean = pulls_here[t] * mean + (1.0 - pulls_here[t]) * filtered[t]
    sent = jnp.where(group == 0, last, mean)
    other = shift_axis(sent, "tg", 1)
    carry = jnp.ones((topics,), jnp.float32)
    responses = []
    for t in range(years):
        carry = (1.0 - gains[years + t]) * carry
        responses.append(carry)
    reach = jnp.zeros_like(carry)
    for t in reversed(range(years)):
        reach = pulls[years + t] * reach + (1.0 - pulls[years + t]) * responses[t]
    weight = jnp.where(group == 0, 1.0, 0.0)
    start = (1.0 - weight) * other
    after = weight * (other + reach * last)
    unit = jnp.eye(years + 2, dtype=jnp.float32)[:, :, None]
    state = unit[years]
    filtered = []
    for t in range(years):
        state = (1.0 - gains_here[t]) * state + gains_here[t] * unit[t]
        filtered.append(state)
    state = unit[years + 1]
    maps = [None] * years
    for t in reversed(range(years)):
        state = pulls_here[t] * state + (1.0 - pulls_here[t]) * filtered[t]
        maps[t] = state
    maps = jnp.stack(maps)
    smoothed = maps[:, years, None, :] * start + maps[:, years + 1, None, :] * after
    for s in range(years):
        smoothed = smoothed + maps[:, s, None, :] * by_year[s]
    return smoothed


def group_maps(gains, pulls, groups):
    gains_g = gains.reshape(groups, -1, gains.shape[-1])
    pulls_g = pulls.reshape(groups, -1, pulls.shape[-1])
    span = gains_g.shape[1]
    carry = jnp.ones_like(gains_g[:, 0])
    responses = []
    for i in range(span):
        carry = (1.0 - gains_g[:, i]) * carry
        responses.append(carry)
    from_start = jnp.zeros_like(carry)
    from_after = jnp.ones_like(carry)
    for i in reversed(range(span)):
        from_start = pulls_g[:, i] * from_start + (1.0 - pulls_g[:, i]) * responses[i]
        from_after = pulls_g[:, i] * from_after
    return carry, from_start, from_after


def body(beta, word_ids, word_counts, block_slot, topic_prior, drift_var, obs_precision):
    local_beta = beta[0]
    own_words = local_beta.shape[0]
    topics = local_beta.shape[1]
    doc_devices = lax.axis_size("doc")
    doc_place = lax.axis_index("doc")
    local_peak = jnp.max(local_beta, axis=0)
    local_total = jnp.sum(jnp.exp(local_beta - local_peak), axis=0)

    slot_ids = word_ids[0]
    local_docs = slot_ids.shape[0]
    slot_width = slot_ids.shape[1]

    per_docs = local_docs * slot_width
    message = jnp.concatenate([
        slot_ids.reshape(-1).astype(jnp.float32),
        word_counts[0].reshape(-1).astype(jnp.float32),
        local_peak,
        local_total,
    ])
    seen = jnp.stack([message] + [shift_doc(message, s) for s in range(1, doc_devices)])
    ints_seen = [
        seen[:, :2 * per_docs].astype(jnp.int32).reshape(doc_devices, 2, local_docs, slot_width)[i]
        for i in range(doc_devices)
    ]
    stats_seen = seen[:, 2 * per_docs:].reshape(doc_devices, 2, topics)
    all_ids = jnp.concatenate([part[0] for part in ints_seen], axis=0)
    block_match = (all_ids // BLOCK)[..., None] == lax.iota(jnp.int32, block_slot.shape[0])
    all_columns = (
        jnp.sum(jnp.where(block_match, block_slot, 0), axis=-1) * BLOCK + all_ids % BLOCK
    )
    all_counts = jnp.concatenate([part[1] for part in ints_seen], axis=0)
    peaks = stats_seen[:, 0]
    totals = stats_seen[:, 1]
    peak_value = jnp.max(peaks, axis=0)
    total_value = jnp.sum(totals * jnp.exp(peaks - peak_value), axis=0)
    normalizer = peak_value + jnp.log(total_value)

    flat_columns = all_columns.reshape(-1)
    local_columns = flat_columns - doc_place * own_words
    row_words = lax.iota(jnp.int32, own_words)
    marks = (row_words[:, None] == local_columns[None, :]).astype(jnp.bfloat16)
    table = to_bf16(local_beta - normalizer)
    partial = (
        lax.dot_general(marks, table, (((0,), (0,)), ((), ())), preferred_element_type=jnp.float32)
        .astype(jnp.bfloat16)
        .reshape(doc_devices, local_docs * slot_width, topics)
    )
    looked = partial
    for s in range(1, doc_devices):
        looked = looked + jnp.roll(shift_doc(partial, s), s, axis=0)
    looked = looked.reshape(local_docs * doc_devices, slot_width, topics)

    doc_topics_all, weighted = e_step(looked, all_counts, topic_prior)
    doc_topics = doc_topics_all[:local_docs]

    flat_weighted = weighted.reshape(-1, topics)
    counts = jnp.dot(marks, flat_weighted, preferred_element_type=jnp.float32)
    pseudo = local_beta + jnp.log1p(counts)

    gains, filt_vars, shrinks, infos = variance_tables(obs_precision, drift_var)
    years_total = obs_precision.shape[0]
    pulls = filt_vars / (filt_vars + drift_var)
    pulls = pulls.at[-1].set(0.0)

    span = lax.axis_size("tl")
    chunk = own_words // span
    by_dest = pseudo.reshape(span, chunk, topics)
    parts = PARTS if chunk % (8 * PARTS) == 0 else 1
    rows = chunk // parts
    done = [
        smooth_part(by_dest[:, i * rows:(i + 1) * rows], gains, pulls) for i in range(parts)
    ]
    back = jnp.concatenate(done, axis=1)
    return (back.reshape(own_words, topics)[None], doc_topics[None])


def smooth_part(by_dest, gains, pulls):
    groups = lax.axis_size("tg")
    span, rows, topics = by_dest.shape
    group = lax.axis_index("tg")
    by_year = lax.all_to_all(by_dest, "tl", split_axis=0, concat_axis=0, tiled=True)
    gains_here = lax.dynamic_slice_in_dim(gains, group * span, span, 0)
    pulls_here = lax.dynamic_slice_in_dim(pulls, group * span, span, 0)
    zero_mean = jnp.zeros((rows, topics), jnp.float32)
    if groups == 1:
        smoothed, _ = kalman(gains_here, pulls_here, zero_mean, zero_mean, by_year)
    elif groups == 2:
        smoothed = two_group_kalman(gains, pulls, by_year)
    else:
        local_smoothed, local_last = kalman(gains_here, pulls_here, zero_mean, zero_mean, by_year)
        summary = jnp.stack([local_last, local_smoothed[0]])
        if groups == 2:
            sent = jnp.where(group == 0, local_last, local_smoothed[0])
            other = shift_axis(sent, "tg", 1)
            ordered = jnp.where(
                group == 0, jnp.stack([summary, jnp.stack([other, other])]),
                jnp.stack([jnp.stack([other, other]), summary]),
            )
        else:
            seen = [summary] + [shift_axis(summary, "tg", s) for s in range(1, groups)]
            ordered = jnp.stack(seen)[(group - jnp.arange(groups)) % groups]
        carry, from_start, from_after = group_maps(gains, pulls, groups)
        entering = [zero_mean]
        for g in range(groups - 1):
            entering.append(ordered[g, 0] + carry[g] * entering[g])
        leaving = [zero_mean] * groups
        for g in reversed(range(1, groups)):
            leaving[g - 1] = (
                ordered[g, 1] + from_start[g] * entering[g] + from_after[g] * leaving[g]
            )
        start = jnp.stack(entering)[group]
        after = jnp.stack(leaving)[group]
        smoothed, _ = kalman(gains_here, pulls_here, start, after, by_year)
    return lax.all_to_all(smoothed, "tl", split_axis=0, concat_axis=0, tiled=True)


def solution(mesh):
    years = mesh.shape["tm"]
    span = 8 if years % 8 == 0 else years
    devices = mesh.devices.reshape(years // span, span, mesh.shape["doc"])
    grouped = jax.sharding.Mesh(devices, ("tg", "tl", "doc"))
    split = P(("tg", "tl"), "doc", None)
    in_specs = (split, split, split, P(), P(), P(), P())
    out_specs = (split, split)
    return jax.shard_map(body, mesh=grouped, in_specs=in_specs, out_specs=out_specs, check_vma=False)
```

```python
import jax
import jax.numpy as jnp
from jax import lax
from jax.experimental import pallas as pl
from jax.experimental.pallas import tpu as pltpu
from jax.sharding import PartitionSpec as P

K = 128
BLOCK = 128
EITERS = 4
PARTS = 1


init_variance = 4.0


def variance_tables(obs_precision, drift_var):

    def forward_step(prior_var, precision):
        denominator = 1.0 + prior_var * precision
        gain_now = prior_var * precision / denominator
        filt_var = prior_var / denominator
        return (filt_var + drift_var, (gain_now, filt_var))

    start_var = jnp.full(drift_var.shape, init_variance, dtype=jnp.float32)
    last_var, (gains, filt_vars) = lax.scan(forward_step, start_var, obs_precision, unroll=True)

    def backward_step(info_next, precision):
        merged = info_next + precision
        shrink = 1.0 / (1.0 + drift_var * merged)
        info_now = merged * shrink
        return (info_now, (shrink, info_now))

    zero_info = jnp.zeros(drift_var.shape, dtype=jnp.float32)
    last_info, (shrinks, infos) = lax.scan(
        backward_step, zero_info, obs_precision[1:], reverse=True
    )
    shrinks = jnp.concatenate([shrinks, jnp.ones_like(zero_info)[None]], axis=0)
    infos = jnp.concatenate([infos, zero_info[None]], axis=0)
    return (gains, filt_vars, shrinks, infos)


def e_step(looked, word_counts, topic_prior):
    counts_float = word_counts.astype(jnp.float32)
    doc_topics = topic_prior + jnp.sum(counts_float, axis=-1, keepdims=True) / K
    scores = looked.astype(jnp.float32)
    for sweep in range(EITERS):
        logits = lax.digamma(doc_topics)[..., None, :] + scores
        peak = lax.optimization_barrier(jnp.max(logits, axis=-1, keepdims=True))
        raised = jnp.exp(logits - peak)
        total = jnp.sum(raised, axis=-1)
        if sweep < EITERS - 1:
            share = counts_float / total
            doc_topics = topic_prior + jnp.sum(share[..., None] * raised, axis=-2)
        else:
            resp = raised / total[..., None]
            doc_topics = topic_prior + jnp.sum(counts_float[..., None] * resp, axis=-2)
    weighted = to_bf16(counts_float[..., None] * resp)
    return (doc_topics, weighted)


def to_bf16(value):
    return lax.reduce_precision(value, exponent_bits=8, mantissa_bits=7).astype(jnp.bfloat16)


def shift_axis(value, axis, s):
    count = lax.axis_size(axis)
    return lax.ppermute(value, axis, [(i, (i + s) % count) for i in range(count)])


def shift_doc(value, s):
    return shift_axis(value, "doc", s)


def kalman_kernel(gain_ref, pull_ref, start_ref, after_ref, pseudo_ref, out_ref, last_ref):
    years = pseudo_ref.shape[0]
    mean = start_ref[...]
    for t in range(years):
        gain_now = gain_ref[pl.ds(t, 1), :]
        mean = (1.0 - gain_now) * mean + gain_now * pseudo_ref[t]
        out_ref[t] = mean
    last_ref[...] = mean
    mean = after_ref[...]
    for t in reversed(range(years)):
        pull_now = pull_ref[pl.ds(t, 1), :]
        mean = pull_now * mean + (1.0 - pull_now) * out_ref[t]
        out_ref[t] = mean


def kalman(gains, pulls, start, after, by_year):
    years, rows, topics = by_year.shape
    block = rows
    whole = pl.BlockSpec((years, topics), lambda i: (0, 0))
    edge = pl.BlockSpec((block, topics), lambda i: (i, 0))
    stack = pl.BlockSpec((years, block, topics), lambda i: (0, i, 0))
    return pl.pallas_call(
        kalman_kernel,
        grid=(rows // block,),
        in_specs=[whole, whole, edge, edge, stack],
        out_specs=(stack, edge),
        out_shape=(
            jax.ShapeDtypeStruct(by_year.shape, jnp.float32),
            jax.ShapeDtypeStruct(start.shape, jnp.float32),
        ),
    )(gains, pulls, start, after, by_year)


def first_pass_kernel(gain_ref, pull_ref, pseudo_ref, sent_ref, last_ref, filt_ref):
    years = pseudo_ref.shape[0]
    group = lax.axis_index("tg")
    base = group * years
    mean = jnp.zeros(pseudo_ref.shape[1:], jnp.float32)
    for t in range(years):
        gain_now = gain_ref[pl.ds(base + t, 1), :]
        mean = (1.0 - gain_now) * mean + gain_now * pseudo_ref[t]
        filt_ref[t] = mean
    last = mean
    mean = jnp.zeros(pseudo_ref.shape[1:], jnp.float32)
    for t in reversed(range(years)):
        pull_now = pull_ref[pl.ds(base + t, 1), :]
        mean = pull_now * mean + (1.0 - pull_now) * filt_ref[t]
    weight = jnp.where(group == 0, 1.0, 0.0)
    sent_ref[...] = weight * last + (1.0 - weight) * mean
    last_ref[...] = last


def second_pass_kernel(gain_ref, pull_ref, other_ref, last_ref, pseudo_ref, out_ref):
    years = pseudo_ref.shape[0]
    group = lax.axis_index("tg")
    base = group * years
    weight = jnp.where(group == 0, 1.0, 0.0)
    carry = jnp.ones((1, gain_ref.shape[1]), jnp.float32)
    responses = []
    for t in range(years):
        carry = (1.0 - gain_ref[pl.ds(years + t, 1), :]) * carry
        responses.append(carry)
    reach = jnp.zeros_like(carry)
    for t in reversed(range(years)):
        pull_now = pull_ref[pl.ds(years + t, 1), :]
        reach = pull_now * reach + (1.0 - pull_now) * responses[t]
    other = other_ref[...]
    mean = (1.0 - weight) * other
    for t in range(years):
        gain_now = gain_ref[pl.ds(base + t, 1), :]
        mean = (1.0 - gain_now) * mean + gain_now * pseudo_ref[t]
        out_ref[t] = mean
    mean = weight * (other + reach * last_ref[...])
    for t in reversed(range(years)):
        pull_now = pull_ref[pl.ds(base + t, 1), :]
        mean = pull_now * mean + (1.0 - pull_now) * out_ref[t]
        out_ref[t] = mean


def two_group_kalman(gains, pulls, by_year):
    years, rows, topics = by_year.shape
    edge = jax.ShapeDtypeStruct((rows, topics), jnp.float32)
    group = lax.axis_index("tg")
    gains_here = lax.dynamic_slice_in_dim(gains, group * years, years, 0)
    pulls_here = lax.dynamic_slice_in_dim(pulls, group * years, years, 0)
    mean = jnp.zeros((rows, topics), jnp.float32)
    filtered = []
    for t in range(years):
        mean = (1.0 - gains_here[t]) * mean + gains_here[t] * by_year[t]
        filtered.append(mean)
    last = mean
    mean = jnp.zeros((rows, topics), jnp.float32)
    for t in reversed(range(years)):
        mean = pulls_here[t] * mean + (1.0 - pulls_here[t]) * filtered[t]
    sent = jnp.where(group == 0, last, mean)
    other = shift_axis(sent, "tg", 1)
    carry = jnp.ones((topics,), jnp.float32)
    responses = []
    for t in range(years):
        carry = (1.0 - gains[years + t]) * carry
        responses.append(carry)
    reach = jnp.zeros_like(carry)
    for t in reversed(range(years)):
        reach = pulls[years + t] * reach + (1.0 - pulls[years + t]) * responses[t]
    weight = jnp.where(group == 0, 1.0, 0.0)
    unit = jnp.eye(years + 2, dtype=jnp.float32)[:, :, None]
    state = unit[years]
    filtered = []
    for t in range(years):
        state = (1.0 - gains_here[t]) * state + gains_here[t] * unit[t]
        filtered.append(state)
    state = unit[years + 1]
    maps = [None] * years
    for t in reversed(range(years)):
        state = pulls_here[t] * state + (1.0 - pulls_here[t]) * filtered[t]
        maps[t] = state
    maps = jnp.stack(maps)
    smoothed = maps[:, years + 1, None, :] * (weight * reach * last)
    for s in range(years):
        smoothed = smoothed + maps[:, s, None, :] * by_year[s]
    via_other = (1.0 - weight) * maps[:, years] + weight * maps[:, years + 1]
    return smoothed + via_other[:, None, :] * other


def group_maps(gains, pulls, groups):
    gains_g = gains.reshape(groups, -1, gains.shape[-1])
    pulls_g = pulls.reshape(groups, -1, pulls.shape[-1])
    span = gains_g.shape[1]
    carry = jnp.ones_like(gains_g[:, 0])
    responses = []
    for i in range(span):
        carry = (1.0 - gains_g[:, i]) * carry
        responses.append(carry)
    from_start = jnp.zeros_like(carry)
    from_after = jnp.ones_like(carry)
    for i in reversed(range(span)):
        from_start = pulls_g[:, i] * from_start + (1.0 - pulls_g[:, i]) * responses[i]
        from_after = pulls_g[:, i] * from_after
    return carry, from_start, from_after


def body(beta, word_ids, word_counts, block_slot, topic_prior, drift_var, obs_precision):
    local_beta = beta[0]
    own_words = local_beta.shape[0]
    topics = local_beta.shape[1]
    doc_devices = lax.axis_size("doc")
    doc_place = lax.axis_index("doc")
    local_peak = jnp.max(local_beta, axis=0)
    local_total = jnp.sum(jnp.exp(local_beta - local_peak), axis=0)

    slot_ids = word_ids[0]
    local_docs = slot_ids.shape[0]
    slot_width = slot_ids.shape[1]

    per_docs = local_docs * slot_width
    message = jnp.concatenate([
        slot_ids.reshape(-1).astype(jnp.float32),
        word_counts[0].reshape(-1).astype(jnp.float32),
        local_peak,
        local_total,
    ])
    seen = jnp.stack([message] + [shift_doc(message, s) for s in range(1, doc_devices)])
    ints_seen = [
        seen[:, :2 * per_docs].astype(jnp.int32).reshape(doc_devices, 2, local_docs, slot_width)[i]
        for i in range(doc_devices)
    ]
    stats_seen = seen[:, 2 * per_docs:].reshape(doc_devices, 2, topics)
    all_ids = jnp.concatenate([part[0] for part in ints_seen], axis=0)
    block_match = (all_ids // BLOCK)[..., None] == lax.iota(jnp.int32, block_slot.shape[0])
    all_columns = (
        jnp.sum(jnp.where(block_match, block_slot, 0), axis=-1) * BLOCK + all_ids % BLOCK
    )
    all_counts = jnp.concatenate([part[1] for part in ints_seen], axis=0)
    peaks = stats_seen[:, 0]
    totals = stats_seen[:, 1]
    peak_value = jnp.max(peaks, axis=0)
    total_value = jnp.sum(totals * jnp.exp(peaks - peak_value), axis=0)
    normalizer = peak_value + jnp.log(total_value)

    flat_columns = all_columns.reshape(-1)
    local_columns = flat_columns - doc_place * own_words
    row_words = lax.iota(jnp.int32, own_words)
    marks = (row_words[:, None] == local_columns[None, :]).astype(jnp.bfloat16)
    table = to_bf16(local_beta - normalizer)
    partial = (
        lax.dot_general(marks, table, (((0,), (0,)), ((), ())), preferred_element_type=jnp.float32)
        .astype(jnp.bfloat16)
        .reshape(doc_devices, local_docs * slot_width, topics)
    )
    looked = partial
    for s in range(1, doc_devices):
        looked = looked + jnp.roll(shift_doc(partial, s), s, axis=0)
    looked = looked.reshape(local_docs * doc_devices, slot_width, topics)

    doc_topics_all, weighted = e_step(looked, all_counts, topic_prior)
    doc_topics = doc_topics_all[:local_docs]

    flat_weighted = weighted.reshape(-1, topics)
    counts = jnp.dot(marks, flat_weighted, preferred_element_type=jnp.float32)
    pseudo = local_beta + jnp.log1p(counts)

    gains, filt_vars, shrinks, infos = variance_tables(obs_precision, drift_var)
    years_total = obs_precision.shape[0]
    pulls = filt_vars / (filt_vars + drift_var)
    pulls = pulls.at[-1].set(0.0)

    span = lax.axis_size("tl")
    chunk = own_words // span
    by_dest = pseudo.reshape(span, chunk, topics)
    parts = PARTS if chunk % (8 * PARTS) == 0 else 1
    rows = chunk // parts
    done = [
        smooth_part(by_dest[:, i * rows:(i + 1) * rows], gains, pulls) for i in range(parts)
    ]
    back = jnp.concatenate(done, axis=1)
    return (back.reshape(own_words, topics)[None], doc_topics[None])


def smooth_part(by_dest, gains, pulls):
    groups = lax.axis_size("tg")
    span, rows, topics = by_dest.shape
    group = lax.axis_index("tg")
    by_year = lax.all_to_all(by_dest, "tl", split_axis=0, concat_axis=0, tiled=True)
    gains_here = lax.dynamic_slice_in_dim(gains, group * span, span, 0)
    pulls_here = lax.dynamic_slice_in_dim(pulls, group * span, span, 0)
    zero_mean = jnp.zeros((rows, topics), jnp.float32)
    if groups == 1:
        smoothed, _ = kalman(gains_here, pulls_here, zero_mean, zero_mean, by_year)
    elif groups == 2:
        smoothed = two_group_kalman(gains, pulls, by_year)
    else:
        local_smoothed, local_last = kalman(gains_here, pulls_here, zero_mean, zero_mean, by_year)
        summary = jnp.stack([local_last, local_smoothed[0]])
        if groups == 2:
            sent = jnp.where(group == 0, local_last, local_smoothed[0])
            other = shift_axis(sent, "tg", 1)
            ordered = jnp.where(
                group == 0, jnp.stack([summary, jnp.stack([other, other])]),
                jnp.stack([jnp.stack([other, other]), summary]),
            )
        else:
            seen = [summary] + [shift_axis(summary, "tg", s) for s in range(1, groups)]
            ordered = jnp.stack(seen)[(group - jnp.arange(groups)) % groups]
        carry, from_start, from_after = group_maps(gains, pulls, groups)
        entering = [zero_mean]
        for g in range(groups - 1):
            entering.append(ordered[g, 0] + carry[g] * entering[g])
        leaving = [zero_mean] * groups
        for g in reversed(range(1, groups)):
            leaving[g - 1] = (
                ordered[g, 1] + from_start[g] * entering[g] + from_after[g] * leaving[g]
            )
        start = jnp.stack(entering)[group]
        after = jnp.stack(leaving)[group]
        smoothed, _ = kalman(gains_here, pulls_here, start, after, by_year)
    return lax.all_to_all(smoothed, "tl", split_axis=0, concat_axis=0, tiled=True)


def solution(mesh):
    years = mesh.shape["tm"]
    span = 8 if years % 8 == 0 else years
    devices = mesh.devices.reshape(years // span, span, mesh.shape["doc"])
    grouped = jax.sharding.Mesh(devices, ("tg", "tl", "doc"))
    split = P(("tg", "tl"), "doc", None)
    in_specs = (split, split, split, P(), P(), P(), P())
    out_specs = (split, split)
    return jax.shard_map(body, mesh=grouped, in_specs=in_specs, out_specs=out_specs, check_vma=False)
```

```python
import jax
import jax.numpy as jnp
from jax import lax
from jax.experimental import pallas as pl
from jax.experimental.pallas import tpu as pltpu
from jax.sharding import PartitionSpec as P

K = 128
BLOCK = 128
EITERS = 4
PARTS = 1


init_variance = 4.0


def variance_tables(obs_precision, drift_var):

    def forward_step(prior_var, precision):
        denominator = 1.0 + prior_var * precision
        gain_now = prior_var * precision / denominator
        filt_var = prior_var / denominator
        return (filt_var + drift_var, (gain_now, filt_var))

    start_var = jnp.full(drift_var.shape, init_variance, dtype=jnp.float32)
    last_var, (gains, filt_vars) = lax.scan(forward_step, start_var, obs_precision, unroll=True)

    def backward_step(info_next, precision):
        merged = info_next + precision
        shrink = 1.0 / (1.0 + drift_var * merged)
        info_now = merged * shrink
        return (info_now, (shrink, info_now))

    zero_info = jnp.zeros(drift_var.shape, dtype=jnp.float32)
    last_info, (shrinks, infos) = lax.scan(
        backward_step, zero_info, obs_precision[1:], reverse=True
    )
    shrinks = jnp.concatenate([shrinks, jnp.ones_like(zero_info)[None]], axis=0)
    infos = jnp.concatenate([infos, zero_info[None]], axis=0)
    return (gains, filt_vars, shrinks, infos)


def e_step(looked, word_counts, topic_prior):
    counts_float = word_counts.astype(jnp.float32)
    doc_topics = topic_prior + jnp.sum(counts_float, axis=-1, keepdims=True) / K
    scores = looked.astype(jnp.float32)
    for sweep in range(EITERS):
        logits = lax.digamma(doc_topics)[..., None, :] + scores
        peak = lax.optimization_barrier(jnp.max(logits, axis=-1, keepdims=True))
        raised = jnp.exp(logits - peak)
        total = jnp.sum(raised, axis=-1)
        if sweep < EITERS - 1:
            share = counts_float / total
            doc_topics = topic_prior + jnp.sum(share[..., None] * raised, axis=-2)
        else:
            resp = raised / total[..., None]
            doc_topics = topic_prior + jnp.sum(counts_float[..., None] * resp, axis=-2)
    weighted = to_bf16(counts_float[..., None] * resp)
    return (doc_topics, weighted)


def to_bf16(value):
    return lax.reduce_precision(value, exponent_bits=8, mantissa_bits=7).astype(jnp.bfloat16)


def shift_axis(value, axis, s):
    count = lax.axis_size(axis)
    return lax.ppermute(value, axis, [(i, (i + s) % count) for i in range(count)])


def shift_doc(value, s):
    return shift_axis(value, "doc", s)


def kalman_kernel(gain_ref, pull_ref, start_ref, after_ref, pseudo_ref, out_ref, last_ref):
    years = pseudo_ref.shape[0]
    mean = start_ref[...]
    for t in range(years):
        gain_now = gain_ref[pl.ds(t, 1), :]
        mean = (1.0 - gain_now) * mean + gain_now * pseudo_ref[t]
        out_ref[t] = mean
    last_ref[...] = mean
    mean = after_ref[...]
    for t in reversed(range(years)):
        pull_now = pull_ref[pl.ds(t, 1), :]
        mean = pull_now * mean + (1.0 - pull_now) * out_ref[t]
        out_ref[t] = mean


def kalman(gains, pulls, start, after, by_year):
    years, rows, topics = by_year.shape
    block = rows
    whole = pl.BlockSpec((years, topics), lambda i: (0, 0))
    edge = pl.BlockSpec((block, topics), lambda i: (i, 0))
    stack = pl.BlockSpec((years, block, topics), lambda i: (0, i, 0))
    return pl.pallas_call(
        kalman_kernel,
        grid=(rows // block,),
        in_specs=[whole, whole, edge, edge, stack],
        out_specs=(stack, edge),
        out_shape=(
            jax.ShapeDtypeStruct(by_year.shape, jnp.float32),
            jax.ShapeDtypeStruct(start.shape, jnp.float32),
        ),
    )(gains, pulls, start, after, by_year)


def first_pass_kernel(gain_ref, pull_ref, pseudo_ref, sent_ref, last_ref, filt_ref):
    years = pseudo_ref.shape[0]
    group = lax.axis_index("tg")
    base = group * years
    mean = jnp.zeros(pseudo_ref.shape[1:], jnp.float32)
    for t in range(years):
        gain_now = gain_ref[pl.ds(base + t, 1), :]
        mean = (1.0 - gain_now) * mean + gain_now * pseudo_ref[t]
        filt_ref[t] = mean
    last = mean
    mean = jnp.zeros(pseudo_ref.shape[1:], jnp.float32)
    for t in reversed(range(years)):
        pull_now = pull_ref[pl.ds(base + t, 1), :]
        mean = pull_now * mean + (1.0 - pull_now) * filt_ref[t]
    weight = jnp.where(group == 0, 1.0, 0.0)
    sent_ref[...] = weight * last + (1.0 - weight) * mean
    last_ref[...] = last


def second_pass_kernel(gain_ref, pull_ref, other_ref, last_ref, pseudo_ref, out_ref):
    years = pseudo_ref.shape[0]
    group = lax.axis_index("tg")
    base = group * years
    weight = jnp.where(group == 0, 1.0, 0.0)
    carry = jnp.ones((1, gain_ref.shape[1]), jnp.float32)
    responses = []
    for t in range(years):
        carry = (1.0 - gain_ref[pl.ds(years + t, 1), :]) * carry
        responses.append(carry)
    reach = jnp.zeros_like(carry)
    for t in reversed(range(years)):
        pull_now = pull_ref[pl.ds(years + t, 1), :]
        reach = pull_now * reach + (1.0 - pull_now) * responses[t]
    other = other_ref[...]
    mean = (1.0 - weight) * other
    for t in range(years):
        gain_now = gain_ref[pl.ds(base + t, 1), :]
        mean = (1.0 - gain_now) * mean + gain_now * pseudo_ref[t]
        out_ref[t] = mean
    mean = weight * (other + reach * last_ref[...])
    for t in reversed(range(years)):
        pull_now = pull_ref[pl.ds(base + t, 1), :]
        mean = pull_now * mean + (1.0 - pull_now) * out_ref[t]
        out_ref[t] = mean


def two_group_kalman(gains, pulls, by_year):
    years, rows, topics = by_year.shape
    edge = jax.ShapeDtypeStruct((rows, topics), jnp.float32)
    group = lax.axis_index("tg")
    gains_here = lax.dynamic_slice_in_dim(gains, group * years, years, 0)
    pulls_here = lax.dynamic_slice_in_dim(pulls, group * years, years, 0)
    mean = jnp.zeros((rows, topics), jnp.float32)
    filtered = []
    for t in range(years):
        mean = (1.0 - gains_here[t]) * mean + gains_here[t] * by_year[t]
        filtered.append(mean)
    last = mean
    mean = jnp.zeros((rows, topics), jnp.float32)
    for t in reversed(range(years)):
        mean = pulls_here[t] * mean + (1.0 - pulls_here[t]) * filtered[t]
    sent = jnp.where(group == 0, last, mean)
    other = shift_axis(sent, "tg", 1)
    carry = jnp.ones((topics,), jnp.float32)
    responses = []
    for t in range(years):
        carry = (1.0 - gains[years + t]) * carry
        responses.append(carry)
    reach = jnp.zeros_like(carry)
    for t in reversed(range(years)):
        reach = pulls[years + t] * reach + (1.0 - pulls[years + t]) * responses[t]
    weight = jnp.where(group == 0, 1.0, 0.0)
    unit = jnp.eye(years + 2, dtype=jnp.float32)[:, :, None]
    state = unit[years]
    filtered = []
    for t in range(years):
        state = (1.0 - gains_here[t]) * state + gains_here[t] * unit[t]
        filtered.append(state)
    state = unit[years + 1]
    maps = [None] * years
    for t in reversed(range(years)):
        state = pulls_here[t] * state + (1.0 - pulls_here[t]) * filtered[t]
        maps[t] = state
    maps = jnp.stack(maps)
    smoothed = maps[:, years + 1, None, :] * (weight * reach * last)
    for s in range(years):
        smoothed = smoothed + maps[:, s, None, :] * by_year[s]
    smoothed = lax.optimization_barrier(smoothed)
    via_other = (1.0 - weight) * maps[:, years] + weight * maps[:, years + 1]
    return smoothed + via_other[:, None, :] * other


def group_maps(gains, pulls, groups):
    gains_g = gains.reshape(groups, -1, gains.shape[-1])
    pulls_g = pulls.reshape(groups, -1, pulls.shape[-1])
    span = gains_g.shape[1]
    carry = jnp.ones_like(gains_g[:, 0])
    responses = []
    for i in range(span):
        carry = (1.0 - gains_g[:, i]) * carry
        responses.append(carry)
    from_start = jnp.zeros_like(carry)
    from_after = jnp.ones_like(carry)
    for i in reversed(range(span)):
        from_start = pulls_g[:, i] * from_start + (1.0 - pulls_g[:, i]) * responses[i]
        from_after = pulls_g[:, i] * from_after
    return carry, from_start, from_after


def body(beta, word_ids, word_counts, block_slot, topic_prior, drift_var, obs_precision):
    local_beta = beta[0]
    own_words = local_beta.shape[0]
    topics = local_beta.shape[1]
    doc_devices = lax.axis_size("doc")
    doc_place = lax.axis_index("doc")
    local_peak = jnp.max(local_beta, axis=0)
    local_total = jnp.sum(jnp.exp(local_beta - local_peak), axis=0)

    slot_ids = word_ids[0]
    local_docs = slot_ids.shape[0]
    slot_width = slot_ids.shape[1]

    per_docs = local_docs * slot_width
    message = jnp.concatenate([
        slot_ids.reshape(-1).astype(jnp.float32),
        word_counts[0].reshape(-1).astype(jnp.float32),
        local_peak,
        local_total,
    ])
    seen = jnp.stack([message] + [shift_doc(message, s) for s in range(1, doc_devices)])
    ints_seen = [
        seen[:, :2 * per_docs].astype(jnp.int32).reshape(doc_devices, 2, local_docs, slot_width)[i]
        for i in range(doc_devices)
    ]
    stats_seen = seen[:, 2 * per_docs:].reshape(doc_devices, 2, topics)
    all_ids = jnp.concatenate([part[0] for part in ints_seen], axis=0)
    block_match = (all_ids // BLOCK)[..., None] == lax.iota(jnp.int32, block_slot.shape[0])
    all_columns = (
        jnp.sum(jnp.where(block_match, block_slot, 0), axis=-1) * BLOCK + all_ids % BLOCK
    )
    all_counts = jnp.concatenate([part[1] for part in ints_seen], axis=0)
    peaks = stats_seen[:, 0]
    totals = stats_seen[:, 1]
    peak_value = jnp.max(peaks, axis=0)
    total_value = jnp.sum(totals * jnp.exp(peaks - peak_value), axis=0)
    normalizer = peak_value + jnp.log(total_value)

    flat_columns = all_columns.reshape(-1)
    local_columns = flat_columns - doc_place * own_words
    row_words = lax.iota(jnp.int32, own_words)
    marks = (row_words[:, None] == local_columns[None, :]).astype(jnp.bfloat16)
    table = to_bf16(local_beta - normalizer)
    partial = (
        lax.dot_general(marks, table, (((0,), (0,)), ((), ())), preferred_element_type=jnp.float32)
        .astype(jnp.bfloat16)
        .reshape(doc_devices, local_docs * slot_width, topics)
    )
    looked = partial
    for s in range(1, doc_devices):
        looked = looked + jnp.roll(shift_doc(partial, s), s, axis=0)
    looked = looked.reshape(local_docs * doc_devices, slot_width, topics)

    doc_topics_all, weighted = e_step(looked, all_counts, topic_prior)
    doc_topics = doc_topics_all[:local_docs]

    flat_weighted = weighted.reshape(-1, topics)
    counts = jnp.dot(marks, flat_weighted, preferred_element_type=jnp.float32)
    pseudo = local_beta + jnp.log1p(counts)

    gains, filt_vars, shrinks, infos = variance_tables(obs_precision, drift_var)
    years_total = obs_precision.shape[0]
    pulls = filt_vars / (filt_vars + drift_var)
    pulls = pulls.at[-1].set(0.0)

    span = lax.axis_size("tl")
    chunk = own_words // span
    by_dest = pseudo.reshape(span, chunk, topics)
    parts = PARTS if chunk % (8 * PARTS) == 0 else 1
    rows = chunk // parts
    done = [
        smooth_part(by_dest[:, i * rows:(i + 1) * rows], gains, pulls) for i in range(parts)
    ]
    back = jnp.concatenate(done, axis=1)
    return (back.reshape(own_words, topics)[None], doc_topics[None])


def smooth_part(by_dest, gains, pulls):
    groups = lax.axis_size("tg")
    span, rows, topics = by_dest.shape
    group = lax.axis_index("tg")
    by_year = lax.all_to_all(by_dest, "tl", split_axis=0, concat_axis=0, tiled=True)
    gains_here = lax.dynamic_slice_in_dim(gains, group * span, span, 0)
    pulls_here = lax.dynamic_slice_in_dim(pulls, group * span, span, 0)
    zero_mean = jnp.zeros((rows, topics), jnp.float32)
    if groups == 1:
        smoothed, _ = kalman(gains_here, pulls_here, zero_mean, zero_mean, by_year)
    elif groups == 2:
        smoothed = two_group_kalman(gains, pulls, by_year)
    else:
        local_smoothed, local_last = kalman(gains_here, pulls_here, zero_mean, zero_mean, by_year)
        summary = jnp.stack([local_last, local_smoothed[0]])
        if groups == 2:
            sent = jnp.where(group == 0, local_last, local_smoothed[0])
            other = shift_axis(sent, "tg", 1)
            ordered = jnp.where(
                group == 0, jnp.stack([summary, jnp.stack([other, other])]),
                jnp.stack([jnp.stack([other, other]), summary]),
            )
        else:
            seen = [summary] + [shift_axis(summary, "tg", s) for s in range(1, groups)]
            ordered = jnp.stack(seen)[(group - jnp.arange(groups)) % groups]
        carry, from_start, from_after = group_maps(gains, pulls, groups)
        entering = [zero_mean]
        for g in range(groups - 1):
            entering.append(ordered[g, 0] + carry[g] * entering[g])
        leaving = [zero_mean] * groups
        for g in reversed(range(1, groups)):
            leaving[g - 1] = (
                ordered[g, 1] + from_start[g] * entering[g] + from_after[g] * leaving[g]
            )
        start = jnp.stack(entering)[group]
        after = jnp.stack(leaving)[group]
        smoothed, _ = kalman(gains_here, pulls_here, start, after, by_year)
    return lax.all_to_all(smoothed, "tl", split_axis=0, concat_axis=0, tiled=True)


def solution(mesh):
    years = mesh.shape["tm"]
    span = 8 if years % 8 == 0 else years
    devices = mesh.devices.reshape(years // span, span, mesh.shape["doc"])
    grouped = jax.sharding.Mesh(devices, ("tg", "tl", "doc"))
    split = P(("tg", "tl"), "doc", None)
    in_specs = (split, split, split, P(), P(), P(), P())
    out_specs = (split, split)
    return jax.shard_map(body, mesh=grouped, in_specs=in_specs, out_specs=out_specs, check_vma=False)
```

```python
import jax
import jax.numpy as jnp
from jax import lax
from jax.experimental import pallas as pl
from jax.experimental.pallas import tpu as pltpu
from jax.sharding import PartitionSpec as P

K = 128
BLOCK = 128
EITERS = 4
PARTS = 1


init_variance = 4.0


def variance_tables(obs_precision, drift_var):

    def forward_step(prior_var, precision):
        denominator = 1.0 + prior_var * precision
        gain_now = prior_var * precision / denominator
        filt_var = prior_var / denominator
        return (filt_var + drift_var, (gain_now, filt_var))

    start_var = jnp.full(drift_var.shape, init_variance, dtype=jnp.float32)
    last_var, (gains, filt_vars) = lax.scan(forward_step, start_var, obs_precision, unroll=True)

    def backward_step(info_next, precision):
        merged = info_next + precision
        shrink = 1.0 / (1.0 + drift_var * merged)
        info_now = merged * shrink
        return (info_now, (shrink, info_now))

    zero_info = jnp.zeros(drift_var.shape, dtype=jnp.float32)
    last_info, (shrinks, infos) = lax.scan(
        backward_step, zero_info, obs_precision[1:], reverse=True
    )
    shrinks = jnp.concatenate([shrinks, jnp.ones_like(zero_info)[None]], axis=0)
    infos = jnp.concatenate([infos, zero_info[None]], axis=0)
    return (gains, filt_vars, shrinks, infos)


def e_step(looked, word_counts, topic_prior):
    counts_float = word_counts.astype(jnp.float32)
    doc_topics = topic_prior + jnp.sum(counts_float, axis=-1, keepdims=True) / K
    scores = looked.astype(jnp.float32)
    for sweep in range(EITERS):
        logits = lax.digamma(doc_topics)[..., None, :] + scores
        peak = lax.optimization_barrier(jnp.max(logits, axis=-1, keepdims=True))
        raised = jnp.exp(logits - peak)
        total = jnp.sum(raised, axis=-1)
        if sweep < EITERS - 1:
            share = counts_float / total
            doc_topics = topic_prior + jnp.sum(share[..., None] * raised, axis=-2)
        else:
            resp = raised / total[..., None]
            doc_topics = topic_prior + jnp.sum(counts_float[..., None] * resp, axis=-2)
    weighted = to_bf16(counts_float[..., None] * resp)
    return (doc_topics, weighted)


def to_bf16(value):
    return lax.reduce_precision(value, exponent_bits=8, mantissa_bits=7).astype(jnp.bfloat16)


def shift_axis(value, axis, s):
    count = lax.axis_size(axis)
    return lax.ppermute(value, axis, [(i, (i + s) % count) for i in range(count)])


def shift_doc(value, s):
    return shift_axis(value, "doc", s)


def kalman_kernel(gain_ref, pull_ref, start_ref, after_ref, pseudo_ref, out_ref, last_ref):
    years = pseudo_ref.shape[0]
    mean = start_ref[...]
    for t in range(years):
        gain_now = gain_ref[pl.ds(t, 1), :]
        mean = (1.0 - gain_now) * mean + gain_now * pseudo_ref[t]
        out_ref[t] = mean
    last_ref[...] = mean
    mean = after_ref[...]
    for t in reversed(range(years)):
        pull_now = pull_ref[pl.ds(t, 1), :]
        mean = pull_now * mean + (1.0 - pull_now) * out_ref[t]
        out_ref[t] = mean


def kalman(gains, pulls, start, after, by_year):
    years, rows, topics = by_year.shape
    block = rows
    whole = pl.BlockSpec((years, topics), lambda i: (0, 0))
    edge = pl.BlockSpec((block, topics), lambda i: (i, 0))
    stack = pl.BlockSpec((years, block, topics), lambda i: (0, i, 0))
    return pl.pallas_call(
        kalman_kernel,
        grid=(rows // block,),
        in_specs=[whole, whole, edge, edge, stack],
        out_specs=(stack, edge),
        out_shape=(
            jax.ShapeDtypeStruct(by_year.shape, jnp.float32),
            jax.ShapeDtypeStruct(start.shape, jnp.float32),
        ),
    )(gains, pulls, start, after, by_year)


def first_pass_kernel(gain_ref, pull_ref, pseudo_ref, sent_ref, last_ref, filt_ref):
    years = pseudo_ref.shape[0]
    group = lax.axis_index("tg")
    base = group * years
    mean = jnp.zeros(pseudo_ref.shape[1:], jnp.float32)
    for t in range(years):
        gain_now = gain_ref[pl.ds(base + t, 1), :]
        mean = (1.0 - gain_now) * mean + gain_now * pseudo_ref[t]
        filt_ref[t] = mean
    last = mean
    mean = jnp.zeros(pseudo_ref.shape[1:], jnp.float32)
    for t in reversed(range(years)):
        pull_now = pull_ref[pl.ds(base + t, 1), :]
        mean = pull_now * mean + (1.0 - pull_now) * filt_ref[t]
    weight = jnp.where(group == 0, 1.0, 0.0)
    sent_ref[...] = weight * last + (1.0 - weight) * mean
    last_ref[...] = last


def second_pass_kernel(gain_ref, pull_ref, other_ref, last_ref, pseudo_ref, out_ref):
    years = pseudo_ref.shape[0]
    group = lax.axis_index("tg")
    base = group * years
    weight = jnp.where(group == 0, 1.0, 0.0)
    carry = jnp.ones((1, gain_ref.shape[1]), jnp.float32)
    responses = []
    for t in range(years):
        carry = (1.0 - gain_ref[pl.ds(years + t, 1), :]) * carry
        responses.append(carry)
    reach = jnp.zeros_like(carry)
    for t in reversed(range(years)):
        pull_now = pull_ref[pl.ds(years + t, 1), :]
        reach = pull_now * reach + (1.0 - pull_now) * responses[t]
    other = other_ref[...]
    mean = (1.0 - weight) * other
    for t in range(years):
        gain_now = gain_ref[pl.ds(base + t, 1), :]
        mean = (1.0 - gain_now) * mean + gain_now * pseudo_ref[t]
        out_ref[t] = mean
    mean = weight * (other + reach * last_ref[...])
    for t in reversed(range(years)):
        pull_now = pull_ref[pl.ds(base + t, 1), :]
        mean = pull_now * mean + (1.0 - pull_now) * out_ref[t]
        out_ref[t] = mean


def two_group_kalman(gains, pulls, by_year):
    years, rows, topics = by_year.shape
    edge = jax.ShapeDtypeStruct((rows, topics), jnp.float32)
    group = lax.axis_index("tg")
    gains_here = lax.dynamic_slice_in_dim(gains, group * years, years, 0)
    pulls_here = lax.dynamic_slice_in_dim(pulls, group * years, years, 0)
    mean = jnp.zeros((rows, topics), jnp.float32)
    filtered = []
    for t in range(years):
        mean = (1.0 - gains_here[t]) * mean + gains_here[t] * by_year[t]
        filtered.append(mean)
    last = mean
    mean = jnp.zeros((rows, topics), jnp.float32)
    for t in reversed(range(years)):
        mean = pulls_here[t] * mean + (1.0 - pulls_here[t]) * filtered[t]
    sent = jnp.where(group == 0, last, mean)
    other = shift_axis(sent, "tg", 1)
    carry = jnp.ones((topics,), jnp.float32)
    responses = []
    for t in range(years):
        carry = (1.0 - gains[years + t]) * carry
        responses.append(carry)
    reach = jnp.zeros_like(carry)
    for t in reversed(range(years)):
        reach = pulls[years + t] * reach + (1.0 - pulls[years + t]) * responses[t]
    weight = jnp.where(group == 0, 1.0, 0.0)
    unit = jnp.eye(years + 2, dtype=jnp.float32)[:, :, None]
    state = unit[years]
    filtered = []
    for t in range(years):
        state = (1.0 - gains_here[t]) * state + gains_here[t] * unit[t]
        filtered.append(state)
    state = unit[years + 1]
    maps = [None] * years
    for t in reversed(range(years)):
        state = pulls_here[t] * state + (1.0 - pulls_here[t]) * filtered[t]
        maps[t] = state
    maps = jnp.stack(maps)
    smoothed = maps[:, years + 1, None, :] * (weight * reach * last)
    for s in range(years):
        smoothed = smoothed + maps[:, s, None, :] * by_year[s]
    smoothed = lax.optimization_barrier(smoothed)
    via_other = (1.0 - weight) * maps[:, years] + weight * maps[:, years + 1]
    return smoothed + via_other[:, None, :] * other


def group_maps(gains, pulls, groups):
    gains_g = gains.reshape(groups, -1, gains.shape[-1])
    pulls_g = pulls.reshape(groups, -1, pulls.shape[-1])
    span = gains_g.shape[1]
    carry = jnp.ones_like(gains_g[:, 0])
    responses = []
    for i in range(span):
        carry = (1.0 - gains_g[:, i]) * carry
        responses.append(carry)
    from_start = jnp.zeros_like(carry)
    from_after = jnp.ones_like(carry)
    for i in reversed(range(span)):
        from_start = pulls_g[:, i] * from_start + (1.0 - pulls_g[:, i]) * responses[i]
        from_after = pulls_g[:, i] * from_after
    return carry, from_start, from_after


def body(beta, word_ids, word_counts, block_slot, topic_prior, drift_var, obs_precision):
    local_beta = beta[0]
    own_words = local_beta.shape[0]
    topics = local_beta.shape[1]
    doc_devices = lax.axis_size("doc")
    doc_place = lax.axis_index("doc")
    local_peak = jnp.max(local_beta, axis=0)
    local_total = jnp.sum(jnp.exp(local_beta - local_peak), axis=0)

    slot_ids = word_ids[0]
    local_docs = slot_ids.shape[0]
    slot_width = slot_ids.shape[1]

    per_docs = local_docs * slot_width
    message = jnp.concatenate([
        slot_ids.reshape(-1).astype(jnp.float32),
        word_counts[0].reshape(-1).astype(jnp.float32),
        local_peak,
        local_total,
    ])
    seen = jnp.stack([message] + [shift_doc(message, s) for s in range(1, doc_devices)])
    ints_seen = [
        seen[:, :2 * per_docs].astype(jnp.int32).reshape(doc_devices, 2, local_docs, slot_width)[i]
        for i in range(doc_devices)
    ]
    stats_seen = seen[:, 2 * per_docs:].reshape(doc_devices, 2, topics)
    all_ids = jnp.concatenate([part[0] for part in ints_seen], axis=0)
    block_match = (all_ids // BLOCK)[..., None] == lax.iota(jnp.int32, block_slot.shape[0])
    all_columns = (
        jnp.sum(jnp.where(block_match, block_slot, 0), axis=-1) * BLOCK + all_ids % BLOCK
    )
    all_counts = jnp.concatenate([part[1] for part in ints_seen], axis=0)
    peaks = stats_seen[:, 0]
    totals = stats_seen[:, 1]
    peak_value = jnp.max(peaks, axis=0)
    total_value = jnp.sum(totals * jnp.exp(peaks - peak_value), axis=0)
    normalizer = peak_value + jnp.log(total_value)

    flat_columns = all_columns.reshape(-1)
    local_columns = flat_columns - doc_place * own_words
    row_words = lax.iota(jnp.int32, own_words)
    marks = (row_words[:, None] == local_columns[None, :]).astype(jnp.bfloat16)
    table = to_bf16(local_beta - normalizer)
    partial = (
        lax.dot_general(marks, table, (((0,), (0,)), ((), ())), preferred_element_type=jnp.float32)
        .astype(jnp.bfloat16)
        .reshape(doc_devices, local_docs * slot_width, topics)
    )
    looked = partial
    for s in range(1, doc_devices):
        looked = looked + jnp.roll(shift_doc(partial, s), s, axis=0)
    looked = looked.reshape(local_docs * doc_devices, slot_width, topics)

    doc_topics_all, weighted = e_step(looked, all_counts, topic_prior)
    doc_topics = doc_topics_all[:local_docs]

    flat_weighted = weighted.reshape(-1, topics)
    held_columns = lax.optimization_barrier(local_columns)
    held_marks = lax.optimization_barrier(
        (row_words[:, None] == held_columns[None, :]).astype(jnp.bfloat16)
    )
    counts = jnp.dot(held_marks, flat_weighted, preferred_element_type=jnp.float32)
    pseudo = local_beta + jnp.log1p(counts)

    gains, filt_vars, shrinks, infos = variance_tables(obs_precision, drift_var)
    years_total = obs_precision.shape[0]
    pulls = filt_vars / (filt_vars + drift_var)
    pulls = pulls.at[-1].set(0.0)

    span = lax.axis_size("tl")
    chunk = own_words // span
    by_dest = pseudo.reshape(span, chunk, topics)
    parts = PARTS if chunk % (8 * PARTS) == 0 else 1
    rows = chunk // parts
    done = [
        smooth_part(by_dest[:, i * rows:(i + 1) * rows], gains, pulls) for i in range(parts)
    ]
    back = jnp.concatenate(done, axis=1)
    return (back.reshape(own_words, topics)[None], doc_topics[None])


def smooth_part(by_dest, gains, pulls):
    groups = lax.axis_size("tg")
    span, rows, topics = by_dest.shape
    group = lax.axis_index("tg")
    by_year = lax.all_to_all(by_dest, "tl", split_axis=0, concat_axis=0, tiled=True)
    gains_here = lax.dynamic_slice_in_dim(gains, group * span, span, 0)
    pulls_here = lax.dynamic_slice_in_dim(pulls, group * span, span, 0)
    zero_mean = jnp.zeros((rows, topics), jnp.float32)
    if groups == 1:
        smoothed, _ = kalman(gains_here, pulls_here, zero_mean, zero_mean, by_year)
    elif groups == 2:
        smoothed = two_group_kalman(gains, pulls, by_year)
    else:
        local_smoothed, local_last = kalman(gains_here, pulls_here, zero_mean, zero_mean, by_year)
        summary = jnp.stack([local_last, local_smoothed[0]])
        if groups == 2:
            sent = jnp.where(group == 0, local_last, local_smoothed[0])
            other = shift_axis(sent, "tg", 1)
            ordered = jnp.where(
                group == 0, jnp.stack([summary, jnp.stack([other, other])]),
                jnp.stack([jnp.stack([other, other]), summary]),
            )
        else:
            seen = [summary] + [shift_axis(summary, "tg", s) for s in range(1, groups)]
            ordered = jnp.stack(seen)[(group - jnp.arange(groups)) % groups]
        carry, from_start, from_after = group_maps(gains, pulls, groups)
        entering = [zero_mean]
        for g in range(groups - 1):
            entering.append(ordered[g, 0] + carry[g] * entering[g])
        leaving = [zero_mean] * groups
        for g in reversed(range(1, groups)):
            leaving[g - 1] = (
                ordered[g, 1] + from_start[g] * entering[g] + from_after[g] * leaving[g]
            )
        start = jnp.stack(entering)[group]
        after = jnp.stack(leaving)[group]
        smoothed, _ = kalman(gains_here, pulls_here, start, after, by_year)
    return lax.all_to_all(smoothed, "tl", split_axis=0, concat_axis=0, tiled=True)


def solution(mesh):
    years = mesh.shape["tm"]
    span = 8 if years % 8 == 0 else years
    devices = mesh.devices.reshape(years // span, span, mesh.shape["doc"])
    grouped = jax.sharding.Mesh(devices, ("tg", "tl", "doc"))
    split = P(("tg", "tl"), "doc", None)
    in_specs = (split, split, split, P(), P(), P(), P())
    out_specs = (split, split)
    return jax.shard_map(body, mesh=grouped, in_specs=in_specs, out_specs=out_specs, check_vma=False)
```

```python
import jax
import jax.numpy as jnp
from jax import lax
from jax.experimental import pallas as pl
from jax.experimental.pallas import tpu as pltpu
from jax.sharding import PartitionSpec as P

K = 128
BLOCK = 128
EITERS = 4
PARTS = 1


init_variance = 4.0


def variance_tables(obs_precision, drift_var):

    def forward_step(prior_var, precision):
        denominator = 1.0 + prior_var * precision
        gain_now = prior_var * precision / denominator
        filt_var = prior_var / denominator
        return (filt_var + drift_var, (gain_now, filt_var))

    start_var = jnp.full(drift_var.shape, init_variance, dtype=jnp.float32)
    last_var, (gains, filt_vars) = lax.scan(forward_step, start_var, obs_precision, unroll=True)

    def backward_step(info_next, precision):
        merged = info_next + precision
        shrink = 1.0 / (1.0 + drift_var * merged)
        info_now = merged * shrink
        return (info_now, (shrink, info_now))

    zero_info = jnp.zeros(drift_var.shape, dtype=jnp.float32)
    last_info, (shrinks, infos) = lax.scan(
        backward_step, zero_info, obs_precision[1:], reverse=True
    )
    shrinks = jnp.concatenate([shrinks, jnp.ones_like(zero_info)[None]], axis=0)
    infos = jnp.concatenate([infos, zero_info[None]], axis=0)
    return (gains, filt_vars, shrinks, infos)


def e_step(looked, word_counts, topic_prior):
    counts_float = word_counts.astype(jnp.float32)
    doc_topics = topic_prior + jnp.sum(counts_float, axis=-1, keepdims=True) / K
    scores = looked.astype(jnp.float32)
    for sweep in range(EITERS):
        logits = lax.digamma(doc_topics)[..., None, :] + scores
        peak = lax.optimization_barrier(jnp.max(logits, axis=-1, keepdims=True))
        raised = jnp.exp(logits - peak)
        total = jnp.sum(raised, axis=-1)
        if sweep < EITERS - 1:
            share = counts_float / total
            doc_topics = topic_prior + jnp.sum(share[..., None] * raised, axis=-2)
        else:
            resp = raised / total[..., None]
            doc_topics = topic_prior + jnp.sum(counts_float[..., None] * resp, axis=-2)
    weighted = to_bf16(counts_float[..., None] * resp)
    return (doc_topics, weighted)


def to_bf16(value):
    return lax.reduce_precision(value, exponent_bits=8, mantissa_bits=7).astype(jnp.bfloat16)


def shift_axis(value, axis, s):
    count = lax.axis_size(axis)
    return lax.ppermute(value, axis, [(i, (i + s) % count) for i in range(count)])


def shift_doc(value, s):
    return shift_axis(value, "doc", s)


def kalman_kernel(gain_ref, pull_ref, start_ref, after_ref, pseudo_ref, out_ref, last_ref):
    years = pseudo_ref.shape[0]
    mean = start_ref[...]
    for t in range(years):
        gain_now = gain_ref[pl.ds(t, 1), :]
        mean = (1.0 - gain_now) * mean + gain_now * pseudo_ref[t]
        out_ref[t] = mean
    last_ref[...] = mean
    mean = after_ref[...]
    for t in reversed(range(years)):
        pull_now = pull_ref[pl.ds(t, 1), :]
        mean = pull_now * mean + (1.0 - pull_now) * out_ref[t]
        out_ref[t] = mean


def kalman(gains, pulls, start, after, by_year):
    years, rows, topics = by_year.shape
    block = rows
    whole = pl.BlockSpec((years, topics), lambda i: (0, 0))
    edge = pl.BlockSpec((block, topics), lambda i: (i, 0))
    stack = pl.BlockSpec((years, block, topics), lambda i: (0, i, 0))
    return pl.pallas_call(
        kalman_kernel,
        grid=(rows // block,),
        in_specs=[whole, whole, edge, edge, stack],
        out_specs=(stack, edge),
        out_shape=(
            jax.ShapeDtypeStruct(by_year.shape, jnp.float32),
            jax.ShapeDtypeStruct(start.shape, jnp.float32),
        ),
    )(gains, pulls, start, after, by_year)


def first_pass_kernel(gain_ref, pull_ref, pseudo_ref, sent_ref, last_ref, filt_ref):
    years = pseudo_ref.shape[0]
    group = lax.axis_index("tg")
    base = group * years
    mean = jnp.zeros(pseudo_ref.shape[1:], jnp.float32)
    for t in range(years):
        gain_now = gain_ref[pl.ds(base + t, 1), :]
        mean = (1.0 - gain_now) * mean + gain_now * pseudo_ref[t]
        filt_ref[t] = mean
    last = mean
    mean = jnp.zeros(pseudo_ref.shape[1:], jnp.float32)
    for t in reversed(range(years)):
        pull_now = pull_ref[pl.ds(base + t, 1), :]
        mean = pull_now * mean + (1.0 - pull_now) * filt_ref[t]
    weight = jnp.where(group == 0, 1.0, 0.0)
    sent_ref[...] = weight * last + (1.0 - weight) * mean
    last_ref[...] = last


def second_pass_kernel(gain_ref, pull_ref, other_ref, last_ref, pseudo_ref, out_ref):
    years = pseudo_ref.shape[0]
    group = lax.axis_index("tg")
    base = group * years
    weight = jnp.where(group == 0, 1.0, 0.0)
    carry = jnp.ones((1, gain_ref.shape[1]), jnp.float32)
    responses = []
    for t in range(years):
        carry = (1.0 - gain_ref[pl.ds(years + t, 1), :]) * carry
        responses.append(carry)
    reach = jnp.zeros_like(carry)
    for t in reversed(range(years)):
        pull_now = pull_ref[pl.ds(years + t, 1), :]
        reach = pull_now * reach + (1.0 - pull_now) * responses[t]
    other = other_ref[...]
    mean = (1.0 - weight) * other
    for t in range(years):
        gain_now = gain_ref[pl.ds(base + t, 1), :]
        mean = (1.0 - gain_now) * mean + gain_now * pseudo_ref[t]
        out_ref[t] = mean
    mean = weight * (other + reach * last_ref[...])
    for t in reversed(range(years)):
        pull_now = pull_ref[pl.ds(base + t, 1), :]
        mean = pull_now * mean + (1.0 - pull_now) * out_ref[t]
        out_ref[t] = mean


def two_group_kalman(gains, pulls, by_year):
    years, rows, topics = by_year.shape
    edge = jax.ShapeDtypeStruct((rows, topics), jnp.float32)
    group = lax.axis_index("tg")
    gains_here = lax.dynamic_slice_in_dim(gains, group * years, years, 0)
    pulls_here = lax.dynamic_slice_in_dim(pulls, group * years, years, 0)
    mean = jnp.zeros((rows, topics), jnp.float32)
    filtered = []
    for t in range(years):
        mean = (1.0 - gains_here[t]) * mean + gains_here[t] * by_year[t]
        filtered.append(mean)
    last = mean
    mean = jnp.zeros((rows, topics), jnp.float32)
    for t in reversed(range(years)):
        mean = pulls_here[t] * mean + (1.0 - pulls_here[t]) * filtered[t]
    sent = jnp.where(group == 0, last, mean)
    other = shift_axis(sent, "tg", 1)
    carry = jnp.ones((topics,), jnp.float32)
    responses = []
    for t in range(years):
        carry = (1.0 - gains[years + t]) * carry
        responses.append(carry)
    reach = jnp.zeros_like(carry)
    for t in reversed(range(years)):
        reach = pulls[years + t] * reach + (1.0 - pulls[years + t]) * responses[t]
    weight = jnp.where(group == 0, 1.0, 0.0)
    unit = jnp.eye(years + 2, dtype=jnp.float32)[:, :, None]
    state = unit[years]
    filtered = []
    for t in range(years):
        state = (1.0 - gains_here[t]) * state + gains_here[t] * unit[t]
        filtered.append(state)
    state = unit[years + 1]
    maps = [None] * years
    for t in reversed(range(years)):
        state = pulls_here[t] * state + (1.0 - pulls_here[t]) * filtered[t]
        maps[t] = state
    maps = jnp.stack(maps)
    smoothed = maps[:, years + 1, None, :] * (weight * reach * last)
    for s in range(years):
        smoothed = smoothed + maps[:, s, None, :] * by_year[s]
    smoothed = lax.optimization_barrier(smoothed)
    via_other = (1.0 - weight) * maps[:, years] + weight * maps[:, years + 1]
    return smoothed + via_other[:, None, :] * other


def group_maps(gains, pulls, groups):
    gains_g = gains.reshape(groups, -1, gains.shape[-1])
    pulls_g = pulls.reshape(groups, -1, pulls.shape[-1])
    span = gains_g.shape[1]
    carry = jnp.ones_like(gains_g[:, 0])
    responses = []
    for i in range(span):
        carry = (1.0 - gains_g[:, i]) * carry
        responses.append(carry)
    from_start = jnp.zeros_like(carry)
    from_after = jnp.ones_like(carry)
    for i in reversed(range(span)):
        from_start = pulls_g[:, i] * from_start + (1.0 - pulls_g[:, i]) * responses[i]
        from_after = pulls_g[:, i] * from_after
    return carry, from_start, from_after


def body(beta, word_ids, word_counts, block_slot, topic_prior, drift_var, obs_precision):
    local_beta = beta[0]
    own_words = local_beta.shape[0]
    topics = local_beta.shape[1]
    doc_devices = lax.axis_size("doc")
    doc_place = lax.axis_index("doc")
    local_peak = jnp.max(local_beta, axis=0)
    local_total = jnp.sum(jnp.exp(local_beta - local_peak), axis=0)

    slot_ids = word_ids[0]
    local_docs = slot_ids.shape[0]
    slot_width = slot_ids.shape[1]

    per_docs = local_docs * slot_width
    message = jnp.concatenate([
        slot_ids.reshape(-1).astype(jnp.float32),
        word_counts[0].reshape(-1).astype(jnp.float32),
        local_peak,
        local_total,
    ])
    seen = jnp.stack([message] + [shift_doc(message, s) for s in range(1, doc_devices)])
    ints_seen = [
        seen[:, :2 * per_docs].astype(jnp.int32).reshape(doc_devices, 2, local_docs, slot_width)[i]
        for i in range(doc_devices)
    ]
    stats_seen = seen[:, 2 * per_docs:].reshape(doc_devices, 2, topics)
    all_ids = jnp.concatenate([part[0] for part in ints_seen], axis=0)
    block_match = (all_ids // BLOCK)[..., None] == lax.iota(jnp.int32, block_slot.shape[0])
    all_columns = (
        jnp.sum(jnp.where(block_match, block_slot, 0), axis=-1) * BLOCK + all_ids % BLOCK
    )
    all_counts = jnp.concatenate([part[1] for part in ints_seen], axis=0)
    peaks = stats_seen[:, 0]
    totals = stats_seen[:, 1]
    peak_value = jnp.max(peaks, axis=0)
    total_value = jnp.sum(totals * jnp.exp(peaks - peak_value), axis=0)
    normalizer = peak_value + jnp.log(total_value)

    flat_columns = all_columns.reshape(-1)
    local_columns = flat_columns - doc_place * own_words
    row_words = lax.iota(jnp.int32, own_words)
    marks = (row_words[:, None] == local_columns[None, :]).astype(jnp.bfloat16)
    table = to_bf16(local_beta - normalizer)
    partial = (
        lax.dot_general(marks, table, (((0,), (0,)), ((), ())), preferred_element_type=jnp.float32)
        .astype(jnp.bfloat16)
        .reshape(doc_devices, local_docs * slot_width, topics)
    )
    looked = partial
    for s in range(1, doc_devices):
        looked = looked + jnp.roll(shift_doc(partial, s), s, axis=0)
    looked = looked.reshape(local_docs * doc_devices, slot_width, topics)

    doc_topics_all, weighted = e_step(looked, all_counts, topic_prior)
    doc_topics = doc_topics_all[:local_docs]

    flat_weighted = weighted.reshape(-1, topics)
    held_columns = lax.optimization_barrier(local_columns)
    held_marks = lax.optimization_barrier(
        (row_words[:, None] == held_columns[None, :]).astype(jnp.bfloat16)
    )
    counts = jnp.dot(held_marks, flat_weighted, preferred_element_type=jnp.float32)
    pseudo = local_beta + jnp.log1p(counts)

    obs_precision, drift_var, pseudo = lax.optimization_barrier((obs_precision, drift_var, pseudo))
    gains, filt_vars, shrinks, infos = variance_tables(obs_precision, drift_var)
    years_total = obs_precision.shape[0]
    pulls = filt_vars / (filt_vars + drift_var)
    pulls = pulls.at[-1].set(0.0)

    span = lax.axis_size("tl")
    chunk = own_words // span
    by_dest = pseudo.reshape(span, chunk, topics)
    parts = PARTS if chunk % (8 * PARTS) == 0 else 1
    rows = chunk // parts
    done = [
        smooth_part(by_dest[:, i * rows:(i + 1) * rows], gains, pulls) for i in range(parts)
    ]
    back = jnp.concatenate(done, axis=1)
    return (back.reshape(own_words, topics)[None], doc_topics[None])


def smooth_part(by_dest, gains, pulls):
    groups = lax.axis_size("tg")
    span, rows, topics = by_dest.shape
    group = lax.axis_index("tg")
    by_year = lax.all_to_all(by_dest, "tl", split_axis=0, concat_axis=0, tiled=True)
    gains_here = lax.dynamic_slice_in_dim(gains, group * span, span, 0)
    pulls_here = lax.dynamic_slice_in_dim(pulls, group * span, span, 0)
    zero_mean = jnp.zeros((rows, topics), jnp.float32)
    if groups == 1:
        smoothed, _ = kalman(gains_here, pulls_here, zero_mean, zero_mean, by_year)
    elif groups == 2:
        smoothed = two_group_kalman(gains, pulls, by_year)
    else:
        local_smoothed, local_last = kalman(gains_here, pulls_here, zero_mean, zero_mean, by_year)
        summary = jnp.stack([local_last, local_smoothed[0]])
        if groups == 2:
            sent = jnp.where(group == 0, local_last, local_smoothed[0])
            other = shift_axis(sent, "tg", 1)
            ordered = jnp.where(
                group == 0, jnp.stack([summary, jnp.stack([other, other])]),
                jnp.stack([jnp.stack([other, other]), summary]),
            )
        else:
            seen = [summary] + [shift_axis(summary, "tg", s) for s in range(1, groups)]
            ordered = jnp.stack(seen)[(group - jnp.arange(groups)) % groups]
        carry, from_start, from_after = group_maps(gains, pulls, groups)
        entering = [zero_mean]
        for g in range(groups - 1):
            entering.append(ordered[g, 0] + carry[g] * entering[g])
        leaving = [zero_mean] * groups
        for g in reversed(range(1, groups)):
            leaving[g - 1] = (
                ordered[g, 1] + from_start[g] * entering[g] + from_after[g] * leaving[g]
            )
        start = jnp.stack(entering)[group]
        after = jnp.stack(leaving)[group]
        smoothed, _ = kalman(gains_here, pulls_here, start, after, by_year)
    return lax.all_to_all(smoothed, "tl", split_axis=0, concat_axis=0, tiled=True)


def solution(mesh):
    years = mesh.shape["tm"]
    span = 8 if years % 8 == 0 else years
    devices = mesh.devices.reshape(years // span, span, mesh.shape["doc"])
    grouped = jax.sharding.Mesh(devices, ("tg", "tl", "doc"))
    split = P(("tg", "tl"), "doc", None)
    in_specs = (split, split, split, P(), P(), P(), P())
    out_specs = (split, split)
    return jax.shard_map(body, mesh=grouped, in_specs=in_specs, out_specs=out_specs, check_vma=False)
```

```python
import jax
import jax.numpy as jnp
from jax import lax
from jax.experimental import pallas as pl
from jax.experimental.pallas import tpu as pltpu
from jax.sharding import PartitionSpec as P

K = 128
BLOCK = 128
EITERS = 4
PARTS = 1


init_variance = 4.0


def variance_tables(obs_precision, drift_var):

    def forward_step(prior_var, precision):
        denominator = 1.0 + prior_var * precision
        gain_now = prior_var * precision / denominator
        filt_var = prior_var / denominator
        return (filt_var + drift_var, (gain_now, filt_var))

    start_var = jnp.full(drift_var.shape, init_variance, dtype=jnp.float32)
    last_var, (gains, filt_vars) = lax.scan(forward_step, start_var, obs_precision, unroll=True)

    def backward_step(info_next, precision):
        merged = info_next + precision
        shrink = 1.0 / (1.0 + drift_var * merged)
        info_now = merged * shrink
        return (info_now, (shrink, info_now))

    zero_info = jnp.zeros(drift_var.shape, dtype=jnp.float32)
    last_info, (shrinks, infos) = lax.scan(
        backward_step, zero_info, obs_precision[1:], reverse=True
    )
    shrinks = jnp.concatenate([shrinks, jnp.ones_like(zero_info)[None]], axis=0)
    infos = jnp.concatenate([infos, zero_info[None]], axis=0)
    return (gains, filt_vars, shrinks, infos)


def e_step(looked, word_counts, topic_prior):
    counts_float = word_counts.astype(jnp.float32)
    doc_topics = topic_prior + jnp.sum(counts_float, axis=-1, keepdims=True) / K
    scores = looked.astype(jnp.float32)
    for sweep in range(EITERS):
        logits = lax.digamma(doc_topics)[..., None, :] + scores
        peak = lax.optimization_barrier(jnp.max(logits, axis=-1, keepdims=True))
        raised = jnp.exp(logits - peak)
        total = jnp.sum(raised, axis=-1)
        if sweep < EITERS - 1:
            share = counts_float / total
            doc_topics = topic_prior + jnp.sum(share[..., None] * raised, axis=-2)
        else:
            resp = raised / total[..., None]
            doc_topics = topic_prior + jnp.sum(counts_float[..., None] * resp, axis=-2)
    weighted = to_bf16(counts_float[..., None] * resp)
    return (doc_topics, weighted)


def to_bf16(value):
    return lax.reduce_precision(value, exponent_bits=8, mantissa_bits=7).astype(jnp.bfloat16)


def shift_axis(value, axis, s):
    count = lax.axis_size(axis)
    return lax.ppermute(value, axis, [(i, (i + s) % count) for i in range(count)])


def shift_doc(value, s):
    return shift_axis(value, "doc", s)


def kalman_kernel(gain_ref, pull_ref, start_ref, after_ref, pseudo_ref, out_ref, last_ref):
    years = pseudo_ref.shape[0]
    mean = start_ref[...]
    for t in range(years):
        gain_now = gain_ref[pl.ds(t, 1), :]
        mean = (1.0 - gain_now) * mean + gain_now * pseudo_ref[t]
        out_ref[t] = mean
    last_ref[...] = mean
    mean = after_ref[...]
    for t in reversed(range(years)):
        pull_now = pull_ref[pl.ds(t, 1), :]
        mean = pull_now * mean + (1.0 - pull_now) * out_ref[t]
        out_ref[t] = mean


def kalman(gains, pulls, start, after, by_year):
    years, rows, topics = by_year.shape
    block = rows
    whole = pl.BlockSpec((years, topics), lambda i: (0, 0))
    edge = pl.BlockSpec((block, topics), lambda i: (i, 0))
    stack = pl.BlockSpec((years, block, topics), lambda i: (0, i, 0))
    return pl.pallas_call(
        kalman_kernel,
        grid=(rows // block,),
        in_specs=[whole, whole, edge, edge, stack],
        out_specs=(stack, edge),
        out_shape=(
            jax.ShapeDtypeStruct(by_year.shape, jnp.float32),
            jax.ShapeDtypeStruct(start.shape, jnp.float32),
        ),
    )(gains, pulls, start, after, by_year)


def first_pass_kernel(gain_ref, pull_ref, pseudo_ref, sent_ref, last_ref, filt_ref):
    years = pseudo_ref.shape[0]
    group = lax.axis_index("tg")
    base = group * years
    mean = jnp.zeros(pseudo_ref.shape[1:], jnp.float32)
    for t in range(years):
        gain_now = gain_ref[pl.ds(base + t, 1), :]
        mean = (1.0 - gain_now) * mean + gain_now * pseudo_ref[t]
        filt_ref[t] = mean
    last = mean
    mean = jnp.zeros(pseudo_ref.shape[1:], jnp.float32)
    for t in reversed(range(years)):
        pull_now = pull_ref[pl.ds(base + t, 1), :]
        mean = pull_now * mean + (1.0 - pull_now) * filt_ref[t]
    weight = jnp.where(group == 0, 1.0, 0.0)
    sent_ref[...] = weight * last + (1.0 - weight) * mean
    last_ref[...] = last


def second_pass_kernel(gain_ref, pull_ref, other_ref, last_ref, pseudo_ref, out_ref):
    years = pseudo_ref.shape[0]
    group = lax.axis_index("tg")
    base = group * years
    weight = jnp.where(group == 0, 1.0, 0.0)
    carry = jnp.ones((1, gain_ref.shape[1]), jnp.float32)
    responses = []
    for t in range(years):
        carry = (1.0 - gain_ref[pl.ds(years + t, 1), :]) * carry
        responses.append(carry)
    reach = jnp.zeros_like(carry)
    for t in reversed(range(years)):
        pull_now = pull_ref[pl.ds(years + t, 1), :]
        reach = pull_now * reach + (1.0 - pull_now) * responses[t]
    other = other_ref[...]
    mean = (1.0 - weight) * other
    for t in range(years):
        gain_now = gain_ref[pl.ds(base + t, 1), :]
        mean = (1.0 - gain_now) * mean + gain_now * pseudo_ref[t]
        out_ref[t] = mean
    mean = weight * (other + reach * last_ref[...])
    for t in reversed(range(years)):
        pull_now = pull_ref[pl.ds(base + t, 1), :]
        mean = pull_now * mean + (1.0 - pull_now) * out_ref[t]
        out_ref[t] = mean


def two_group_kalman(gains, pulls, by_year):
    years, rows, topics = by_year.shape
    edge = jax.ShapeDtypeStruct((rows, topics), jnp.float32)
    group = lax.axis_index("tg")
    gains_here = lax.dynamic_slice_in_dim(gains, group * years, years, 0)
    pulls_here = lax.dynamic_slice_in_dim(pulls, group * years, years, 0)
    mean = jnp.zeros((rows, topics), jnp.float32)
    filtered = []
    for t in range(years):
        mean = (1.0 - gains_here[t]) * mean + gains_here[t] * by_year[t]
        filtered.append(mean)
    last = mean
    mean = jnp.zeros((rows, topics), jnp.float32)
    for t in reversed(range(years)):
        mean = pulls_here[t] * mean + (1.0 - pulls_here[t]) * filtered[t]
    sent = jnp.where(group == 0, last, mean)
    other = shift_axis(sent, "tg", 1)
    carry = jnp.ones((topics,), jnp.float32)
    responses = []
    for t in range(years):
        carry = (1.0 - gains[years + t]) * carry
        responses.append(carry)
    reach = jnp.zeros_like(carry)
    for t in reversed(range(years)):
        reach = pulls[years + t] * reach + (1.0 - pulls[years + t]) * responses[t]
    weight = jnp.where(group == 0, 1.0, 0.0)
    unit = jnp.eye(years + 2, dtype=jnp.float32)[:, :, None]
    state = unit[years]
    filtered = []
    for t in range(years):
        state = (1.0 - gains_here[t]) * state + gains_here[t] * unit[t]
        filtered.append(state)
    state = unit[years + 1]
    maps = [None] * years
    for t in reversed(range(years)):
        state = pulls_here[t] * state + (1.0 - pulls_here[t]) * filtered[t]
        maps[t] = state
    maps = jnp.stack(maps)
    smoothed = maps[:, years + 1, None, :] * (weight * reach * last)
    for s in range(years):
        smoothed = smoothed + maps[:, s, None, :] * by_year[s]
    smoothed = lax.optimization_barrier(smoothed)
    via_other = (1.0 - weight) * maps[:, years] + weight * maps[:, years + 1]
    return smoothed + via_other[:, None, :] * other


def group_maps(gains, pulls, groups):
    gains_g = gains.reshape(groups, -1, gains.shape[-1])
    pulls_g = pulls.reshape(groups, -1, pulls.shape[-1])
    span = gains_g.shape[1]
    carry = jnp.ones_like(gains_g[:, 0])
    responses = []
    for i in range(span):
        carry = (1.0 - gains_g[:, i]) * carry
        responses.append(carry)
    from_start = jnp.zeros_like(carry)
    from_after = jnp.ones_like(carry)
    for i in reversed(range(span)):
        from_start = pulls_g[:, i] * from_start + (1.0 - pulls_g[:, i]) * responses[i]
        from_after = pulls_g[:, i] * from_after
    return carry, from_start, from_after


def body(beta, word_ids, word_counts, block_slot, topic_prior, drift_var, obs_precision):
    local_beta = beta[0]
    own_words = local_beta.shape[0]
    topics = local_beta.shape[1]
    doc_devices = lax.axis_size("doc")
    doc_place = lax.axis_index("doc")
    local_peak = jnp.max(local_beta, axis=0)
    local_total = jnp.sum(jnp.exp(local_beta - local_peak), axis=0)

    slot_ids = word_ids[0]
    local_docs = slot_ids.shape[0]
    slot_width = slot_ids.shape[1]

    per_docs = local_docs * slot_width
    message = jnp.concatenate([
        slot_ids.reshape(-1).astype(jnp.float32),
        word_counts[0].reshape(-1).astype(jnp.float32),
        local_peak,
        local_total,
    ])
    seen = jnp.stack([message] + [shift_doc(message, s) for s in range(1, doc_devices)])
    ints_seen = [
        seen[:, :2 * per_docs].astype(jnp.int32).reshape(doc_devices, 2, local_docs, slot_width)[i]
        for i in range(doc_devices)
    ]
    stats_seen = seen[:, 2 * per_docs:].reshape(doc_devices, 2, topics)
    all_ids = jnp.concatenate([part[0] for part in ints_seen], axis=0)
    block_match = (all_ids // BLOCK)[..., None] == lax.iota(jnp.int32, block_slot.shape[0])
    all_columns = (
        jnp.sum(jnp.where(block_match, block_slot, 0), axis=-1) * BLOCK + all_ids % BLOCK
    )
    all_counts = jnp.concatenate([part[1] for part in ints_seen], axis=0)
    peaks = stats_seen[:, 0]
    totals = stats_seen[:, 1]
    peak_value = jnp.max(peaks, axis=0)
    total_value = jnp.sum(totals * jnp.exp(peaks - peak_value), axis=0)
    normalizer = peak_value + jnp.log(total_value)

    flat_columns = all_columns.reshape(-1)
    local_columns = flat_columns - doc_place * own_words
    row_words = lax.iota(jnp.int32, own_words)
    marks = (row_words[:, None] == local_columns[None, :]).astype(jnp.bfloat16)
    table = to_bf16(local_beta - normalizer)
    slot_marks = (local_columns[:, None] == row_words[None, :]).astype(jnp.bfloat16)
    partial = (
        jnp.dot(slot_marks, table, preferred_element_type=jnp.float32)
        .astype(jnp.bfloat16)
        .reshape(doc_devices, local_docs * slot_width, topics)
    )
    looked = partial
    for s in range(1, doc_devices):
        looked = looked + jnp.roll(shift_doc(partial, s), s, axis=0)
    looked = looked.reshape(local_docs * doc_devices, slot_width, topics)

    doc_topics_all, weighted = e_step(looked, all_counts, topic_prior)
    doc_topics = doc_topics_all[:local_docs]

    flat_weighted = weighted.reshape(-1, topics)
    counts = jnp.dot(marks, flat_weighted, preferred_element_type=jnp.float32)
    pseudo = local_beta + jnp.log1p(counts)

    gains, filt_vars, shrinks, infos = variance_tables(obs_precision, drift_var)
    years_total = obs_precision.shape[0]
    pulls = filt_vars / (filt_vars + drift_var)
    pulls = pulls.at[-1].set(0.0)

    span = lax.axis_size("tl")
    chunk = own_words // span
    by_dest = pseudo.reshape(span, chunk, topics)
    parts = PARTS if chunk % (8 * PARTS) == 0 else 1
    rows = chunk // parts
    done = [
        smooth_part(by_dest[:, i * rows:(i + 1) * rows], gains, pulls) for i in range(parts)
    ]
    back = jnp.concatenate(done, axis=1)
    return (back.reshape(own_words, topics)[None], doc_topics[None])


def smooth_part(by_dest, gains, pulls):
    groups = lax.axis_size("tg")
    span, rows, topics = by_dest.shape
    group = lax.axis_index("tg")
    by_year = lax.all_to_all(by_dest, "tl", split_axis=0, concat_axis=0, tiled=True)
    gains_here = lax.dynamic_slice_in_dim(gains, group * span, span, 0)
    pulls_here = lax.dynamic_slice_in_dim(pulls, group * span, span, 0)
    zero_mean = jnp.zeros((rows, topics), jnp.float32)
    if groups == 1:
        smoothed, _ = kalman(gains_here, pulls_here, zero_mean, zero_mean, by_year)
    elif groups == 2:
        smoothed = two_group_kalman(gains, pulls, by_year)
    else:
        local_smoothed, local_last = kalman(gains_here, pulls_here, zero_mean, zero_mean, by_year)
        summary = jnp.stack([local_last, local_smoothed[0]])
        if groups == 2:
            sent = jnp.where(group == 0, local_last, local_smoothed[0])
            other = shift_axis(sent, "tg", 1)
            ordered = jnp.where(
                group == 0, jnp.stack([summary, jnp.stack([other, other])]),
                jnp.stack([jnp.stack([other, other]), summary]),
            )
        else:
            seen = [summary] + [shift_axis(summary, "tg", s) for s in range(1, groups)]
            ordered = jnp.stack(seen)[(group - jnp.arange(groups)) % groups]
        carry, from_start, from_after = group_maps(gains, pulls, groups)
        entering = [zero_mean]
        for g in range(groups - 1):
            entering.append(ordered[g, 0] + carry[g] * entering[g])
        leaving = [zero_mean] * groups
        for g in reversed(range(1, groups)):
            leaving[g - 1] = (
                ordered[g, 1] + from_start[g] * entering[g] + from_after[g] * leaving[g]
            )
        start = jnp.stack(entering)[group]
        after = jnp.stack(leaving)[group]
        smoothed, _ = kalman(gains_here, pulls_here, start, after, by_year)
    return lax.all_to_all(smoothed, "tl", split_axis=0, concat_axis=0, tiled=True)


def solution(mesh):
    years = mesh.shape["tm"]
    span = 8 if years % 8 == 0 else years
    devices = mesh.devices.reshape(years // span, span, mesh.shape["doc"])
    grouped = jax.sharding.Mesh(devices, ("tg", "tl", "doc"))
    split = P(("tg", "tl"), "doc", None)
    in_specs = (split, split, split, P(), P(), P(), P())
    out_specs = (split, split)
    return jax.shard_map(body, mesh=grouped, in_specs=in_specs, out_specs=out_specs, check_vma=False)
```

```python
import jax
import jax.numpy as jnp
from jax import lax
from jax.experimental import pallas as pl
from jax.experimental.pallas import tpu as pltpu
from jax.sharding import PartitionSpec as P

K = 128
BLOCK = 128
EITERS = 4
PARTS = 1


init_variance = 4.0


def variance_tables(obs_precision, drift_var):

    def forward_step(prior_var, precision):
        denominator = 1.0 + prior_var * precision
        gain_now = prior_var * precision / denominator
        filt_var = prior_var / denominator
        return (filt_var + drift_var, (gain_now, filt_var))

    start_var = jnp.full(drift_var.shape, init_variance, dtype=jnp.float32)
    last_var, (gains, filt_vars) = lax.scan(forward_step, start_var, obs_precision, unroll=True)

    def backward_step(info_next, precision):
        merged = info_next + precision
        shrink = 1.0 / (1.0 + drift_var * merged)
        info_now = merged * shrink
        return (info_now, (shrink, info_now))

    zero_info = jnp.zeros(drift_var.shape, dtype=jnp.float32)
    last_info, (shrinks, infos) = lax.scan(
        backward_step, zero_info, obs_precision[1:], reverse=True
    )
    shrinks = jnp.concatenate([shrinks, jnp.ones_like(zero_info)[None]], axis=0)
    infos = jnp.concatenate([infos, zero_info[None]], axis=0)
    return (gains, filt_vars, shrinks, infos)


def e_step(looked, word_counts, topic_prior):
    counts_float = word_counts.astype(jnp.float32)
    doc_topics = topic_prior + jnp.sum(counts_float, axis=-1, keepdims=True) / K
    scores = looked.astype(jnp.float32)
    for sweep in range(EITERS):
        logits = lax.digamma(doc_topics)[..., None, :] + scores
        peak = lax.optimization_barrier(jnp.max(logits, axis=-1, keepdims=True))
        raised = jnp.exp(logits - peak)
        total = jnp.sum(raised, axis=-1)
        if sweep < EITERS - 1:
            share = counts_float / total
            doc_topics = topic_prior + jnp.sum(share[..., None] * raised, axis=-2)
        else:
            resp = raised / total[..., None]
            doc_topics = topic_prior + jnp.sum(counts_float[..., None] * resp, axis=-2)
    weighted = to_bf16(counts_float[..., None] * resp)
    return (doc_topics, weighted)


def to_bf16(value):
    return lax.reduce_precision(value, exponent_bits=8, mantissa_bits=7).astype(jnp.bfloat16)


def shift_axis(value, axis, s):
    count = lax.axis_size(axis)
    return lax.ppermute(value, axis, [(i, (i + s) % count) for i in range(count)])


def shift_doc(value, s):
    return shift_axis(value, "doc", s)


def kalman_kernel(gain_ref, pull_ref, start_ref, after_ref, pseudo_ref, out_ref, last_ref):
    years = pseudo_ref.shape[0]
    mean = start_ref[...]
    for t in range(years):
        gain_now = gain_ref[pl.ds(t, 1), :]
        mean = (1.0 - gain_now) * mean + gain_now * pseudo_ref[t]
        out_ref[t] = mean
    last_ref[...] = mean
    mean = after_ref[...]
    for t in reversed(range(years)):
        pull_now = pull_ref[pl.ds(t, 1), :]
        mean = pull_now * mean + (1.0 - pull_now) * out_ref[t]
        out_ref[t] = mean


def kalman(gains, pulls, start, after, by_year):
    years, rows, topics = by_year.shape
    block = rows
    whole = pl.BlockSpec((years, topics), lambda i: (0, 0))
    edge = pl.BlockSpec((block, topics), lambda i: (i, 0))
    stack = pl.BlockSpec((years, block, topics), lambda i: (0, i, 0))
    return pl.pallas_call(
        kalman_kernel,
        grid=(rows // block,),
        in_specs=[whole, whole, edge, edge, stack],
        out_specs=(stack, edge),
        out_shape=(
            jax.ShapeDtypeStruct(by_year.shape, jnp.float32),
            jax.ShapeDtypeStruct(start.shape, jnp.float32),
        ),
    )(gains, pulls, start, after, by_year)


def first_pass_kernel(gain_ref, pull_ref, pseudo_ref, sent_ref, last_ref, filt_ref):
    years = pseudo_ref.shape[0]
    group = lax.axis_index("tg")
    base = group * years
    mean = jnp.zeros(pseudo_ref.shape[1:], jnp.float32)
    for t in range(years):
        gain_now = gain_ref[pl.ds(base + t, 1), :]
        mean = (1.0 - gain_now) * mean + gain_now * pseudo_ref[t]
        filt_ref[t] = mean
    last = mean
    mean = jnp.zeros(pseudo_ref.shape[1:], jnp.float32)
    for t in reversed(range(years)):
        pull_now = pull_ref[pl.ds(base + t, 1), :]
        mean = pull_now * mean + (1.0 - pull_now) * filt_ref[t]
    weight = jnp.where(group == 0, 1.0, 0.0)
    sent_ref[...] = weight * last + (1.0 - weight) * mean
    last_ref[...] = last


def second_pass_kernel(gain_ref, pull_ref, other_ref, last_ref, pseudo_ref, out_ref):
    years = pseudo_ref.shape[0]
    group = lax.axis_index("tg")
    base = group * years
    weight = jnp.where(group == 0, 1.0, 0.0)
    carry = jnp.ones((1, gain_ref.shape[1]), jnp.float32)
    responses = []
    for t in range(years):
        carry = (1.0 - gain_ref[pl.ds(years + t, 1), :]) * carry
        responses.append(carry)
    reach = jnp.zeros_like(carry)
    for t in reversed(range(years)):
        pull_now = pull_ref[pl.ds(years + t, 1), :]
        reach = pull_now * reach + (1.0 - pull_now) * responses[t]
    other = other_ref[...]
    mean = (1.0 - weight) * other
    for t in range(years):
        gain_now = gain_ref[pl.ds(base + t, 1), :]
        mean = (1.0 - gain_now) * mean + gain_now * pseudo_ref[t]
        out_ref[t] = mean
    mean = weight * (other + reach * last_ref[...])
    for t in reversed(range(years)):
        pull_now = pull_ref[pl.ds(base + t, 1), :]
        mean = pull_now * mean + (1.0 - pull_now) * out_ref[t]
        out_ref[t] = mean


def two_group_kalman(gains, pulls, by_year):
    years, rows, topics = by_year.shape
    edge = jax.ShapeDtypeStruct((rows, topics), jnp.float32)
    group = lax.axis_index("tg")
    gains_here = lax.dynamic_slice_in_dim(gains, group * years, years, 0)
    pulls_here = lax.dynamic_slice_in_dim(pulls, group * years, years, 0)
    mean = jnp.zeros((rows, topics), jnp.float32)
    filtered = []
    for t in range(years):
        mean = (1.0 - gains_here[t]) * mean + gains_here[t] * by_year[t]
        filtered.append(mean)
    last = mean
    mean = jnp.zeros((rows, topics), jnp.float32)
    for t in reversed(range(years)):
        mean = pulls_here[t] * mean + (1.0 - pulls_here[t]) * filtered[t]
    sent = jnp.where(group == 0, last, mean)
    other = shift_axis(sent, "tg", 1)
    carry = jnp.ones((topics,), jnp.float32)
    responses = []
    for t in range(years):
        carry = (1.0 - gains[years + t]) * carry
        responses.append(carry)
    reach = jnp.zeros_like(carry)
    for t in reversed(range(years)):
        reach = pulls[years + t] * reach + (1.0 - pulls[years + t]) * responses[t]
    weight = jnp.where(group == 0, 1.0, 0.0)
    unit = jnp.eye(years + 2, dtype=jnp.float32)[:, :, None]
    state = unit[years]
    filtered = []
    for t in range(years):
        state = (1.0 - gains_here[t]) * state + gains_here[t] * unit[t]
        filtered.append(state)
    state = unit[years + 1]
    maps = [None] * years
    for t in reversed(range(years)):
        state = pulls_here[t] * state + (1.0 - pulls_here[t]) * filtered[t]
        maps[t] = state
    maps = jnp.stack(maps)
    smoothed = maps[:, years + 1, None, :] * (weight * reach * last)
    for s in range(years):
        smoothed = smoothed + maps[:, s, None, :] * by_year[s]
    smoothed = lax.optimization_barrier(smoothed)
    via_other = (1.0 - weight) * maps[:, years] + weight * maps[:, years + 1]
    return smoothed + via_other[:, None, :] * other


def group_maps(gains, pulls, groups):
    gains_g = gains.reshape(groups, -1, gains.shape[-1])
    pulls_g = pulls.reshape(groups, -1, pulls.shape[-1])
    span = gains_g.shape[1]
    carry = jnp.ones_like(gains_g[:, 0])
    responses = []
    for i in range(span):
        carry = (1.0 - gains_g[:, i]) * carry
        responses.append(carry)
    from_start = jnp.zeros_like(carry)
    from_after = jnp.ones_like(carry)
    for i in reversed(range(span)):
        from_start = pulls_g[:, i] * from_start + (1.0 - pulls_g[:, i]) * responses[i]
        from_after = pulls_g[:, i] * from_after
    return carry, from_start, from_after


def body(beta, word_ids, word_counts, block_slot, topic_prior, drift_var, obs_precision):
    local_beta = beta[0]
    own_words = local_beta.shape[0]
    topics = local_beta.shape[1]
    doc_devices = lax.axis_size("doc")
    doc_place = lax.axis_index("doc")
    local_peak = jnp.max(local_beta, axis=0)
    local_total = jnp.sum(jnp.exp(local_beta - local_peak), axis=0)

    slot_ids = word_ids[0]
    local_docs = slot_ids.shape[0]
    slot_width = slot_ids.shape[1]

    per_docs = local_docs * slot_width
    message = jnp.concatenate([
        slot_ids.reshape(-1).astype(jnp.float32),
        word_counts[0].reshape(-1).astype(jnp.float32),
        local_peak,
        local_total,
    ])
    seen = jnp.stack([message] + [shift_doc(message, s) for s in range(1, doc_devices)])
    ints_seen = [
        seen[:, :2 * per_docs].astype(jnp.int32).reshape(doc_devices, 2, local_docs, slot_width)[i]
        for i in range(doc_devices)
    ]
    stats_seen = seen[:, 2 * per_docs:].reshape(doc_devices, 2, topics)
    all_ids = jnp.concatenate([part[0] for part in ints_seen], axis=0)
    block_match = (all_ids // BLOCK)[..., None] == lax.iota(jnp.int32, block_slot.shape[0])
    all_columns = (
        jnp.sum(jnp.where(block_match, block_slot, 0), axis=-1) * BLOCK + all_ids % BLOCK
    )
    all_counts = jnp.concatenate([part[1] for part in ints_seen], axis=0)
    peaks = stats_seen[:, 0]
    totals = stats_seen[:, 1]
    peak_value = jnp.max(peaks, axis=0)
    total_value = jnp.sum(totals * jnp.exp(peaks - peak_value), axis=0)
    normalizer = peak_value + jnp.log(total_value)

    flat_columns = all_columns.reshape(-1)
    local_columns = flat_columns - doc_place * own_words
    row_words = lax.iota(jnp.int32, own_words)
    marks = (row_words[:, None] == local_columns[None, :]).astype(jnp.bfloat16)
    table = to_bf16(local_beta - normalizer)
    slot_marks = (local_columns[:, None] == row_words[None, :]).astype(jnp.bfloat16)
    partial = (
        jnp.dot(slot_marks, table, preferred_element_type=jnp.float32)
        .astype(jnp.bfloat16)
        .reshape(doc_devices, local_docs * slot_width, topics)
    )
    looked = partial
    for s in range(1, doc_devices):
        looked = looked + jnp.roll(shift_doc(partial, s), s, axis=0)
    looked = looked.reshape(local_docs * doc_devices, slot_width, topics)

    doc_topics_all, weighted = e_step(looked, all_counts, topic_prior)
    doc_topics = doc_topics_all[:local_docs]

    flat_weighted = weighted.reshape(-1, topics)
    counts = jnp.dot(flat_weighted.T, slot_marks, preferred_element_type=jnp.float32).T
    pseudo = local_beta + jnp.log1p(counts)

    gains, filt_vars, shrinks, infos = variance_tables(obs_precision, drift_var)
    years_total = obs_precision.shape[0]
    pulls = filt_vars / (filt_vars + drift_var)
    pulls = pulls.at[-1].set(0.0)

    span = lax.axis_size("tl")
    chunk = own_words // span
    by_dest = pseudo.reshape(span, chunk, topics)
    parts = PARTS if chunk % (8 * PARTS) == 0 else 1
    rows = chunk // parts
    done = [
        smooth_part(by_dest[:, i * rows:(i + 1) * rows], gains, pulls) for i in range(parts)
    ]
    back = jnp.concatenate(done, axis=1)
    return (back.reshape(own_words, topics)[None], doc_topics[None])


def smooth_part(by_dest, gains, pulls):
    groups = lax.axis_size("tg")
    span, rows, topics = by_dest.shape
    group = lax.axis_index("tg")
    by_year = lax.all_to_all(by_dest, "tl", split_axis=0, concat_axis=0, tiled=True)
    gains_here = lax.dynamic_slice_in_dim(gains, group * span, span, 0)
    pulls_here = lax.dynamic_slice_in_dim(pulls, group * span, span, 0)
    zero_mean = jnp.zeros((rows, topics), jnp.float32)
    if groups == 1:
        smoothed, _ = kalman(gains_here, pulls_here, zero_mean, zero_mean, by_year)
    elif groups == 2:
        smoothed = two_group_kalman(gains, pulls, by_year)
    else:
        local_smoothed, local_last = kalman(gains_here, pulls_here, zero_mean, zero_mean, by_year)
        summary = jnp.stack([local_last, local_smoothed[0]])
        if groups == 2:
            sent = jnp.where(group == 0, local_last, local_smoothed[0])
            other = shift_axis(sent, "tg", 1)
            ordered = jnp.where(
                group == 0, jnp.stack([summary, jnp.stack([other, other])]),
                jnp.stack([jnp.stack([other, other]), summary]),
            )
        else:
            seen = [summary] + [shift_axis(summary, "tg", s) for s in range(1, groups)]
            ordered = jnp.stack(seen)[(group - jnp.arange(groups)) % groups]
        carry, from_start, from_after = group_maps(gains, pulls, groups)
        entering = [zero_mean]
        for g in range(groups - 1):
            entering.append(ordered[g, 0] + carry[g] * entering[g])
        leaving = [zero_mean] * groups
        for g in reversed(range(1, groups)):
            leaving[g - 1] = (
                ordered[g, 1] + from_start[g] * entering[g] + from_after[g] * leaving[g]
            )
        start = jnp.stack(entering)[group]
        after = jnp.stack(leaving)[group]
        smoothed, _ = kalman(gains_here, pulls_here, start, after, by_year)
    return lax.all_to_all(smoothed, "tl", split_axis=0, concat_axis=0, tiled=True)


def solution(mesh):
    years = mesh.shape["tm"]
    span = 8 if years % 8 == 0 else years
    devices = mesh.devices.reshape(years // span, span, mesh.shape["doc"])
    grouped = jax.sharding.Mesh(devices, ("tg", "tl", "doc"))
    split = P(("tg", "tl"), "doc", None)
    in_specs = (split, split, split, P(), P(), P(), P())
    out_specs = (split, split)
    return jax.shard_map(body, mesh=grouped, in_specs=in_specs, out_specs=out_specs, check_vma=False)
```
